32 devices in a mesh: graph: 16 (over z, y, core), head: 2 (over x).
Axes of the slice: x: 2, y: 2, z: 4, core: 2. Of those that a mesh axis runs over, the one named last changes fastest.
Arguments:
- nodes: bfloat16 [2048, 1024], P('graph'), may hold values from -6 to 6
- gain: float32 [1024], replicated, may hold values from 0.1 to 1.9
- w_query: bfloat16 [1024, 1024], P(None, 'head'), may hold values from -3 to 3
- w_key: bfloat16 [1024, 1024], P(None, 'head'), may hold values from -0.1875 to 0.1875
- w_value: bfloat16 [1024, 1024], P(None, 'head'), may hold values from -0.1875 to 0.1875
- w_out: bfloat16 [1024, 1024], P('head'), may hold values from -0.5 to 0.5
- links: int32 [16, 4], P('graph'), may hold values 0 or 1
- cotangent: bfloat16 [2048, 1024], P('graph'), may hold values from -6 to 6
Outputs:
- mixed: bfloat16 [2048, 1024], P('graph', 'head')
- nodes_grad: bfloat16 [2048, 1024], P('graph')
- gain_grad: float32 [1024], replicated
- w_query_grad: float32 [1024, 1024], P('graph', 'head')
- w_key_grad: float32 [1024, 1024], P('graph', 'head')
- w_value_grad: float32 [1024, 1024], P('graph', 'head')
- w_out_grad: float32 [1024, 1024], P('head', 'graph')
The draws below stay inside these ranges and needn't reach their ends.
All inputs are finite; a program needn't handle non-finite values. No bound on the sum of `links` on one device may be relied on, other than what follows from the above.
Results may differ from the reference program's by a relative error of at most 0.019.
The reference program's roundings to bfloat16 on the way (of `normed`, `probs_low`, `attended`, `grad_attended` and `grad_query`) count: a program that leaves them out, or rounds other values in their place, can miss the bound.
Values may be sent and summed in bfloat16 or wider, within the bound.
No kernel may reach another device: no remote copies, remote signals or barrier semaphores. Data moves between devices by JAX's collectives and lax.ppermute only.
A program may use at most 64 MiB of HBM per device.

```python
import math
import jax
import jax.numpy as jnp
from jax import lax

D = 1024
HEADS = 16
HEAD_DIM = 64
BLK = 128
NB = 16
NODES = 2048
LEV = 4
SLOTS = 5


def draw_w_query(key, part):
    head_key = jax.random.fold_in(key, 11)
    value_key = jax.random.fold_in(key, 12)
    levels = jnp.array([0.5, 1.0, 2.0, 4.0], jnp.float32)
    head_of = jnp.arange(D, dtype=jnp.int32) // HEAD_DIM
    picks = jax.random.randint(head_key, (HEADS,), 0, 4)
    factor = levels[picks[head_of]]
    spread = 1.0 / math.sqrt(D)
    entries = jnp.clip(jax.random.normal(value_key, (D, D), jnp.float32), -4.0, 4.0)
    return (entries * spread * factor[None, :]).astype(jnp.bfloat16)


def with_ends(values, key, low, high):
    spot = [jax.random.randint(jax.random.fold_in(key, axis), (), 0, length) for axis, length in enumerate(values.shape)]
    widest = values.shape.index(max(values.shape))
    beside = spot[:widest] + [(spot[widest] + 1) % values.shape[widest]] + spot[widest + 1:]
    return values.at[tuple(spot)].set(low).at[tuple(beside)].set(high)


def block_scale(key, dims, cuts, smallest, largest):
    factor_of = 1.0
    for dim, blocks in cuts:
        steps = jax.random.uniform(jax.random.fold_in(jax.random.fold_in(key, 6), dim), (blocks,), jnp.float32, smallest / len(cuts), largest / len(cuts))
        factor_of = factor_of * jnp.repeat(jnp.exp(steps), dims[dim] // blocks).reshape((-1,) + (1,) * (len(dims) - 1 - dim))
    return factor_of


def gaussian(key, extent, deviation, limit, split=(), kind=jnp.bfloat16):
    drawn = jax.random.normal(key, extent, jnp.float32) * deviation
    if len(split) > 0:
        drawn = block_scale(key, extent, split, -0.22, 0.18) * drawn
    return jnp.clip(drawn, min=-limit, max=limit).astype(kind)


def setup_inputs(seed: int = 0) -> dict:
    arg_keys = jax.random.split(jax.random.key(seed), 9)
    return {
        "nodes": gaussian(arg_keys[0], (NODES, D), 1.0, 6.0, ((0, 16),)),
        "gain": jnp.clip(1.0 + 0.18 * jax.random.normal(arg_keys[1], (D,), jnp.float32), 0.1, 1.9),
        "w_query": draw_w_query(jax.random.fold_in(arg_keys[8], 71), 0),
        "w_key": gaussian(arg_keys[3], (D, D), D ** -0.5, 0.1875, ((1, 2),)),
        "w_value": gaussian(arg_keys[4], (D, D), D ** -0.5, 0.1875, ((1, 2),)),
        "w_out": gaussian(arg_keys[5], (D, D), (D // 8) ** -0.5, 0.5, ((0, 2),)),
        "links": with_ends((jax.random.randint(arg_keys[6], (NB, LEV), 0, 4) < 3).astype(jnp.int32), jax.random.fold_in(arg_keys[6], 1), 0, 1),
        "cotangent": gaussian(arg_keys[7], (NODES, D), 1.0, 6.0, ((0, 16),)),
    }


EPS = 1e-05
NEG = -1e+30

def reference(nodes, gain, w_query, w_key, w_value, w_out, links, cotangent):
    score_scale = HEAD_DIM ** (-0.5)
    wide_nodes = nodes.astype(jnp.float32)
    inverse = lax.rsqrt(lax.optimization_barrier(jnp.mean(wide_nodes * wide_nodes, axis=1, keepdims=True)) + EPS)
    normed = (wide_nodes * inverse * gain).astype(jnp.bfloat16)
    query = jnp.dot(normed, w_query, preferred_element_type=jnp.float32).astype(jnp.bfloat16)
    keys = jnp.dot(normed, w_key, preferred_element_type=jnp.float32).astype(jnp.bfloat16)
    values = jnp.dot(normed, w_value, preferred_element_type=jnp.float32).astype(jnp.bfloat16)
    head_shape = (NB, BLK, HEADS, HEAD_DIM)
    query_blocks = query.reshape(head_shape)
    key_blocks = keys.reshape(head_shape)
    value_blocks = values.reshape(head_shape)
    block_ids = jnp.arange(NB, dtype=jnp.int32)
    table = jnp.stack([block_ids] + [jnp.bitwise_xor(block_ids, jnp.int32(1 << level)) for level in range(LEV)], axis=1)
    active = jnp.concatenate([jnp.ones((NB, 1), jnp.int32), links], axis=1)
    slot_ids = jnp.arange(SLOTS, dtype=jnp.int32)

    def scores_of(block):
        seen_keys = key_blocks[table[block]].astype(jnp.float32)
        scores = jnp.einsum('qhe,skhe->hqsk', query_blocks[block].astype(jnp.float32), seen_keys) * score_scale
        scores = jnp.where(active[block][None, None, :, None] > 0, scores, NEG)
        return (scores, seen_keys)

    def forward_block(block):
        scores, seen_keys = scores_of(block)
        top = lax.optimization_barrier(jnp.max(scores, axis=(2, 3), keepdims=True))
        total = lax.optimization_barrier(jnp.sum(jnp.exp(scores - top), axis=(2, 3), keepdims=True))
        probs_low = (jnp.exp(scores - top) / total).astype(jnp.bfloat16)
        seen_values = value_blocks[table[block]].astype(jnp.float32)
        output = jnp.einsum('hqsk,skhe->qhe', probs_low.astype(jnp.float32), seen_values).astype(jnp.bfloat16)
        return (output, top[:, :, 0, 0], total[:, :, 0, 0])
    attended_blocks, tops, totals = lax.map(forward_block, block_ids)
    attended = attended_blocks.reshape(NODES, D)
    mixed = jnp.dot(attended, w_out, preferred_element_type=jnp.float32).astype(jnp.bfloat16)
    grad_attended = jnp.dot(cotangent, w_out.T, preferred_element_type=jnp.float32).astype(jnp.bfloat16)
    w_out_grad = jnp.dot(attended.T, cotangent, preferred_element_type=jnp.float32)
    grad_blocks = grad_attended.reshape(head_shape)

    def query_pass(block):
        scores, seen_keys = scores_of(block)
        probs = jnp.exp(scores - tops[block][:, :, None, None]) / totals[block][:, :, None, None]
        seen_values = value_blocks[table[block]].astype(jnp.float32)
        grad_probs = jnp.einsum('qhe,skhe->hqsk', grad_blocks[block].astype(jnp.float32), seen_values)
        delta = lax.optimization_barrier(jnp.sum(probs * grad_probs, axis=(2, 3)))
        grad_scores = probs * (grad_probs - delta[:, :, None, None]) * score_scale
        grad_q = jnp.einsum('hqsk,skhe->qhe', grad_scores, seen_keys).astype(jnp.bfloat16)
        return (grad_q, delta)
    grad_query_blocks, deltas = lax.map(query_pass, block_ids)

    def key_pass(block):
        sources = table[block]
        source_queries = query_blocks[sources].astype(jnp.float32)
        source_grads = grad_blocks[sources].astype(jnp.float32)
        allowed = active[sources, slot_ids]
        scores = jnp.einsum('sqhe,khe->shqk', source_queries, key_blocks[block].astype(jnp.float32)) * score_scale
        scores = jnp.where(allowed[:, None, None, None] > 0, scores, NEG)
        probs = jnp.exp(scores - tops[sources][..., None]) / totals[sources][..., None]
        grad_probs = jnp.einsum('sqhe,khe->shqk', source_grads, value_blocks[block].astype(jnp.float32))
        grad_scores = probs * (grad_probs - deltas[sources][..., None]) * score_scale
        key_terms = jnp.einsum('shqk,sqhe->skhe', grad_scores, source_queries).astype(jnp.bfloat16)
        probs_low = probs.astype(jnp.bfloat16).astype(jnp.float32)
        value_terms = jnp.einsum('shqk,sqhe->skhe', probs_low, source_grads).astype(jnp.bfloat16)
        key_terms, value_terms = lax.optimization_barrier((key_terms, value_terms))
        grad_k = lax.optimization_barrier(jnp.sum(key_terms.astype(jnp.float32), axis=0)).astype(jnp.bfloat16)
        grad_v = lax.optimization_barrier(jnp.sum(value_terms.astype(jnp.float32), axis=0)).astype(jnp.bfloat16)
        return (grad_k, grad_v)
    grad_key_blocks, grad_value_blocks = lax.map(key_pass, block_ids)
    grad_query = grad_query_blocks.reshape(NODES, D)
    grad_key = grad_key_blocks.reshape(NODES, D)
    grad_value = grad_value_blocks.reshape(NODES, D)
    w_query_grad = jnp.dot(normed.T, grad_query, preferred_element_type=jnp.float32)
    w_key_grad = jnp.dot(normed.T, grad_key, preferred_element_type=jnp.float32)
    w_value_grad = jnp.dot(normed.T, grad_value, preferred_element_type=jnp.float32)
    grad_normed = jnp.dot(grad_query, w_query.T, preferred_element_type=jnp.float32) + jnp.dot(grad_key, w_key.T, preferred_element_type=jnp.float32) + jnp.dot(grad_value, w_value.T, preferred_element_type=jnp.float32)
    gain_grad = lax.optimization_barrier(jnp.sum(grad_normed * wide_nodes * inverse, axis=0))
    scaled = grad_normed * gain
    nodes_grad = (inverse * (scaled - wide_nodes * inverse * inverse * lax.optimization_barrier(jnp.mean(scaled * wide_nodes, axis=1, keepdims=True)))).astype(jnp.bfloat16)
    return (mixed, nodes_grad, gain_grad, w_query_grad, w_key_grad, w_value_grad, w_out_grad)
```

```python
import jax
import jax.numpy as jnp
from jax import lax
from jax.sharding import PartitionSpec as P

HEAD_DIM = 64


EPS = 1e-05
NEG = -1e30


def from_partner(value, axis, apart):
    mask = 2**apart
    pairs = [(source, source ^ mask) for source in range(lax.axis_size(axis))]
    return lax.ppermute(value, axis, pairs)


def bit_major_rows(matrix, levels):
    rows, width = matrix.shape
    inner = width >> levels
    shaped = matrix.reshape((rows,) + (2,) * levels + (inner,))
    order = (0,) + tuple(range(levels, 0, -1)) + (levels + 1,)
    return shaped.transpose(order).reshape(rows, width)


def halving_sum(partial, axis, levels):
    me = lax.axis_index(axis)
    for bit in range(levels):
        half = partial.shape[0] // 2
        mine = (me >> bit) & 1
        keep = lax.dynamic_slice_in_dim(partial, mine * half, half, 0)
        send = lax.dynamic_slice_in_dim(partial, (1 - mine) * half, half, 0)
        got = from_partner(send.astype(jnp.bfloat16), axis, bit)
        partial = keep + got.astype(jnp.float32)
    return partial


def doubling_sum(value, axis, levels):
    for bit in range(levels):
        value = value + from_partner(value, axis, bit)
    return value


def head_swap(value):
    return lax.ppermute(value, "head", [(0, 1), (1, 0)])


def flip_blocks(array, level):
    step = 1 << level
    shaped = array.reshape((array.shape[0] // (2 * step), 2, step) + array.shape[1:])
    return jnp.flip(shaped, axis=1).reshape(array.shape)


def shards(nodes, gain, w_query, w_key, w_value, w_out, links, cotangent):
    blocks_dev = links.shape[0]
    local_levels = blocks_dev.bit_length() - 1
    graph_levels = lax.axis_size("graph").bit_length() - 1
    node_rows, width = nodes.shape
    block_len = node_rows // blocks_dev
    columns = w_query.shape[1]
    local_heads = columns // HEAD_DIM
    score_scale = HEAD_DIM ** (-0.5)
    contract_rows = (((0,), (0,)), ((), ()))
    wide_nodes = nodes.astype(jnp.float32)
    inverse = lax.rsqrt(jnp.mean(wide_nodes * wide_nodes, axis=1, keepdims=True) + EPS)
    normed = (wide_nodes * inverse * gain).astype(jnp.bfloat16)
    query = jnp.dot(normed, w_query, preferred_element_type=jnp.float32).astype(jnp.bfloat16)
    keys = jnp.dot(normed, w_key, preferred_element_type=jnp.float32).astype(jnp.bfloat16)
    values = jnp.dot(normed, w_value, preferred_element_type=jnp.float32).astype(jnp.bfloat16)
    key_blocks = keys.reshape(blocks_dev, block_len, columns)
    value_blocks = values.reshape(blocks_dev, block_len, columns)
    bit_order = list(range(graph_levels))
    remote = {}
    for bit in bit_order:
        remote[bit] = from_partner((key_blocks, value_blocks), "graph", bit)
    key_slots = (
        [key_blocks]
        + [flip_blocks(key_blocks, level) for level in range(local_levels)]
        + [remote[bit][0] for bit in range(graph_levels)]
    )
    value_slots = (
        [value_blocks]
        + [flip_blocks(value_blocks, level) for level in range(local_levels)]
        + [remote[bit][1] for bit in range(graph_levels)]
    )
    slot_count = len(key_slots)
    head_shape = (blocks_dev, block_len, local_heads, HEAD_DIM)
    keys_all = jnp.stack(key_slots).reshape((slot_count,) + head_shape)
    values_all = jnp.stack(value_slots).reshape((slot_count,) + head_shape)
    query_heads = query.reshape(head_shape)
    active = jnp.concatenate([jnp.ones((blocks_dev, 1), jnp.int32), links], axis=1)
    allowed = active[:, None, None, :, None] > 0
    scores = (
        jnp.einsum("bqhe,sbkhe->bhqsk", query_heads, keys_all, preferred_element_type=jnp.float32)
        * score_scale
    )
    scores = jnp.where(allowed, scores, NEG)
    top = jnp.max(scores, axis=(3, 4), keepdims=True)
    raised = jnp.exp(scores - top)
    total = jnp.sum(raised, axis=(3, 4), keepdims=True)
    probs = raised / total
    probs_low = probs.astype(jnp.bfloat16)
    attended = jnp.einsum(
        "bhqsk,sbkhe->bqhe", probs_low, values_all, preferred_element_type=jnp.float32
    )
    attended = attended.astype(jnp.bfloat16).reshape(node_rows, columns)
    head_me = lax.axis_index("head")
    mixed_terms = jnp.dot(attended, w_out, preferred_element_type=jnp.float32)
    own_mixed = lax.dynamic_slice_in_dim(mixed_terms, head_me * columns, columns, 1)
    other_mixed = lax.dynamic_slice_in_dim(mixed_terms, (1 - head_me) * columns, columns, 1)
    mixed = (own_mixed + head_swap(other_mixed)).astype(jnp.bfloat16)
    grad_attended = jnp.dot(cotangent, w_out.T, preferred_element_type=jnp.float32).astype(
        jnp.bfloat16
    )
    out_terms = lax.dot_general(
        bit_major_rows(cotangent, graph_levels), attended, contract_rows,
        preferred_element_type=jnp.float32,
    )
    w_out_grad = halving_sum(out_terms, "graph", graph_levels).T
    grad_heads = grad_attended.reshape(head_shape)
    grad_probs = jnp.einsum(
        "bqhe,sbkhe->bhqsk", grad_heads, values_all, preferred_element_type=jnp.float32
    )
    delta = jnp.sum(probs * grad_probs, axis=(3, 4), keepdims=True)
    grad_scores = probs * (grad_probs - delta) * score_scale
    grad_query = jnp.einsum("bhqsk,sbkhe->bqhe", grad_scores, keys_all.astype(jnp.float32))
    grad_query = grad_query.astype(jnp.bfloat16).reshape(node_rows, columns)
    slot_block_shape = (slot_count, blocks_dev, block_len, columns)
    key_terms = jnp.einsum("bhqsk,bqhe->sbkhe", grad_scores, query_heads.astype(jnp.float32))
    key_terms = key_terms.astype(jnp.bfloat16).reshape(slot_block_shape)
    value_terms = jnp.einsum(
        "bhqsk,bqhe->sbkhe", probs_low, grad_heads, preferred_element_type=jnp.float32
    )
    value_terms = value_terms.astype(jnp.bfloat16).reshape(slot_block_shape)
    grad_key = key_terms[0].astype(jnp.float32)
    grad_value = value_terms[0].astype(jnp.float32)
    returned = {}
    for bit in bit_order:
        slot = 1 + local_levels + bit
        returned[bit] = from_partner((key_terms[slot], value_terms[slot]), "graph", bit)
    for bit in range(graph_levels):
        grad_key = grad_key + returned[bit][0].astype(jnp.float32)
        grad_value = grad_value + returned[bit][1].astype(jnp.float32)
    grad_key = grad_key.astype(jnp.bfloat16).reshape(node_rows, columns)
    grad_value = grad_value.astype(jnp.bfloat16).reshape(node_rows, columns)
    joined_rows = halving_sum(
        lax.dot_general(
            bit_major_rows(normed, graph_levels),
            jnp.concatenate([grad_query, grad_key, grad_value], axis=1),
            contract_rows,
            preferred_element_type=jnp.float32,
        ),
        "graph",
        graph_levels,
    )
    w_query_grad = joined_rows[:, :columns]
    w_key_grad = joined_rows[:, columns : 2 * columns]
    w_value_grad = joined_rows[:, 2 * columns :]
    feature_terms = (
        jnp.dot(grad_query, w_query.T, preferred_element_type=jnp.float32)
        + jnp.dot(grad_key, w_key.T, preferred_element_type=jnp.float32)
        + jnp.dot(grad_value, w_value.T, preferred_element_type=jnp.float32)
    )
    grad_normed = feature_terms + head_swap(feature_terms)
    gain_grad = doubling_sum(
        jnp.sum(grad_normed * wide_nodes * inverse, axis=0), "graph", graph_levels
    )
    scaled = grad_normed * gain
    nodes_grad = (
        inverse
        * (
            scaled
            - wide_nodes * inverse * inverse * jnp.mean(scaled * wide_nodes, axis=1, keepdims=True)
        )
    ).astype(jnp.bfloat16)
    return (mixed, nodes_grad, gain_grad, w_query_grad, w_key_grad, w_value_grad, w_out_grad)


def solution(mesh):
    in_specs = (
        P("graph", None),
        P(),
        P(None, "head"),
        P(None, "head"),
        P(None, "head"),
        P("head", None),
        P("graph", None),
        P("graph", None),
    )
    out_specs = (
        P("graph", "head"),
        P("graph", None),
        P(),
        P("graph", "head"),
        P("graph", "head"),
        P("graph", "head"),
        P("head", "graph"),
    )
    return jax.shard_map(shards, mesh=mesh, in_specs=in_specs, out_specs=out_specs, check_vma=False)
```

```python
import jax
import jax.numpy as jnp
from jax import lax
from jax.sharding import PartitionSpec as P

HEAD_DIM = 64


EPS = 1e-05
NEG = -1e30


def from_partner(value, axis, apart):
    mask = 2**apart
    pairs = [(source, source ^ mask) for source in range(lax.axis_size(axis))]
    return lax.ppermute(value, axis, pairs)


def bit_major_rows(matrix, order):
    rows, width = matrix.shape
    levels = len(order)
    inner = width >> levels
    shaped = matrix.reshape((rows,) + (2,) * levels + (inner,))
    axes = (0,) + tuple(levels - bit for bit in order) + (levels + 1,)
    return shaped.transpose(axes).reshape(rows, width)


def halving_sum(partial, axis, order):
    me = lax.axis_index(axis)
    for bit in order:
        half = partial.shape[0] // 2
        mine = (me >> bit) & 1
        keep = lax.dynamic_slice_in_dim(partial, mine * half, half, 0)
        send = lax.dynamic_slice_in_dim(partial, (1 - mine) * half, half, 0)
        got = from_partner(send.astype(jnp.bfloat16), axis, bit)
        partial = keep + got.astype(jnp.float32)
    return partial


def split_orders(levels):
    first = tuple(range(levels))
    if levels < 3:
        return first, first
    return first, (0, 2, 1) + first[3:]


def scatter_rows(pairs, axis, levels):
    contract = (((0,), (0,)), ((), ()))
    chunks = []
    for index, order in enumerate(split_orders(levels)):
        pieces = []
        for left, right in pairs:
            cut = right.shape[1] // 2
            piece = right[:, index * cut : (index + 1) * cut]
            pieces.append(
                lax.dot_general(
                    bit_major_rows(left, order), piece, contract,
                    preferred_element_type=jnp.float32,
                )
            )
        chunks.append(halving_sum(jnp.concatenate(pieces, axis=1), axis, order))
    results = []
    offset = 0
    for left, right in pairs:
        cut = right.shape[1] // 2
        results.append(
            jnp.concatenate([chunk[:, offset : offset + cut] for chunk in chunks], axis=1)
        )
        offset += cut
    return results


def doubling_sum(value, axis, levels):
    for bit in range(levels):
        value = value + from_partner(value, axis, bit)
    return value


def head_swap(value):
    return lax.ppermute(value, "head", [(0, 1), (1, 0)])


def flip_blocks(array, level):
    step = 1 << level
    shaped = array.reshape((array.shape[0] // (2 * step), 2, step) + array.shape[1:])
    return jnp.flip(shaped, axis=1).reshape(array.shape)


def shards(nodes, gain, w_query, w_key, w_value, w_out, links, cotangent):
    blocks_dev = links.shape[0]
    local_levels = blocks_dev.bit_length() - 1
    graph_levels = lax.axis_size("graph").bit_length() - 1
    node_rows, width = nodes.shape
    block_len = node_rows // blocks_dev
    columns = w_query.shape[1]
    local_heads = columns // HEAD_DIM
    score_scale = HEAD_DIM ** (-0.5)
    contract_rows = (((0,), (0,)), ((), ()))
    wide_nodes = nodes.astype(jnp.float32)
    inverse = lax.rsqrt(jnp.mean(wide_nodes * wide_nodes, axis=1, keepdims=True) + EPS)
    normed = (wide_nodes * inverse * gain).astype(jnp.bfloat16)
    query = jnp.dot(normed, w_query, preferred_element_type=jnp.float32).astype(jnp.bfloat16)
    keys = jnp.dot(normed, w_key, preferred_element_type=jnp.float32).astype(jnp.bfloat16)
    values = jnp.dot(normed, w_value, preferred_element_type=jnp.float32).astype(jnp.bfloat16)
    key_blocks = keys.reshape(blocks_dev, block_len, columns)
    value_blocks = values.reshape(blocks_dev, block_len, columns)
    bit_order = list(range(graph_levels))
    remote = {}
    for bit in bit_order:
        remote[bit] = from_partner((key_blocks, value_blocks), "graph", bit)
    key_slots = (
        [key_blocks]
        + [flip_blocks(key_blocks, level) for level in range(local_levels)]
        + [remote[bit][0] for bit in range(graph_levels)]
    )
    value_slots = (
        [value_blocks]
        + [flip_blocks(value_blocks, level) for level in range(local_levels)]
        + [remote[bit][1] for bit in range(graph_levels)]
    )
    slot_count = len(key_slots)
    head_shape = (blocks_dev, block_len, local_heads, HEAD_DIM)
    keys_all = jnp.stack(key_slots).reshape((slot_count,) + head_shape)
    values_all = jnp.stack(value_slots).reshape((slot_count,) + head_shape)
    query_heads = query.reshape(head_shape)
    active = jnp.concatenate([jnp.ones((blocks_dev, 1), jnp.int32), links], axis=1)
    allowed = active[:, None, None, :, None] > 0
    scores = (
        jnp.einsum("bqhe,sbkhe->bhqsk", query_heads, keys_all, preferred_element_type=jnp.float32)
        * score_scale
    )
    scores = jnp.where(allowed, scores, NEG)
    top = jnp.max(scores, axis=(3, 4), keepdims=True)
    raised = jnp.exp(scores - top)
    total = jnp.sum(raised, axis=(3, 4), keepdims=True)
    probs = raised / total
    probs_low = probs.astype(jnp.bfloat16)
    attended = jnp.einsum(
        "bhqsk,sbkhe->bqhe", probs_low, values_all, preferred_element_type=jnp.float32
    )
    attended = attended.astype(jnp.bfloat16).reshape(node_rows, columns)
    head_me = lax.axis_index("head")
    mixed_terms = jnp.dot(attended, w_out, preferred_element_type=jnp.float32)
    own_mixed = lax.dynamic_slice_in_dim(mixed_terms, head_me * columns, columns, 1)
    other_mixed = lax.dynamic_slice_in_dim(mixed_terms, (1 - head_me) * columns, columns, 1)
    mixed = (own_mixed + head_swap(other_mixed)).astype(jnp.bfloat16)
    grad_attended = jnp.dot(cotangent, w_out.T, preferred_element_type=jnp.float32).astype(
        jnp.bfloat16
    )
    grad_heads = grad_attended.reshape(head_shape)
    grad_probs = jnp.einsum(
        "bqhe,sbkhe->bhqsk", grad_heads, values_all, preferred_element_type=jnp.float32
    )
    delta = jnp.sum(probs * grad_probs, axis=(3, 4), keepdims=True)
    grad_scores = probs * (grad_probs - delta) * score_scale
    grad_query = jnp.einsum("bhqsk,sbkhe->bqhe", grad_scores, keys_all.astype(jnp.float32))
    grad_query = grad_query.astype(jnp.bfloat16).reshape(node_rows, columns)
    slot_block_shape = (slot_count, blocks_dev, block_len, columns)
    key_terms = jnp.einsum("bhqsk,bqhe->sbkhe", grad_scores, query_heads.astype(jnp.float32))
    key_terms = key_terms.astype(jnp.bfloat16).reshape(slot_block_shape)
    value_terms = jnp.einsum(
        "bhqsk,bqhe->sbkhe", probs_low, grad_heads, preferred_element_type=jnp.float32
    )
    value_terms = value_terms.astype(jnp.bfloat16).reshape(slot_block_shape)
    grad_key = key_terms[0].astype(jnp.float32)
    grad_value = value_terms[0].astype(jnp.float32)
    returned = {}
    for bit in bit_order:
        slot = 1 + local_levels + bit
        returned[bit] = from_partner((key_terms[slot], value_terms[slot]), "graph", bit)
    for bit in range(graph_levels):
        grad_key = grad_key + returned[bit][0].astype(jnp.float32)
        grad_value = grad_value + returned[bit][1].astype(jnp.float32)
    grad_key = grad_key.astype(jnp.bfloat16).reshape(node_rows, columns)
    grad_value = grad_value.astype(jnp.bfloat16).reshape(node_rows, columns)
    w_out_rows, w_query_grad = scatter_rows(
        [(cotangent, attended), (normed, grad_query)], "graph", graph_levels
    )
    w_out_grad = w_out_rows.T
    w_key_grad, w_value_grad = scatter_rows(
        [(normed, grad_key), (normed, grad_value)], "graph", graph_levels
    )
    feature_terms = (
        jnp.dot(grad_query, w_query.T, preferred_element_type=jnp.float32)
        + jnp.dot(grad_key, w_key.T, preferred_element_type=jnp.float32)
        + jnp.dot(grad_value, w_value.T, preferred_element_type=jnp.float32)
    )
    low_terms = feature_terms.astype(jnp.bfloat16)
    grad_normed = low_terms.astype(jnp.float32) + head_swap(low_terms).astype(jnp.float32)
    gain_grad = doubling_sum(
        jnp.sum(grad_normed * wide_nodes * inverse, axis=0), "graph", graph_levels
    )
    scaled = grad_normed * gain
    nodes_grad = (
        inverse
        * (
            scaled
            - wide_nodes * inverse * inverse * jnp.mean(scaled * wide_nodes, axis=1, keepdims=True)
        )
    ).astype(jnp.bfloat16)
    return (mixed, nodes_grad, gain_grad, w_query_grad, w_key_grad, w_value_grad, w_out_grad)


def solution(mesh):
    in_specs = (
        P("graph", None),
        P(),
        P(None, "head"),
        P(None, "head"),
        P(None, "head"),
        P("head", None),
        P("graph", None),
        P("graph", None),
    )
    out_specs = (
        P("graph", "head"),
        P("graph", None),
        P(),
        P("graph", "head"),
        P("graph", "head"),
        P("graph", "head"),
        P("head", "graph"),
    )
    return jax.shard_map(shards, mesh=mesh, in_specs=in_specs, out_specs=out_specs, check_vma=False)
```

```python
import jax
import jax.numpy as jnp
from jax import lax
from jax.sharding import PartitionSpec as P

HEAD_DIM = 64


EPS = 1e-05
NEG = -1e30


def from_partner(value, axis, apart):
    mask = 2**apart
    pairs = [(source, source ^ mask) for source in range(lax.axis_size(axis))]
    return lax.ppermute(value, axis, pairs)


def bit_major_rows(matrix, order):
    rows, width = matrix.shape
    levels = len(order)
    inner = width >> levels
    shaped = matrix.reshape((rows,) + (2,) * levels + (inner,))
    axes = (0,) + tuple(levels - bit for bit in order) + (levels + 1,)
    return shaped.transpose(axes).reshape(rows, width)


def halving_step(partial, axis, bit):
    me = lax.axis_index(axis)
    half = partial.shape[0] // 2
    mine = (me >> bit) & 1
    keep = lax.dynamic_slice_in_dim(partial, mine * half, half, 0)
    send = lax.dynamic_slice_in_dim(partial, (1 - mine) * half, half, 0)
    got = from_partner(send.astype(jnp.bfloat16), axis, bit)
    return keep + got.astype(jnp.float32)


def split_orders(levels):
    first = tuple(range(levels))
    if levels < 3:
        return first, first
    return first, (0, 2, 1) + first[3:]


def scatter_begin(pairs, levels):
    contract = (((0,), (0,)), ((), ()))
    chunks = []
    for index, order in enumerate(split_orders(levels)):
        pieces = []
        for left, right in pairs:
            cut = right.shape[1] // 2
            piece = right[:, index * cut : (index + 1) * cut]
            pieces.append(
                lax.dot_general(
                    bit_major_rows(left, order), piece, contract,
                    preferred_element_type=jnp.float32,
                )
            )
        chunks.append(jnp.concatenate(pieces, axis=1))
    return chunks, 0


def scatter_step(state, axis, levels):
    chunks, done = state
    if done == levels:
        return state
    orders = split_orders(levels)
    return [halving_step(c, axis, o[done]) for c, o in zip(chunks, orders)], done + 1


def scatter_end(state, pairs, axis, levels):
    while state[1] < levels:
        state = scatter_step(state, axis, levels)
    chunks = state[0]
    results = []
    offset = 0
    for left, right in pairs:
        cut = right.shape[1] // 2
        results.append(
            jnp.concatenate([chunk[:, offset : offset + cut] for chunk in chunks], axis=1)
        )
        offset += cut
    return results


def doubling_sum(value, axis, levels):
    for bit in range(levels):
        value = value + from_partner(value, axis, bit)
    return value


def head_swap(value):
    return lax.ppermute(value, "head", [(0, 1), (1, 0)])


def flip_blocks(array, level):
    step = 1 << level
    shaped = array.reshape((array.shape[0] // (2 * step), 2, step) + array.shape[1:])
    return jnp.flip(shaped, axis=1).reshape(array.shape)


def shards(nodes, gain, w_query, w_key, w_value, w_out, links, cotangent):
    blocks_dev = links.shape[0]
    local_levels = blocks_dev.bit_length() - 1
    graph_levels = lax.axis_size("graph").bit_length() - 1
    node_rows, width = nodes.shape
    block_len = node_rows // blocks_dev
    columns = w_query.shape[1]
    local_heads = columns // HEAD_DIM
    score_scale = HEAD_DIM ** (-0.5)
    contract_rows = (((0,), (0,)), ((), ()))
    wide_nodes = nodes.astype(jnp.float32)
    inverse = lax.rsqrt(jnp.mean(wide_nodes * wide_nodes, axis=1, keepdims=True) + EPS)
    normed = (wide_nodes * inverse * gain).astype(jnp.bfloat16)
    query = jnp.dot(normed, w_query, preferred_element_type=jnp.float32).astype(jnp.bfloat16)
    keys = jnp.dot(normed, w_key, preferred_element_type=jnp.float32).astype(jnp.bfloat16)
    values = jnp.dot(normed, w_value, preferred_element_type=jnp.float32).astype(jnp.bfloat16)
    key_blocks = keys.reshape(blocks_dev, block_len, columns)
    value_blocks = values.reshape(blocks_dev, block_len, columns)
    bit_order = list(range(graph_levels))
    remote = {}
    for bit in bit_order:
        remote[bit] = from_partner((key_blocks, value_blocks), "graph", bit)
    key_slots = (
        [key_blocks]
        + [flip_blocks(key_blocks, level) for level in range(local_levels)]
        + [remote[bit][0] for bit in range(graph_levels)]
    )
    value_slots = (
        [value_blocks]
        + [flip_blocks(value_blocks, level) for level in range(local_levels)]
        + [remote[bit][1] for bit in range(graph_levels)]
    )
    slot_count = len(key_slots)
    head_shape = (blocks_dev, block_len, local_heads, HEAD_DIM)
    keys_all = jnp.stack(key_slots).reshape((slot_count,) + head_shape)
    values_all = jnp.stack(value_slots).reshape((slot_count,) + head_shape)
    query_heads = query.reshape(head_shape)
    active = jnp.concatenate([jnp.ones((blocks_dev, 1), jnp.int32), links], axis=1)
    allowed = active[:, None, None, :, None] > 0
    scores = (
        jnp.einsum("bqhe,sbkhe->bhqsk", query_heads, keys_all, preferred_element_type=jnp.float32)
        * score_scale
    )
    scores = jnp.where(allowed, scores, NEG)
    top = jnp.max(scores, axis=(3, 4), keepdims=True)
    raised = jnp.exp(scores - top)
    total = jnp.sum(raised, axis=(3, 4), keepdims=True)
    probs = raised / total
    probs_low = probs.astype(jnp.bfloat16)
    attended = jnp.einsum(
        "bhqsk,sbkhe->bqhe", probs_low, values_all, preferred_element_type=jnp.float32
    )
    attended = attended.astype(jnp.bfloat16).reshape(node_rows, columns)
    head_me = lax.axis_index("head")
    mixed_terms = jnp.dot(attended, w_out, preferred_element_type=jnp.float32)
    own_mixed = lax.dynamic_slice_in_dim(mixed_terms, head_me * columns, columns, 1)
    other_mixed = lax.dynamic_slice_in_dim(mixed_terms, (1 - head_me) * columns, columns, 1)
    mixed = (own_mixed + head_swap(other_mixed)).astype(jnp.bfloat16)
    grad_attended = jnp.dot(cotangent, w_out.T, preferred_element_type=jnp.float32).astype(
        jnp.bfloat16
    )
    grad_heads = grad_attended.reshape(head_shape)
    grad_probs = jnp.einsum(
        "bqhe,sbkhe->bhqsk", grad_heads, values_all, preferred_element_type=jnp.float32
    )
    delta = jnp.sum(probs * grad_probs, axis=(3, 4), keepdims=True)
    grad_scores = probs * (grad_probs - delta) * score_scale
    grad_query = jnp.einsum("bhqsk,sbkhe->bqhe", grad_scores, keys_all.astype(jnp.float32))
    grad_query = grad_query.astype(jnp.bfloat16).reshape(node_rows, columns)
    slot_block_shape = (slot_count, blocks_dev, block_len, columns)
    key_terms = jnp.einsum("bhqsk,bqhe->sbkhe", grad_scores, query_heads.astype(jnp.float32))
    key_terms = key_terms.astype(jnp.bfloat16).reshape(slot_block_shape)
    value_terms = jnp.einsum(
        "bhqsk,bqhe->sbkhe", probs_low, grad_heads, preferred_element_type=jnp.float32
    )
    value_terms = value_terms.astype(jnp.bfloat16).reshape(slot_block_shape)
    grad_key = key_terms[0].astype(jnp.float32)
    grad_value = value_terms[0].astype(jnp.float32)
    out_pairs = [(cotangent, attended), (normed, grad_query)]
    early = scatter_step(scatter_begin(out_pairs, graph_levels), "graph", graph_levels)
    early_chunks, key_terms, value_terms = lax.optimization_barrier(
        (early[0], key_terms, value_terms)
    )
    early = scatter_step((early_chunks, early[1]), "graph", graph_levels)
    returned = {}
    for bit in bit_order:
        slot = 1 + local_levels + bit
        returned[bit] = from_partner((key_terms[slot], value_terms[slot]), "graph", bit)
    for bit in range(graph_levels):
        grad_key = grad_key + returned[bit][0].astype(jnp.float32)
        grad_value = grad_value + returned[bit][1].astype(jnp.float32)
    grad_key = grad_key.astype(jnp.bfloat16).reshape(node_rows, columns)
    grad_value = grad_value.astype(jnp.bfloat16).reshape(node_rows, columns)
    early_chunks, grad_key, grad_value = lax.optimization_barrier(
        (early[0], grad_key, grad_value)
    )
    early = scatter_step((early_chunks, early[1]), "graph", graph_levels)
    kv_pairs = [(normed, grad_key), (normed, grad_value)]
    late = scatter_step(scatter_begin(kv_pairs, graph_levels), "graph", graph_levels)
    w_out_rows, w_query_grad = scatter_end(early, out_pairs, "graph", graph_levels)
    w_out_grad = w_out_rows.T
    late = scatter_step(late, "graph", graph_levels)
    feature_terms = (
        jnp.dot(grad_query, w_query.T, preferred_element_type=jnp.float32)
        + jnp.dot(grad_key, w_key.T, preferred_element_type=jnp.float32)
        + jnp.dot(grad_value, w_value.T, preferred_element_type=jnp.float32)
    )
    low_terms = feature_terms.astype(jnp.bfloat16)
    grad_normed = low_terms.astype(jnp.float32) + head_swap(low_terms).astype(jnp.float32)
    gain_terms = jnp.sum(grad_normed * wide_nodes * inverse, axis=0)
    gain_terms, late_chunks = lax.optimization_barrier((gain_terms, late[0]))
    w_key_grad, w_value_grad = scatter_end((late_chunks, late[1]), kv_pairs, "graph", graph_levels)
    gain_grad = doubling_sum(gain_terms, "graph", graph_levels)
    scaled = grad_normed * gain
    nodes_grad = (
        inverse
        * (
            scaled
            - wide_nodes * inverse * inverse * jnp.mean(scaled * wide_nodes, axis=1, keepdims=True)
        )
    ).astype(jnp.bfloat16)
    return (mixed, nodes_grad, gain_grad, w_query_grad, w_key_grad, w_value_grad, w_out_grad)


def solution(mesh):
    in_specs = (
        P("graph", None),
        P(),
        P(None, "head"),
        P(None, "head"),
        P(None, "head"),
        P("head", None),
        P("graph", None),
        P("graph", None),
    )
    out_specs = (
        P("graph", "head"),
        P("graph", None),
        P(),
        P("graph", "head"),
        P("graph", "head"),
        P("graph", "head"),
        P("head", "graph"),
    )
    return jax.shard_map(shards, mesh=mesh, in_specs=in_specs, out_specs=out_specs, check_vma=False)
```

```python
import jax
import jax.numpy as jnp
from jax import lax
from jax.sharding import PartitionSpec as P

HEAD_DIM = 64


EPS = 1e-05
NEG = -1e30


def from_partner(value, axis, apart):
    mask = 2**apart
    pairs = [(source, source ^ mask) for source in range(lax.axis_size(axis))]
    return lax.ppermute(value, axis, pairs)


def bit_major_rows(matrix, order):
    rows, width = matrix.shape
    levels = len(order)
    inner = width >> levels
    shaped = matrix.reshape((rows,) + (2,) * levels + (inner,))
    axes = (0,) + tuple(levels - bit for bit in order) + (levels + 1,)
    return shaped.transpose(axes).reshape(rows, width)


def halving_sum(partial, axis, order):
    me = lax.axis_index(axis)
    for bit in order:
        half = partial.shape[0] // 2
        mine = (me >> bit) & 1
        keep = lax.dynamic_slice_in_dim(partial, mine * half, half, 0)
        send = lax.dynamic_slice_in_dim(partial, (1 - mine) * half, half, 0)
        got = from_partner(send.astype(jnp.bfloat16), axis, bit)
        partial = keep + got.astype(jnp.float32)
    return partial


def split_orders(levels):
    first = tuple(range(levels))
    if levels < 3:
        return first, first
    return first, (0, 2, 1) + first[3:]


def scatter_rows(pairs, axis, levels):
    contract = (((0,), (0,)), ((), ()))
    chunks = []
    for index, order in enumerate(split_orders(levels)):
        pieces = []
        for left, right in pairs:
            cut = right.shape[1] // 2
            piece = right[:, index * cut : (index + 1) * cut]
            pieces.append(
                lax.dot_general(
                    bit_major_rows(left, order), piece, contract,
                    preferred_element_type=jnp.float32,
                )
            )
        chunks.append(halving_sum(jnp.concatenate(pieces, axis=1), axis, order))
    results = []
    offset = 0
    for left, right in pairs:
        cut = right.shape[1] // 2
        results.append(
            jnp.concatenate([chunk[:, offset : offset + cut] for chunk in chunks], axis=1)
        )
        offset += cut
    return results


def doubling_sum(value, axis, levels):
    for bit in range(levels):
        value = value + from_partner(value, axis, bit)
    return value


def head_swap(value):
    return lax.ppermute(value, "head", [(0, 1), (1, 0)])


def flip_blocks(array, level):
    step = 1 << level
    shaped = array.reshape((array.shape[0] // (2 * step), 2, step) + array.shape[1:])
    return jnp.flip(shaped, axis=1).reshape(array.shape)


def shards(nodes, gain, w_query, w_key, w_value, w_out, links, cotangent):
    blocks_dev = links.shape[0]
    local_levels = blocks_dev.bit_length() - 1
    graph_levels = lax.axis_size("graph").bit_length() - 1
    node_rows, width = nodes.shape
    block_len = node_rows // blocks_dev
    columns = w_query.shape[1]
    local_heads = columns // HEAD_DIM
    score_scale = HEAD_DIM ** (-0.5)
    contract_rows = (((0,), (0,)), ((), ()))
    wide_nodes = nodes.astype(jnp.float32)
    inverse = lax.rsqrt(jnp.mean(wide_nodes * wide_nodes, axis=1, keepdims=True) + EPS)
    normed = (wide_nodes * inverse * gain).astype(jnp.bfloat16)
    query = jnp.dot(normed, w_query, preferred_element_type=jnp.float32).astype(jnp.bfloat16)
    keys = jnp.dot(normed, w_key, preferred_element_type=jnp.float32).astype(jnp.bfloat16)
    values = jnp.dot(normed, w_value, preferred_element_type=jnp.float32).astype(jnp.bfloat16)
    key_blocks = keys.reshape(blocks_dev, block_len, columns)
    value_blocks = values.reshape(blocks_dev, block_len, columns)
    bit_order = list(range(graph_levels))[::-1]
    joined_blocks = jnp.concatenate([key_blocks, value_blocks], axis=2)
    remote = {}
    for bit in bit_order:
        got = from_partner(joined_blocks, "graph", bit)
        remote[bit] = (got[:, :, :columns], got[:, :, columns:])
    key_slots = (
        [key_blocks]
        + [flip_blocks(key_blocks, level) for level in range(local_levels)]
        + [remote[bit][0] for bit in range(graph_levels)]
    )
    value_slots = (
        [value_blocks]
        + [flip_blocks(value_blocks, level) for level in range(local_levels)]
        + [remote[bit][1] for bit in range(graph_levels)]
    )
    slot_count = len(key_slots)
    head_shape = (blocks_dev, block_len, local_heads, HEAD_DIM)
    keys_all = jnp.stack(key_slots).reshape((slot_count,) + head_shape)
    values_all = jnp.stack(value_slots).reshape((slot_count,) + head_shape)
    query_heads = query.reshape(head_shape)
    active = jnp.concatenate([jnp.ones((blocks_dev, 1), jnp.int32), links], axis=1)
    allowed = active[:, None, None, :, None] > 0
    scores = (
        jnp.einsum("bqhe,sbkhe->bhqsk", query_heads, keys_all, preferred_element_type=jnp.float32)
        * score_scale
    )
    scores = jnp.where(allowed, scores, NEG)
    top = jnp.max(scores, axis=(3, 4), keepdims=True)
    raised = jnp.exp(scores - top)
    total = jnp.sum(raised, axis=(3, 4), keepdims=True)
    probs = raised / total
    probs_low = probs.astype(jnp.bfloat16)
    attended = jnp.einsum(
        "bhqsk,sbkhe->bqhe", probs_low, values_all, preferred_element_type=jnp.float32
    )
    attended = attended.astype(jnp.bfloat16).reshape(node_rows, columns)
    head_me = lax.axis_index("head")
    mixed_terms = jnp.dot(attended, w_out, preferred_element_type=jnp.float32)
    own_mixed = lax.dynamic_slice_in_dim(mixed_terms, head_me * columns, columns, 1)
    other_mixed = lax.dynamic_slice_in_dim(mixed_terms, (1 - head_me) * columns, columns, 1)
    mixed = (own_mixed + head_swap(other_mixed)).astype(jnp.bfloat16)
    grad_attended = jnp.dot(cotangent, w_out.T, preferred_element_type=jnp.float32).astype(
        jnp.bfloat16
    )
    grad_heads = grad_attended.reshape(head_shape)
    grad_probs = jnp.einsum(
        "bqhe,sbkhe->bhqsk", grad_heads, values_all, preferred_element_type=jnp.float32
    )
    delta = jnp.sum(probs * grad_probs, axis=(3, 4), keepdims=True)
    grad_scores = probs * (grad_probs - delta) * score_scale
    grad_query = jnp.einsum("bhqsk,sbkhe->bqhe", grad_scores, keys_all.astype(jnp.float32))
    grad_query = grad_query.astype(jnp.bfloat16).reshape(node_rows, columns)
    slot_block_shape = (slot_count, blocks_dev, block_len, columns)
    key_terms = jnp.einsum("bhqsk,bqhe->sbkhe", grad_scores, query_heads.astype(jnp.float32))
    key_terms = key_terms.astype(jnp.bfloat16).reshape(slot_block_shape)
    value_terms = jnp.einsum(
        "bhqsk,bqhe->sbkhe", probs_low, grad_heads, preferred_element_type=jnp.float32
    )
    value_terms = value_terms.astype(jnp.bfloat16).reshape(slot_block_shape)
    grad_key = key_terms[0].astype(jnp.float32)
    grad_value = value_terms[0].astype(jnp.float32)
    returned = {}
    for bit in bit_order:
        slot = 1 + local_levels + bit
        got = from_partner(
            jnp.concatenate([key_terms[slot], value_terms[slot]], axis=2), "graph", bit
        )
        returned[bit] = (got[:, :, :columns], got[:, :, columns:])
    for bit in range(graph_levels):
        grad_key = grad_key + returned[bit][0].astype(jnp.float32)
        grad_value = grad_value + returned[bit][1].astype(jnp.float32)
    grad_key = grad_key.astype(jnp.bfloat16).reshape(node_rows, columns)
    grad_value = grad_value.astype(jnp.bfloat16).reshape(node_rows, columns)
    w_out_rows, w_query_grad = scatter_rows(
        [(cotangent, attended), (normed, grad_query)], "graph", graph_levels
    )
    w_out_grad = w_out_rows.T
    w_key_grad, w_value_grad = scatter_rows(
        [(normed, grad_key), (normed, grad_value)], "graph", graph_levels
    )
    feature_terms = (
        jnp.dot(grad_query, w_query.T, preferred_element_type=jnp.float32)
        + jnp.dot(grad_key, w_key.T, preferred_element_type=jnp.float32)
        + jnp.dot(grad_value, w_value.T, preferred_element_type=jnp.float32)
    )
    low_terms = feature_terms.astype(jnp.bfloat16)
    grad_normed = low_terms.astype(jnp.float32) + head_swap(low_terms).astype(jnp.float32)
    gain_terms = jnp.sum(low_terms.astype(jnp.float32) * wide_nodes * inverse, axis=0)
    gain_grad = doubling_sum(gain_terms + head_swap(gain_terms), "graph", graph_levels)
    scaled = grad_normed * gain
    nodes_grad = (
        inverse
        * (
            scaled
            - wide_nodes * inverse * inverse * jnp.mean(scaled * wide_nodes, axis=1, keepdims=True)
        )
    ).astype(jnp.bfloat16)
    return (mixed, nodes_grad, gain_grad, w_query_grad, w_key_grad, w_value_grad, w_out_grad)


def solution(mesh):
    in_specs = (
        P("graph", None),
        P(),
        P(None, "head"),
        P(None, "head"),
        P(None, "head"),
        P("head", None),
        P("graph", None),
        P("graph", None),
    )
    out_specs = (
        P("graph", "head"),
        P("graph", None),
        P(),
        P("graph", "head"),
        P("graph", "head"),
        P("graph", "head"),
        P("head", "graph"),
    )
    return jax.shard_map(shards, mesh=mesh, in_specs=in_specs, out_specs=out_specs, check_vma=False)
```

```python
import jax
import jax.numpy as jnp
from jax import lax
from jax.sharding import PartitionSpec as P
import functools
from jax.experimental import pallas as pl
from jax.experimental.pallas import tpu as pltpu

HEAD_DIM = 64


EPS = 1e-05
NEG = -1e30


def from_partner(value, axis, apart):
    mask = 2**apart
    pairs = [(source, source ^ mask) for source in range(lax.axis_size(axis))]
    return lax.ppermute(value, axis, pairs)


def bit_major_rows(matrix, order):
    rows, width = matrix.shape
    levels = len(order)
    inner = width >> levels
    shaped = matrix.reshape((rows,) + (2,) * levels + (inner,))
    axes = (0,) + tuple(levels - bit for bit in order) + (levels + 1,)
    return shaped.transpose(axes).reshape(rows, width)


def halving_sum(partial, axis, order):
    me = lax.axis_index(axis)
    for bit in order:
        half = partial.shape[0] // 2
        mine = (me >> bit) & 1
        keep = lax.dynamic_slice_in_dim(partial, mine * half, half, 0)
        send = lax.dynamic_slice_in_dim(partial, (1 - mine) * half, half, 0)
        got = from_partner(send.astype(jnp.bfloat16), axis, bit)
        partial = keep + got.astype(jnp.float32)
    return partial


def split_orders(levels):
    first = tuple(range(levels))
    if levels < 3:
        return first, first
    return first, (0, 2, 1) + first[3:]


def scatter_rows(pairs, axis, levels):
    contract = (((0,), (0,)), ((), ()))
    chunks = []
    for index, order in enumerate(split_orders(levels)):
        pieces = []
        for left, right in pairs:
            cut = right.shape[1] // 2
            piece = right[:, index * cut : (index + 1) * cut]
            pieces.append(
                lax.dot_general(
                    bit_major_rows(left, order), piece, contract,
                    preferred_element_type=jnp.float32,
                )
            )
        chunks.append(halving_sum(jnp.concatenate(pieces, axis=1), axis, order))
    results = []
    offset = 0
    for left, right in pairs:
        cut = right.shape[1] // 2
        results.append(
            jnp.concatenate([chunk[:, offset : offset + cut] for chunk in chunks], axis=1)
        )
        offset += cut
    return results


def doubling_sum(value, axis, levels):
    for bit in range(levels):
        value = value + from_partner(value, axis, bit)
    return value


def head_swap(value):
    return lax.ppermute(value, "head", [(0, 1), (1, 0)])


def flip_blocks(array, level):
    step = 1 << level
    shaped = array.reshape((array.shape[0] // (2 * step), 2, step) + array.shape[1:])
    return jnp.flip(shaped, axis=1).reshape(array.shape)


def attention_kernel(slots, pairs, active_ref, q_ref, g_ref, *refs):
    key_refs = refs[:slots]
    value_refs = refs[slots : 2 * slots]
    att_ref, gq_ref = refs[2 * slots], refs[2 * slots + 1]
    term_refs = refs[2 * slots + 2 : 3 * slots + 2]
    block = pl.program_id(0)
    scale = HEAD_DIM ** (-0.5)
    width = 2 * HEAD_DIM
    lane = lax.broadcasted_iota(jnp.int32, (q_ref.shape[0], width), 1)
    low_lanes = lane < HEAD_DIM
    flags = [active_ref[block * slots + s] > 0 for s in range(slots)]
    contract_last = (((1,), (1,)), ((), ()))
    contract_first = (((0,), (0,)), ((), ()))
    highest = lax.Precision.HIGHEST
    for pair in range(pairs):
        cols = pl.ds(pair * width, width)
        q2 = q_ref[:, cols]
        g2 = g_ref[:, cols]
        keys = [key_refs[s][:, cols] for s in range(slots)]
        values = [value_refs[s][:, cols] for s in range(slots)]
        outs = []
        for half in range(2):
            sel = low_lanes if half == 0 else jnp.logical_not(low_lanes)
            qm = jnp.where(sel, q2, jnp.zeros_like(q2))
            gm = jnp.where(sel, g2, jnp.zeros_like(g2))
            scores = []
            for s in range(slots):
                raw = lax.dot_general(qm, keys[s], contract_last, preferred_element_type=jnp.float32) * scale
                scores.append(jnp.where(flags[s], raw, NEG))
            top = functools.reduce(jnp.maximum, [jnp.max(x, axis=1, keepdims=True) for x in scores])
            raised = [jnp.exp(x - top) for x in scores]
            total = functools.reduce(jnp.add, [jnp.sum(x, axis=1, keepdims=True) for x in raised])
            probs = [x / total for x in raised]
            probs_low = [x.astype(jnp.bfloat16) for x in probs]
            attended = functools.reduce(jnp.add, [
                jnp.dot(probs_low[s], values[s], preferred_element_type=jnp.float32) for s in range(slots)
            ])
            grad_probs = [
                lax.dot_general(gm, values[s], contract_last, preferred_element_type=jnp.float32)
                for s in range(slots)
            ]
            delta = functools.reduce(jnp.add, [
                jnp.sum(probs[s] * grad_probs[s], axis=1, keepdims=True) for s in range(slots)
            ])
            grad_scores = [probs[s] * (grad_probs[s] - delta) * scale for s in range(slots)]
            grad_query = functools.reduce(jnp.add, [
                jnp.dot(grad_scores[s], keys[s].astype(jnp.float32), precision=highest,
                        preferred_element_type=jnp.float32)
                for s in range(slots)
            ])
            key_terms = [
                lax.dot_general(grad_scores[s], q2.astype(jnp.float32), contract_first,
                                precision=highest, preferred_element_type=jnp.float32)
                for s in range(slots)
            ]
            value_terms = [
                lax.dot_general(probs_low[s], g2, contract_first, preferred_element_type=jnp.float32)
                for s in range(slots)
            ]
            outs.append((attended, grad_query, key_terms, value_terms))
        (att_a, gq_a, kt_a, vt_a), (att_b, gq_b, kt_b, vt_b) = outs
        att_ref[:, cols] = jnp.where(low_lanes, att_a, att_b).astype(att_ref.dtype)
        gq_ref[:, cols] = jnp.where(low_lanes, gq_a, gq_b).astype(gq_ref.dtype)
        for s in range(slots):
            term_refs[s][:, cols] = jnp.where(low_lanes, kt_a[s], kt_b[s]).astype(jnp.bfloat16)
            term_refs[s][:, pl.ds(q_ref.shape[1] + pair * width, width)] = jnp.where(
                low_lanes, vt_a[s], vt_b[s]
            ).astype(jnp.bfloat16)


def block_attention(active, query, grad, joined_slots):
    blocks, rows, columns = query.shape
    slots = len(joined_slots)
    pairs = columns // (2 * HEAD_DIM)
    spec = pl.BlockSpec((None, rows, columns), lambda b, act: (b, 0, 0))
    value_spec = pl.BlockSpec((None, rows, columns), lambda b, act: (b, 0, 1))
    wide_spec = pl.BlockSpec((None, rows, 2 * columns), lambda b, act: (b, 0, 0))
    shape = jax.ShapeDtypeStruct((blocks, rows, columns), jnp.bfloat16)
    wide = jax.ShapeDtypeStruct((blocks, rows, 2 * columns), jnp.bfloat16)
    outs = pl.pallas_call(
        functools.partial(attention_kernel, slots, pairs),
        grid_spec=pltpu.PrefetchScalarGridSpec(
            num_scalar_prefetch=1,
            grid=(blocks,),
            in_specs=[spec] * (2 + slots) + [value_spec] * slots,
            out_specs=[spec] * 2 + [wide_spec] * slots,
        ),
        out_shape=[shape] * 2 + [wide] * slots,
    )(active.reshape(-1), query, grad, *joined_slots, *joined_slots)
    return outs[0], outs[1], outs[2:]


def shards(nodes, gain, w_query, w_key, w_value, w_out, links, cotangent):
    blocks_dev = links.shape[0]
    local_levels = blocks_dev.bit_length() - 1
    graph_levels = lax.axis_size("graph").bit_length() - 1
    node_rows, width = nodes.shape
    block_len = node_rows // blocks_dev
    columns = w_query.shape[1]
    local_heads = columns // HEAD_DIM
    score_scale = HEAD_DIM ** (-0.5)
    contract_rows = (((0,), (0,)), ((), ()))
    wide_nodes = nodes.astype(jnp.float32)
    inverse = lax.rsqrt(jnp.mean(wide_nodes * wide_nodes, axis=1, keepdims=True) + EPS)
    normed = (wide_nodes * inverse * gain).astype(jnp.bfloat16)
    query = jnp.dot(normed, w_query, preferred_element_type=jnp.float32).astype(jnp.bfloat16)
    keys = jnp.dot(normed, w_key, preferred_element_type=jnp.float32).astype(jnp.bfloat16)
    values = jnp.dot(normed, w_value, preferred_element_type=jnp.float32).astype(jnp.bfloat16)
    key_blocks = keys.reshape(blocks_dev, block_len, columns)
    value_blocks = values.reshape(blocks_dev, block_len, columns)
    bit_order = list(range(graph_levels))[::-1]
    joined_blocks = jnp.concatenate([key_blocks, value_blocks], axis=2)
    remote = {}
    for bit in bit_order:
        remote[bit] = from_partner(joined_blocks, "graph", bit)
    joined_slots = (
        [joined_blocks]
        + [flip_blocks(joined_blocks, level) for level in range(local_levels)]
        + [remote[bit] for bit in range(graph_levels)]
    )
    active = jnp.concatenate([jnp.ones((blocks_dev, 1), jnp.int32), links], axis=1)
    grad_attended = jnp.dot(cotangent, w_out.T, preferred_element_type=jnp.float32).astype(
        jnp.bfloat16
    )
    attended, grad_query, term_slots = block_attention(
        active,
        query.reshape(blocks_dev, block_len, columns),
        grad_attended.reshape(blocks_dev, block_len, columns),
        joined_slots,
    )
    attended = attended.reshape(node_rows, columns)
    grad_query = grad_query.reshape(node_rows, columns)
    head_me = lax.axis_index("head")
    mixed_terms = jnp.dot(attended, w_out, preferred_element_type=jnp.float32)
    own_mixed = lax.dynamic_slice_in_dim(mixed_terms, head_me * columns, columns, 1)
    other_mixed = lax.dynamic_slice_in_dim(mixed_terms, (1 - head_me) * columns, columns, 1)
    mixed = (own_mixed + head_swap(other_mixed)).astype(jnp.bfloat16)
    grad_key = term_slots[0][:, :, :columns].astype(jnp.float32)
    grad_value = term_slots[0][:, :, columns:].astype(jnp.float32)
    returned = {}
    for bit in bit_order:
        slot = 1 + local_levels + bit
        got = from_partner(term_slots[slot], "graph", bit)
        returned[bit] = (got[:, :, :columns], got[:, :, columns:])
    for bit in range(graph_levels):
        grad_key = grad_key + returned[bit][0].astype(jnp.float32)
        grad_value = grad_value + returned[bit][1].astype(jnp.float32)
    grad_key = grad_key.astype(jnp.bfloat16).reshape(node_rows, columns)
    grad_value = grad_value.astype(jnp.bfloat16).reshape(node_rows, columns)
    w_out_rows, w_query_grad = scatter_rows(
        [(cotangent, attended), (normed, grad_query)], "graph", graph_levels
    )
    w_out_grad = w_out_rows.T
    w_key_grad, w_value_grad = scatter_rows(
        [(normed, grad_key), (normed, grad_value)], "graph", graph_levels
    )
    feature_terms = (
        jnp.dot(grad_query, w_query.T, preferred_element_type=jnp.float32)
        + jnp.dot(grad_key, w_key.T, preferred_element_type=jnp.float32)
        + jnp.dot(grad_value, w_value.T, preferred_element_type=jnp.float32)
    )
    low_terms = feature_terms.astype(jnp.bfloat16)
    grad_normed = low_terms.astype(jnp.float32) + head_swap(low_terms).astype(jnp.float32)
    gain_terms = jnp.sum(low_terms.astype(jnp.float32) * wide_nodes * inverse, axis=0)
    gain_grad = doubling_sum(gain_terms + head_swap(gain_terms), "graph", graph_levels)
    scaled = grad_normed * gain
    nodes_grad = (
        inverse
        * (
            scaled
            - wide_nodes * inverse * inverse * jnp.mean(scaled * wide_nodes, axis=1, keepdims=True)
        )
    ).astype(jnp.bfloat16)
    return (mixed, nodes_grad, gain_grad, w_query_grad, w_key_grad, w_value_grad, w_out_grad)


def solution(mesh):
    in_specs = (
        P("graph", None),
        P(),
        P(None, "head"),
        P(None, "head"),
        P(None, "head"),
        P("head", None),
        P("graph", None),
        P("graph", None),
    )
    out_specs = (
        P("graph", "head"),
        P("graph", None),
        P(),
        P("graph", "head"),
        P("graph", "head"),
        P("graph", "head"),
        P("head", "graph"),
    )
    return jax.shard_map(shards, mesh=mesh, in_specs=in_specs, out_specs=out_specs, check_vma=False)
```

```python
import jax
import jax.numpy as jnp
from jax import lax
from jax.sharding import PartitionSpec as P
import functools
from jax.experimental import pallas as pl
from jax.experimental.pallas import tpu as pltpu

HEAD_DIM = 64


EPS = 1e-05
NEG = -1e30


def from_partner(value, axis, apart):
    mask = 2**apart
    pairs = [(source, source ^ mask) for source in range(lax.axis_size(axis))]
    return lax.ppermute(value, axis, pairs)


def bit_major_rows(matrix, order):
    rows, width = matrix.shape
    levels = len(order)
    inner = width >> levels
    shaped = matrix.reshape((rows,) + (2,) * levels + (inner,))
    axes = (0,) + tuple(levels - bit for bit in order) + (levels + 1,)
    return shaped.transpose(axes).reshape(rows, width)


def as_pairs(vector):
    high = vector.astype(jnp.bfloat16)
    low = (vector - high.astype(jnp.float32)).astype(jnp.bfloat16)
    return high, low


def from_pairs(high, low):
    return high.astype(jnp.float32) + low.astype(jnp.float32)


def halving_sum(partial, axis, order, extra=None):
    me = lax.axis_index(axis)
    width = partial.shape[1]
    for bit in order:
        half = partial.shape[0] // 2
        mine = (me >> bit) & 1
        keep = lax.dynamic_slice_in_dim(partial, mine * half, half, 0)
        send = lax.dynamic_slice_in_dim(partial, (1 - mine) * half, half, 0)
        send = send.astype(jnp.bfloat16)
        if extra is not None:
            high, low = as_pairs(extra)
            code = jnp.concatenate([high, low]).reshape(-1, width)
            send = jnp.concatenate([send, code], axis=0)
        got = from_partner(send, axis, bit)
        if extra is not None:
            code = got[half:].reshape(2, -1)
            extra = from_pairs(high, low) + from_pairs(code[0], code[1])
            got = got[:half]
        partial = keep + got.astype(jnp.float32)
    return partial, extra


def split_orders(levels):
    first = tuple(range(levels))
    if levels < 3:
        return first, first
    return first, (0, 2, 1) + first[3:]


def scatter_rows(pairs, axis, levels, extra):
    contract = (((0,), (0,)), ((), ()))
    chunks = []
    for index, order in enumerate(split_orders(levels)):
        pieces = []
        for left, right in pairs:
            cut = right.shape[1] // 2
            piece = right[:, index * cut : (index + 1) * cut]
            pieces.append(
                lax.dot_general(
                    bit_major_rows(left, order), piece, contract,
                    preferred_element_type=jnp.float32,
                )
            )
        chunk, summed = halving_sum(
            jnp.concatenate(pieces, axis=1), axis, order, extra if index == 0 else None
        )
        chunks.append(chunk)
        if index == 0:
            extra = summed
    results = []
    offset = 0
    for left, right in pairs:
        cut = right.shape[1] // 2
        results.append(
            jnp.concatenate([chunk[:, offset : offset + cut] for chunk in chunks], axis=1)
        )
        offset += cut
    return results, extra


def doubling_sum(value, axis, levels):
    for bit in range(levels):
        value = value + from_partner(value, axis, bit)
    return value


def head_swap(value):
    return lax.ppermute(value, "head", [(0, 1), (1, 0)])


def flip_blocks(array, level):
    step = 1 << level
    shaped = array.reshape((array.shape[0] // (2 * step), 2, step) + array.shape[1:])
    return jnp.flip(shaped, axis=1).reshape(array.shape)


def attention_kernel(slots, pairs, active_ref, q_ref, g_ref, *refs):
    key_refs = refs[:slots]
    value_refs = refs[slots : 2 * slots]
    att_ref, gq_ref = refs[2 * slots], refs[2 * slots + 1]
    term_refs = refs[2 * slots + 2 : 3 * slots + 2]
    block = pl.program_id(0)
    scale = HEAD_DIM ** (-0.5)
    width = 2 * HEAD_DIM
    lane = lax.broadcasted_iota(jnp.int32, (q_ref.shape[0], width), 1)
    low_lanes = lane < HEAD_DIM
    flags = [active_ref[block * slots + s] > 0 for s in range(slots)]
    contract_last = (((1,), (1,)), ((), ()))
    contract_first = (((0,), (0,)), ((), ()))
    highest = lax.Precision.HIGHEST
    for pair in range(pairs):
        cols = pl.ds(pair * width, width)
        q2 = q_ref[:, cols]
        g2 = g_ref[:, cols]
        keys = [key_refs[s][:, cols] for s in range(slots)]
        values = [value_refs[s][:, cols] for s in range(slots)]
        outs = []
        for half in range(2):
            sel = low_lanes if half == 0 else jnp.logical_not(low_lanes)
            qm = jnp.where(sel, q2, jnp.zeros_like(q2))
            gm = jnp.where(sel, g2, jnp.zeros_like(g2))
            scores = []
            for s in range(slots):
                raw = lax.dot_general(qm, keys[s], contract_last, preferred_element_type=jnp.float32) * scale
                scores.append(jnp.where(flags[s], raw, NEG))
            top = functools.reduce(jnp.maximum, [jnp.max(x, axis=1, keepdims=True) for x in scores])
            raised = [jnp.exp(x - top) for x in scores]
            total = functools.reduce(jnp.add, [jnp.sum(x, axis=1, keepdims=True) for x in raised])
            probs = [x / total for x in raised]
            probs_low = [x.astype(jnp.bfloat16) for x in probs]
            attended = functools.reduce(jnp.add, [
                jnp.dot(probs_low[s], values[s], preferred_element_type=jnp.float32) for s in range(slots)
            ])
            grad_probs = [
                lax.dot_general(gm, values[s], contract_last, preferred_element_type=jnp.float32)
                for s in range(slots)
            ]
            delta = functools.reduce(jnp.add, [
                jnp.sum(probs[s] * grad_probs[s], axis=1, keepdims=True) for s in range(slots)
            ])
            grad_scores = [probs[s] * (grad_probs[s] - delta) * scale for s in range(slots)]
            grad_query = functools.reduce(jnp.add, [
                jnp.dot(grad_scores[s], keys[s].astype(jnp.float32), precision=highest,
                        preferred_element_type=jnp.float32)
                for s in range(slots)
            ])
            key_terms = [
                lax.dot_general(grad_scores[s], q2.astype(jnp.float32), contract_first,
                                precision=highest, preferred_element_type=jnp.float32)
                for s in range(slots)
            ]
            value_terms = [
                lax.dot_general(probs_low[s], g2, contract_first, preferred_element_type=jnp.float32)
                for s in range(slots)
            ]
            outs.append((attended, grad_query, key_terms, value_terms))
        (att_a, gq_a, kt_a, vt_a), (att_b, gq_b, kt_b, vt_b) = outs
        att_ref[:, cols] = jnp.where(low_lanes, att_a, att_b).astype(att_ref.dtype)
        gq_ref[:, cols] = jnp.where(low_lanes, gq_a, gq_b).astype(gq_ref.dtype)
        for s in range(slots):
            term_refs[s][:, cols] = jnp.where(low_lanes, kt_a[s], kt_b[s]).astype(jnp.bfloat16)
            term_refs[s][:, pl.ds(q_ref.shape[1] + pair * width, width)] = jnp.where(
                low_lanes, vt_a[s], vt_b[s]
            ).astype(jnp.bfloat16)


def block_attention(active, query, grad, joined_slots):
    blocks, rows, columns = query.shape
    slots = len(joined_slots)
    pairs = columns // (2 * HEAD_DIM)
    spec = pl.BlockSpec((None, rows, columns), lambda b, act: (b, 0, 0))
    value_spec = pl.BlockSpec((None, rows, columns), lambda b, act: (b, 0, 1))
    wide_spec = pl.BlockSpec((None, rows, 2 * columns), lambda b, act: (b, 0, 0))
    shape = jax.ShapeDtypeStruct((blocks, rows, columns), jnp.bfloat16)
    wide = jax.ShapeDtypeStruct((blocks, rows, 2 * columns), jnp.bfloat16)
    outs = pl.pallas_call(
        functools.partial(attention_kernel, slots, pairs),
        grid_spec=pltpu.PrefetchScalarGridSpec(
            num_scalar_prefetch=1,
            grid=(blocks,),
            in_specs=[spec] * (2 + slots) + [value_spec] * slots,
            out_specs=[spec] * 2 + [wide_spec] * slots,
        ),
        out_shape=[shape] * 2 + [wide] * slots,
    )(active.reshape(-1), query, grad, *joined_slots, *joined_slots)
    return outs[0], outs[1], outs[2:]


def shards(nodes, gain, w_query, w_key, w_value, w_out, links, cotangent):
    blocks_dev = links.shape[0]
    local_levels = blocks_dev.bit_length() - 1
    graph_levels = lax.axis_size("graph").bit_length() - 1
    node_rows, width = nodes.shape
    block_len = node_rows // blocks_dev
    columns = w_query.shape[1]
    local_heads = columns // HEAD_DIM
    score_scale = HEAD_DIM ** (-0.5)
    contract_rows = (((0,), (0,)), ((), ()))
    wide_nodes = nodes.astype(jnp.float32)
    inverse = lax.rsqrt(jnp.mean(wide_nodes * wide_nodes, axis=1, keepdims=True) + EPS)
    normed = (wide_nodes * inverse * gain).astype(jnp.bfloat16)
    query = jnp.dot(normed, w_query, preferred_element_type=jnp.float32).astype(jnp.bfloat16)
    keys = jnp.dot(normed, w_key, preferred_element_type=jnp.float32).astype(jnp.bfloat16)
    values = jnp.dot(normed, w_value, preferred_element_type=jnp.float32).astype(jnp.bfloat16)
    key_blocks = keys.reshape(blocks_dev, block_len, columns)
    value_blocks = values.reshape(blocks_dev, block_len, columns)
    bit_order = list(range(graph_levels))[::-1]
    joined_blocks = jnp.concatenate([key_blocks, value_blocks], axis=2)
    remote = {}
    for bit in bit_order:
        remote[bit] = from_partner(joined_blocks, "graph", bit)
    joined_slots = (
        [joined_blocks]
        + [flip_blocks(joined_blocks, level) for level in range(local_levels)]
        + [remote[bit] for bit in range(graph_levels)]
    )
    active = jnp.concatenate([jnp.ones((blocks_dev, 1), jnp.int32), links], axis=1)
    grad_attended = jnp.dot(cotangent, w_out.T, preferred_element_type=jnp.float32).astype(
        jnp.bfloat16
    )
    attended, grad_query, term_slots = block_attention(
        active,
        query.reshape(blocks_dev, block_len, columns),
        grad_attended.reshape(blocks_dev, block_len, columns),
        joined_slots,
    )
    attended = attended.reshape(node_rows, columns)
    grad_query = grad_query.reshape(node_rows, columns)
    head_me = lax.axis_index("head")
    mixed_terms = jnp.dot(attended, w_out, preferred_element_type=jnp.float32)
    own_mixed = lax.dynamic_slice_in_dim(mixed_terms, head_me * columns, columns, 1)
    other_mixed = lax.dynamic_slice_in_dim(mixed_terms, (1 - head_me) * columns, columns, 1)
    mixed = (own_mixed + head_swap(other_mixed)).astype(jnp.bfloat16)
    grad_key = term_slots[0][:, :, :columns].astype(jnp.float32)
    grad_value = term_slots[0][:, :, columns:].astype(jnp.float32)
    returned = {}
    for bit in bit_order:
        slot = 1 + local_levels + bit
        got = from_partner(term_slots[slot], "graph", bit)
        returned[bit] = (got[:, :, :columns], got[:, :, columns:])
    for bit in range(graph_levels):
        grad_key = grad_key + returned[bit][0].astype(jnp.float32)
        grad_value = grad_value + returned[bit][1].astype(jnp.float32)
    grad_key = grad_key.astype(jnp.bfloat16).reshape(node_rows, columns)
    grad_value = grad_value.astype(jnp.bfloat16).reshape(node_rows, columns)
    feature_terms = (
        jnp.dot(grad_query, w_query.T, preferred_element_type=jnp.float32)
        + jnp.dot(grad_key, w_key.T, preferred_element_type=jnp.float32)
        + jnp.dot(grad_value, w_value.T, preferred_element_type=jnp.float32)
    )
    low_terms = feature_terms.astype(jnp.bfloat16)
    gain_terms = jnp.sum(low_terms.astype(jnp.float32) * wide_nodes * inverse, axis=0)
    (w_out_rows, w_query_grad, w_key_grad, w_value_grad), gain_part = scatter_rows(
        [(cotangent, attended), (normed, grad_query), (normed, grad_key), (normed, grad_value)],
        "graph", graph_levels, gain_terms,
    )
    w_out_grad = w_out_rows.T
    gain_grad = gain_part + head_swap(gain_part)
    grad_normed = low_terms.astype(jnp.float32) + head_swap(low_terms).astype(jnp.float32)
    scaled = grad_normed * gain
    nodes_grad = (
        inverse
        * (
            scaled
            - wide_nodes * inverse * inverse * jnp.mean(scaled * wide_nodes, axis=1, keepdims=True)
        )
    ).astype(jnp.bfloat16)
    return (mixed, nodes_grad, gain_grad, w_query_grad, w_key_grad, w_value_grad, w_out_grad)


def solution(mesh):
    in_specs = (
        P("graph", None),
        P(),
        P(None, "head"),
        P(None, "head"),
        P(None, "head"),
        P("head", None),
        P("graph", None),
        P("graph", None),
    )
    out_specs = (
        P("graph", "head"),
        P("graph", None),
        P(),
        P("graph", "head"),
        P("graph", "head"),
        P("graph", "head"),
        P("head", "graph"),
    )
    return jax.shard_map(shards, mesh=mesh, in_specs=in_specs, out_specs=out_specs, check_vma=False)
```

```python
import jax
import jax.numpy as jnp
from jax import lax
from jax.sharding import PartitionSpec as P
import functools
from jax.experimental import pallas as pl
from jax.experimental.pallas import tpu as pltpu

HEAD_DIM = 64


EPS = 1e-05
NEG = -1e30


def from_partner(value, axis, apart):
    mask = 2**apart
    pairs = [(source, source ^ mask) for source in range(lax.axis_size(axis))]
    return lax.ppermute(value, axis, pairs)


def bit_major_rows(matrix, order):
    rows, width = matrix.shape
    levels = len(order)
    inner = width >> levels
    shaped = matrix.reshape((rows,) + (2,) * levels + (inner,))
    axes = (0,) + tuple(levels - bit for bit in order) + (levels + 1,)
    return shaped.transpose(axes).reshape(rows, width)


def halving_sum(partial, axis, order):
    me = lax.axis_index(axis)
    for bit in order:
        half = partial.shape[0] // 2
        mine = (me >> bit) & 1
        keep = lax.dynamic_slice_in_dim(partial, mine * half, half, 0)
        send = lax.dynamic_slice_in_dim(partial, (1 - mine) * half, half, 0)
        got = from_partner(send.astype(jnp.bfloat16), axis, bit)
        partial = keep + got.astype(jnp.float32)
    return partial


def split_orders(levels):
    first = tuple(range(levels))
    if levels < 3:
        return first, first
    return first, (0, 2, 1) + first[3:]


def scatter_rows(pairs, axis, levels):
    contract = (((0,), (0,)), ((), ()))
    chunks = []
    for index, order in enumerate(split_orders(levels)):
        pieces = []
        for left, right in pairs:
            cut = right.shape[1] // 2
            piece = right[:, index * cut : (index + 1) * cut]
            pieces.append(
                lax.dot_general(
                    bit_major_rows(left, order), piece, contract,
                    preferred_element_type=jnp.float32,
                )
            )
        chunks.append(halving_sum(jnp.concatenate(pieces, axis=1), axis, order))
    results = []
    offset = 0
    for left, right in pairs:
        cut = right.shape[1] // 2
        results.append(
            jnp.concatenate([chunk[:, offset : offset + cut] for chunk in chunks], axis=1)
        )
        offset += cut
    return results


def doubling_sum(value, axis, levels):
    for bit in range(levels):
        value = value + from_partner(value, axis, bit)
    return value


def head_swap(value):
    return lax.ppermute(value, "head", [(0, 1), (1, 0)])


def flip_blocks(array, level):
    step = 1 << level
    shaped = array.reshape((array.shape[0] // (2 * step), 2, step) + array.shape[1:])
    return jnp.flip(shaped, axis=1).reshape(array.shape)


def attention_kernel(slots, pairs, active_ref, q_ref, g_ref, *refs):
    key_refs = refs[:slots]
    value_refs = refs[slots : 2 * slots]
    att_ref, gq_ref = refs[2 * slots], refs[2 * slots + 1]
    term_refs = refs[2 * slots + 2 : 3 * slots + 2]
    block = pl.program_id(0)
    scale = HEAD_DIM ** (-0.5)
    width = 2 * HEAD_DIM
    lane = lax.broadcasted_iota(jnp.int32, (q_ref.shape[0], width), 1)
    low_lanes = lane < HEAD_DIM
    flags = [active_ref[block * slots + s] > 0 for s in range(slots)]
    contract_last = (((1,), (1,)), ((), ()))
    contract_first = (((0,), (0,)), ((), ()))
    for pair in range(pairs):
        cols = pl.ds(pair * width, width)
        q2 = q_ref[:, cols]
        g2 = g_ref[:, cols]
        keys = [key_refs[s][:, cols] for s in range(slots)]
        values = [value_refs[s][:, cols] for s in range(slots)]
        outs = []
        for half in range(2):
            sel = low_lanes if half == 0 else jnp.logical_not(low_lanes)
            qm = jnp.where(sel, q2, jnp.zeros_like(q2))
            gm = jnp.where(sel, g2, jnp.zeros_like(g2))
            scores = []
            for s in range(slots):
                raw = lax.dot_general(qm, keys[s], contract_last, preferred_element_type=jnp.float32) * scale
                scores.append(jnp.where(flags[s], raw, NEG))
            top = functools.reduce(jnp.maximum, [jnp.max(x, axis=1, keepdims=True) for x in scores])
            raised = [jnp.exp(x - top) for x in scores]
            total = functools.reduce(jnp.add, [jnp.sum(x, axis=1, keepdims=True) for x in raised])
            spread = 1.0 / total
            probs = [x * spread for x in raised]
            probs_low = [x.astype(jnp.bfloat16) for x in probs]
            attended = functools.reduce(jnp.add, [
                jnp.dot(probs_low[s], values[s], preferred_element_type=jnp.float32) for s in range(slots)
            ])
            grad_probs = [
                lax.dot_general(gm, values[s], contract_last, preferred_element_type=jnp.float32)
                for s in range(slots)
            ]
            delta = functools.reduce(jnp.add, [
                jnp.sum(probs[s] * grad_probs[s], axis=1, keepdims=True) for s in range(slots)
            ])
            grad_scores = [
                (probs[s] * (grad_probs[s] - delta) * scale).astype(jnp.bfloat16)
                for s in range(slots)
            ]
            grad_query = functools.reduce(jnp.add, [
                jnp.dot(grad_scores[s], keys[s], preferred_element_type=jnp.float32)
                for s in range(slots)
            ])
            key_terms = [
                lax.dot_general(grad_scores[s], q2, contract_first,
                                preferred_element_type=jnp.float32)
                for s in range(slots)
            ]
            value_terms = [
                lax.dot_general(probs_low[s], g2, contract_first, preferred_element_type=jnp.float32)
                for s in range(slots)
            ]
            outs.append((attended, grad_query, key_terms, value_terms))
        (att_a, gq_a, kt_a, vt_a), (att_b, gq_b, kt_b, vt_b) = outs
        att_ref[:, cols] = jnp.where(low_lanes, att_a, att_b).astype(att_ref.dtype)
        gq_ref[:, cols] = jnp.where(low_lanes, gq_a, gq_b).astype(gq_ref.dtype)
        for s in range(slots):
            term_refs[s][:, cols] = jnp.where(low_lanes, kt_a[s], kt_b[s]).astype(jnp.bfloat16)
            term_refs[s][:, pl.ds(q_ref.shape[1] + pair * width, width)] = jnp.where(
                low_lanes, vt_a[s], vt_b[s]
            ).astype(jnp.bfloat16)


def block_attention(active, query, grad, joined_slots):
    blocks, rows, columns = query.shape
    slots = len(joined_slots)
    pairs = columns // (2 * HEAD_DIM)
    spec = pl.BlockSpec((None, rows, columns), lambda b, act: (b, 0, 0))
    value_spec = pl.BlockSpec((None, rows, columns), lambda b, act: (b, 0, 1))
    wide_spec = pl.BlockSpec((None, rows, 2 * columns), lambda b, act: (b, 0, 0))
    shape = jax.ShapeDtypeStruct((blocks, rows, columns), jnp.bfloat16)
    wide = jax.ShapeDtypeStruct((blocks, rows, 2 * columns), jnp.bfloat16)
    outs = pl.pallas_call(
        functools.partial(attention_kernel, slots, pairs),
        grid_spec=pltpu.PrefetchScalarGridSpec(
            num_scalar_prefetch=1,
            grid=(blocks,),
            in_specs=[spec] * (2 + slots) + [value_spec] * slots,
            out_specs=[spec] * 2 + [wide_spec] * slots,
        ),
        out_shape=[shape] * 2 + [wide] * slots,
    )(active.reshape(-1), query, grad, *joined_slots, *joined_slots)
    return outs[0], outs[1], outs[2:]


def shards(nodes, gain, w_query, w_key, w_value, w_out, links, cotangent):
    blocks_dev = links.shape[0]
    local_levels = blocks_dev.bit_length() - 1
    graph_levels = lax.axis_size("graph").bit_length() - 1
    node_rows, width = nodes.shape
    block_len = node_rows // blocks_dev
    columns = w_query.shape[1]
    local_heads = columns // HEAD_DIM
    score_scale = HEAD_DIM ** (-0.5)
    contract_rows = (((0,), (0,)), ((), ()))
    wide_nodes = nodes.astype(jnp.float32)
    inverse = lax.rsqrt(jnp.mean(wide_nodes * wide_nodes, axis=1, keepdims=True) + EPS)
    normed = (wide_nodes * inverse * gain).astype(jnp.bfloat16)
    query = jnp.dot(normed, w_query, preferred_element_type=jnp.float32).astype(jnp.bfloat16)
    keys = jnp.dot(normed, w_key, preferred_element_type=jnp.float32).astype(jnp.bfloat16)
    values = jnp.dot(normed, w_value, preferred_element_type=jnp.float32).astype(jnp.bfloat16)
    key_blocks = keys.reshape(blocks_dev, block_len, columns)
    value_blocks = values.reshape(blocks_dev, block_len, columns)
    bit_order = list(range(graph_levels))[::-1]
    joined_blocks = jnp.concatenate([key_blocks, value_blocks], axis=2)
    remote = {}
    for bit in bit_order:
        remote[bit] = from_partner(joined_blocks, "graph", bit)
    joined_slots = (
        [joined_blocks]
        + [flip_blocks(joined_blocks, level) for level in range(local_levels)]
        + [remote[bit] for bit in range(graph_levels)]
    )
    active = jnp.concatenate([jnp.ones((blocks_dev, 1), jnp.int32), links], axis=1)
    grad_attended = jnp.dot(cotangent, w_out.T, preferred_element_type=jnp.float32).astype(
        jnp.bfloat16
    )
    attended, grad_query, term_slots = block_attention(
        active,
        query.reshape(blocks_dev, block_len, columns),
        grad_attended.reshape(blocks_dev, block_len, columns),
        joined_slots,
    )
    attended = attended.reshape(node_rows, columns)
    grad_query = grad_query.reshape(node_rows, columns)
    head_me = lax.axis_index("head")
    mixed_terms = jnp.dot(attended, w_out, preferred_element_type=jnp.float32)
    own_mixed = lax.dynamic_slice_in_dim(mixed_terms, head_me * columns, columns, 1)
    other_mixed = lax.dynamic_slice_in_dim(mixed_terms, (1 - head_me) * columns, columns, 1)
    mixed = (own_mixed + head_swap(other_mixed)).astype(jnp.bfloat16)
    grad_key = term_slots[0][:, :, :columns].astype(jnp.float32)
    grad_value = term_slots[0][:, :, columns:].astype(jnp.float32)
    returned = {}
    for bit in bit_order:
        slot = 1 + local_levels + bit
        got = from_partner(term_slots[slot], "graph", bit)
        returned[bit] = (got[:, :, :columns], got[:, :, columns:])
    for bit in range(graph_levels):
        grad_key = grad_key + returned[bit][0].astype(jnp.float32)
        grad_value = grad_value + returned[bit][1].astype(jnp.float32)
    grad_key = grad_key.astype(jnp.bfloat16).reshape(node_rows, columns)
    grad_value = grad_value.astype(jnp.bfloat16).reshape(node_rows, columns)
    w_out_rows, w_query_grad = scatter_rows(
        [(cotangent, attended), (normed, grad_query)], "graph", graph_levels
    )
    w_out_grad = w_out_rows.T
    w_key_grad, w_value_grad = scatter_rows(
        [(normed, grad_key), (normed, grad_value)], "graph", graph_levels
    )
    feature_terms = (
        jnp.dot(grad_query, w_query.T, preferred_element_type=jnp.float32)
        + jnp.dot(grad_key, w_key.T, preferred_element_type=jnp.float32)
        + jnp.dot(grad_value, w_value.T, preferred_element_type=jnp.float32)
    )
    low_terms = feature_terms.astype(jnp.bfloat16)
    grad_normed = low_terms.astype(jnp.float32) + head_swap(low_terms).astype(jnp.float32)
    gain_terms = jnp.sum(low_terms.astype(jnp.float32) * wide_nodes * inverse, axis=0)
    gain_grad = doubling_sum(gain_terms + head_swap(gain_terms), "graph", graph_levels)
    scaled = grad_normed * gain
    nodes_grad = (
        inverse
        * (
            scaled
            - wide_nodes * inverse * inverse * jnp.mean(scaled * wide_nodes, axis=1, keepdims=True)
        )
    ).astype(jnp.bfloat16)
    return (mixed, nodes_grad, gain_grad, w_query_grad, w_key_grad, w_value_grad, w_out_grad)


def solution(mesh):
    in_specs = (
        P("graph", None),
        P(),
        P(None, "head"),
        P(None, "head"),
        P(None, "head"),
        P("head", None),
        P("graph", None),
        P("graph", None),
    )
    out_specs = (
        P("graph", "head"),
        P("graph", None),
        P(),
        P("graph", "head"),
        P("graph", "head"),
        P("graph", "head"),
        P("head", "graph"),
    )
    return jax.shard_map(shards, mesh=mesh, in_specs=in_specs, out_specs=out_specs, check_vma=False)
```

```python
import jax
import jax.numpy as jnp
from jax import lax
from jax.sharding import PartitionSpec as P
import functools
from jax.experimental import pallas as pl
from jax.experimental.pallas import tpu as pltpu

HEAD_DIM = 64


EPS = 1e-05
NEG = -1e30


def from_partner(value, axis, apart):
    mask = 2**apart
    pairs = [(source, source ^ mask) for source in range(lax.axis_size(axis))]
    return lax.ppermute(value, axis, pairs)


def bit_major_rows(matrix, order):
    rows, width = matrix.shape
    levels = len(order)
    inner = width >> levels
    shaped = matrix.reshape((rows,) + (2,) * levels + (inner,))
    axes = (0,) + tuple(levels - bit for bit in order) + (levels + 1,)
    return shaped.transpose(axes).reshape(rows, width)


def halving_sum(partial, axis, order):
    me = lax.axis_index(axis)
    for bit in order:
        half = partial.shape[0] // 2
        mine = (me >> bit) & 1
        keep = lax.dynamic_slice_in_dim(partial, mine * half, half, 0)
        send = lax.dynamic_slice_in_dim(partial, (1 - mine) * half, half, 0)
        got = from_partner(send.astype(jnp.bfloat16), axis, bit)
        partial = keep + got.astype(jnp.float32)
    return partial


def split_orders(levels):
    first = tuple(range(levels))
    if levels < 3:
        return first, first
    return first, (0, 2, 1) + first[3:]


def scatter_rows(pairs, axis, levels):
    contract = (((0,), (0,)), ((), ()))
    chunks = []
    for index, order in enumerate(split_orders(levels)):
        pieces = []
        for left, right in pairs:
            cut = right.shape[1] // 2
            piece = right[:, index * cut : (index + 1) * cut]
            pieces.append(
                lax.dot_general(
                    bit_major_rows(left, order), piece, contract,
                    preferred_element_type=jnp.float32,
                )
            )
        chunks.append(halving_sum(jnp.concatenate(pieces, axis=1), axis, order))
    results = []
    offset = 0
    for left, right in pairs:
        cut = right.shape[1] // 2
        results.append(
            jnp.concatenate([chunk[:, offset : offset + cut] for chunk in chunks], axis=1)
        )
        offset += cut
    return results


def doubling_sum(value, axis, levels):
    for bit in range(levels):
        value = value + from_partner(value, axis, bit)
    return value


def head_swap(value):
    return lax.ppermute(value, "head", [(0, 1), (1, 0)])


def flip_blocks(array, level):
    step = 1 << level
    shaped = array.reshape((array.shape[0] // (2 * step), 2, step) + array.shape[1:])
    return jnp.flip(shaped, axis=1).reshape(array.shape)


def attention_kernel(slots, pairs, active_ref, q_ref, g_ref, *refs):
    key_refs = refs[:slots]
    value_refs = refs[slots : 2 * slots]
    att_ref, gq_ref = refs[2 * slots], refs[2 * slots + 1]
    term_refs = refs[2 * slots + 2 : 3 * slots + 2]
    block = pl.program_id(0)
    scale = HEAD_DIM ** (-0.5)
    width = 2 * HEAD_DIM
    lane = lax.broadcasted_iota(jnp.int32, (q_ref.shape[0], width), 1)
    low_lanes = lane < HEAD_DIM
    flags = [active_ref[block * slots + s] > 0 for s in range(slots)]
    contract_last = (((1,), (1,)), ((), ()))
    contract_first = (((0,), (0,)), ((), ()))
    for pair in range(pairs):
        cols = pl.ds(pair * width, width)
        q2 = q_ref[:, cols]
        g2 = g_ref[:, cols]
        keys = [key_refs[s][:, cols] for s in range(slots)]
        values = [value_refs[s][:, cols] for s in range(slots)]
        outs = []
        for half in range(2):
            sel = low_lanes if half == 0 else jnp.logical_not(low_lanes)
            qm = jnp.where(sel, q2, jnp.zeros_like(q2))
            gm = jnp.where(sel, g2, jnp.zeros_like(g2))
            scores = []
            for s in range(slots):
                raw = lax.dot_general(qm, keys[s], contract_last, preferred_element_type=jnp.float32) * scale
                scores.append(jnp.where(flags[s], raw, NEG))
            top = functools.reduce(jnp.maximum, [jnp.max(x, axis=1, keepdims=True) for x in scores])
            raised = [jnp.exp(x - top) for x in scores]
            total = functools.reduce(jnp.add, [jnp.sum(x, axis=1, keepdims=True) for x in raised])
            spread = 1.0 / total
            probs = [x * spread for x in raised]
            probs_low = [x.astype(jnp.bfloat16) for x in probs]
            attended = functools.reduce(jnp.add, [
                jnp.dot(probs_low[s], values[s], preferred_element_type=jnp.float32) for s in range(slots)
            ])
            grad_probs = [
                lax.dot_general(gm, values[s], contract_last, preferred_element_type=jnp.float32)
                for s in range(slots)
            ]
            delta = functools.reduce(jnp.add, [
                jnp.sum(probs[s] * grad_probs[s], axis=1, keepdims=True) for s in range(slots)
            ])
            grad_scores = [
                (probs[s] * (grad_probs[s] - delta) * scale).astype(jnp.bfloat16)
                for s in range(slots)
            ]
            grad_query = functools.reduce(jnp.add, [
                jnp.dot(grad_scores[s], keys[s], preferred_element_type=jnp.float32)
                for s in range(slots)
            ])
            key_terms = [
                lax.dot_general(grad_scores[s], q2, contract_first,
                                preferred_element_type=jnp.float32)
                for s in range(slots)
            ]
            value_terms = [
                lax.dot_general(probs_low[s], g2, contract_first, preferred_element_type=jnp.float32)
                for s in range(slots)
            ]
            outs.append((attended, grad_query, key_terms, value_terms))
        (att_a, gq_a, kt_a, vt_a), (att_b, gq_b, kt_b, vt_b) = outs
        att_ref[:, cols] = jnp.where(low_lanes, att_a, att_b).astype(att_ref.dtype)
        gq_ref[:, cols] = jnp.where(low_lanes, gq_a, gq_b).astype(gq_ref.dtype)
        for s in range(slots):
            term_refs[s][:, cols] = jnp.where(low_lanes, kt_a[s], kt_b[s]).astype(jnp.bfloat16)
            term_refs[s][:, pl.ds(q_ref.shape[1] + pair * width, width)] = jnp.where(
                low_lanes, vt_a[s], vt_b[s]
            ).astype(jnp.bfloat16)


def block_attention(active, query, grad, joined_slots):
    blocks, rows, columns = query.shape
    slots = len(joined_slots)
    pairs = columns // (2 * HEAD_DIM)
    spec = pl.BlockSpec((None, rows, columns), lambda b, act: (b, 0, 0))
    value_spec = pl.BlockSpec((None, rows, columns), lambda b, act: (b, 0, 1))
    wide_spec = pl.BlockSpec((None, rows, 2 * columns), lambda b, act: (b, 0, 0))
    shape = jax.ShapeDtypeStruct((blocks, rows, columns), jnp.bfloat16)
    wide = jax.ShapeDtypeStruct((blocks, rows, 2 * columns), jnp.bfloat16)
    outs = pl.pallas_call(
        functools.partial(attention_kernel, slots, pairs),
        grid_spec=pltpu.PrefetchScalarGridSpec(
            num_scalar_prefetch=1,
            grid=(blocks,),
            in_specs=[spec] * (2 + slots) + [value_spec] * slots,
            out_specs=[spec] * 2 + [wide_spec] * slots,
        ),
        out_shape=[shape] * 2 + [wide] * slots,
    )(active.reshape(-1), query, grad, *joined_slots, *joined_slots)
    return outs[0], outs[1], outs[2:]


def shards(nodes, gain, w_query, w_key, w_value, w_out, links, cotangent):
    blocks_dev = links.shape[0]
    local_levels = blocks_dev.bit_length() - 1
    graph_levels = lax.axis_size("graph").bit_length() - 1
    node_rows, width = nodes.shape
    block_len = node_rows // blocks_dev
    columns = w_query.shape[1]
    local_heads = columns // HEAD_DIM
    score_scale = HEAD_DIM ** (-0.5)
    contract_rows = (((0,), (0,)), ((), ()))
    wide_nodes = nodes.astype(jnp.float32)
    inverse = lax.rsqrt(jnp.mean(wide_nodes * wide_nodes, axis=1, keepdims=True) + EPS)
    normed = (wide_nodes * inverse * gain).astype(jnp.bfloat16)
    query = jnp.dot(normed, w_query, preferred_element_type=jnp.float32).astype(jnp.bfloat16)
    keys = jnp.dot(normed, w_key, preferred_element_type=jnp.float32).astype(jnp.bfloat16)
    values = jnp.dot(normed, w_value, preferred_element_type=jnp.float32).astype(jnp.bfloat16)
    key_blocks = keys.reshape(blocks_dev, block_len, columns)
    value_blocks = values.reshape(blocks_dev, block_len, columns)
    bit_order = list(range(graph_levels))[::-1]
    joined_blocks = jnp.concatenate([key_blocks, value_blocks], axis=2)
    remote = {}
    for bit in bit_order:
        remote[bit] = from_partner(joined_blocks, "graph", bit)
    joined_slots = (
        [joined_blocks]
        + [flip_blocks(joined_blocks, level) for level in range(local_levels)]
        + [remote[bit] for bit in range(graph_levels)]
    )
    active = jnp.concatenate([jnp.ones((blocks_dev, 1), jnp.int32), links], axis=1)
    grad_attended = jnp.dot(cotangent, w_out.T, preferred_element_type=jnp.float32).astype(
        jnp.bfloat16
    )
    attended, grad_query, term_slots = block_attention(
        active,
        query.reshape(blocks_dev, block_len, columns),
        grad_attended.reshape(blocks_dev, block_len, columns),
        joined_slots,
    )
    attended = attended.reshape(node_rows, columns)
    grad_query = grad_query.reshape(node_rows, columns)
    head_me = lax.axis_index("head")
    mixed_terms = jnp.dot(attended, w_out, preferred_element_type=jnp.float32)
    own_mixed = lax.dynamic_slice_in_dim(mixed_terms, head_me * columns, columns, 1)
    other_mixed = lax.dynamic_slice_in_dim(mixed_terms, (1 - head_me) * columns, columns, 1)
    mixed = (own_mixed + head_swap(other_mixed)).astype(jnp.bfloat16)
    grad_key = term_slots[0][:, :, :columns].astype(jnp.float32)
    grad_value = term_slots[0][:, :, columns:].astype(jnp.float32)
    returned = {}
    for bit in bit_order:
        slot = 1 + local_levels + bit
        got = from_partner(term_slots[slot], "graph", bit)
        returned[bit] = (got[:, :, :columns], got[:, :, columns:])
    for bit in range(graph_levels):
        grad_key = grad_key + returned[bit][0].astype(jnp.float32)
        grad_value = grad_value + returned[bit][1].astype(jnp.float32)
    grad_key = grad_key.astype(jnp.bfloat16).reshape(node_rows, columns)
    grad_value = grad_value.astype(jnp.bfloat16).reshape(node_rows, columns)
    w_out_rows, w_query_grad = scatter_rows(
        [(cotangent, attended), (normed, grad_query)], "graph", graph_levels
    )
    w_out_grad = w_out_rows.T
    w_key_grad, w_value_grad = scatter_rows(
        [(normed, grad_key), (normed, grad_value)], "graph", graph_levels
    )
    feature_terms = (
        jnp.dot(grad_query, w_query.T, preferred_element_type=jnp.float32)
        + jnp.dot(grad_key, w_key.T, preferred_element_type=jnp.float32)
        + jnp.dot(grad_value, w_value.T, preferred_element_type=jnp.float32)
    )
    low_terms = feature_terms.astype(jnp.bfloat16)
    grad_normed = low_terms.astype(jnp.float32) + head_swap(low_terms).astype(jnp.float32)
    gain_terms = jnp.sum(low_terms.astype(jnp.float32) * wide_nodes * inverse, axis=0)
    padded = jnp.zeros((16, width), jnp.float32).at[0].set(gain_terms)
    gain_grad = lax.psum(padded, ("graph", "head"))[0]
    scaled = grad_normed * gain
    nodes_grad = (
        inverse
        * (
            scaled
            - wide_nodes * inverse * inverse * jnp.mean(scaled * wide_nodes, axis=1, keepdims=True)
        )
    ).astype(jnp.bfloat16)
    return (mixed, nodes_grad, gain_grad, w_query_grad, w_key_grad, w_value_grad, w_out_grad)


def solution(mesh):
    in_specs = (
        P("graph", None),
        P(),
        P(None, "head"),
        P(None, "head"),
        P(None, "head"),
        P("head", None),
        P("graph", None),
        P("graph", None),
    )
    out_specs = (
        P("graph", "head"),
        P("graph", None),
        P(),
        P("graph", "head"),
        P("graph", "head"),
        P("graph", "head"),
        P("head", "graph"),
    )
    return jax.shard_map(shards, mesh=mesh, in_specs=in_specs, out_specs=out_specs, check_vma=False)
```

```python
import jax
import jax.numpy as jnp
from jax import lax
from jax.sharding import PartitionSpec as P
import functools
from jax.experimental import pallas as pl
from jax.experimental.pallas import tpu as pltpu

HEAD_DIM = 64


EPS = 1e-05
NEG = -1e30


def from_partner(value, axis, apart):
    mask = 2**apart
    pairs = [(source, source ^ mask) for source in range(lax.axis_size(axis))]
    return lax.ppermute(value, axis, pairs)


def bit_major_rows(matrix, order):
    rows, width = matrix.shape
    levels = len(order)
    inner = width >> levels
    shaped = matrix.reshape((rows,) + (2,) * levels + (inner,))
    axes = (0,) + tuple(levels - bit for bit in order) + (levels + 1,)
    return shaped.transpose(axes).reshape(rows, width)


def halving_sum(partial, axis, order, extra=None):
    me = lax.axis_index(axis)
    for bit in order:
        half = partial.shape[0] // 2
        mine = (me >> bit) & 1
        keep = lax.dynamic_slice_in_dim(partial, mine * half, half, 0)
        send = lax.dynamic_slice_in_dim(partial, (1 - mine) * half, half, 0)
        got = from_partner(send.astype(jnp.bfloat16), axis, bit)
        partial = keep + got.astype(jnp.float32)
        if extra is not None:
            extra = extra + from_partner(extra, axis, bit)
            partial, extra = lax.optimization_barrier((partial, extra))
    return partial, extra


def split_orders(levels):
    first = tuple(range(levels))
    if levels < 3:
        return first, first
    return first, (0, 2, 1) + first[3:]


def scatter_rows(pairs, axis, levels, extra=None):
    contract = (((0,), (0,)), ((), ()))
    chunks = []
    for index, order in enumerate(split_orders(levels)):
        pieces = []
        for left, right in pairs:
            cut = right.shape[1] // 2
            piece = right[:, index * cut : (index + 1) * cut]
            pieces.append(
                lax.dot_general(
                    bit_major_rows(left, order), piece, contract,
                    preferred_element_type=jnp.float32,
                )
            )
        chunk, summed = halving_sum(
            jnp.concatenate(pieces, axis=1), axis, order, extra if index == 0 else None
        )
        chunks.append(chunk)
        if index == 0:
            extra = summed
    results = []
    offset = 0
    for left, right in pairs:
        cut = right.shape[1] // 2
        results.append(
            jnp.concatenate([chunk[:, offset : offset + cut] for chunk in chunks], axis=1)
        )
        offset += cut
    return results, extra


def doubling_sum(value, axis, levels):
    for bit in range(levels):
        value = value + from_partner(value, axis, bit)
    return value


def head_swap(value):
    return lax.ppermute(value, "head", [(0, 1), (1, 0)])


def flip_blocks(array, level):
    step = 1 << level
    shaped = array.reshape((array.shape[0] // (2 * step), 2, step) + array.shape[1:])
    return jnp.flip(shaped, axis=1).reshape(array.shape)


def attention_kernel(slots, pairs, active_ref, q_ref, g_ref, *refs):
    key_refs = refs[:slots]
    value_refs = refs[slots : 2 * slots]
    att_ref, gq_ref = refs[2 * slots], refs[2 * slots + 1]
    term_refs = refs[2 * slots + 2 : 3 * slots + 2]
    block = pl.program_id(0)
    scale = HEAD_DIM ** (-0.5)
    width = 2 * HEAD_DIM
    lane = lax.broadcasted_iota(jnp.int32, (q_ref.shape[0], width), 1)
    low_lanes = lane < HEAD_DIM
    flags = [active_ref[block * slots + s] > 0 for s in range(slots)]
    contract_last = (((1,), (1,)), ((), ()))
    contract_first = (((0,), (0,)), ((), ()))
    for pair in range(pairs):
        cols = pl.ds(pair * width, width)
        q2 = q_ref[:, cols]
        g2 = g_ref[:, cols]
        keys = [key_refs[s][:, cols] for s in range(slots)]
        values = [value_refs[s][:, cols] for s in range(slots)]
        outs = []
        for half in range(2):
            sel = low_lanes if half == 0 else jnp.logical_not(low_lanes)
            qm = jnp.where(sel, q2, jnp.zeros_like(q2))
            gm = jnp.where(sel, g2, jnp.zeros_like(g2))
            scores = []
            for s in range(slots):
                raw = lax.dot_general(qm, keys[s], contract_last, preferred_element_type=jnp.float32) * scale
                scores.append(jnp.where(flags[s], raw, NEG))
            top = functools.reduce(jnp.maximum, [jnp.max(x, axis=1, keepdims=True) for x in scores])
            raised = [jnp.exp(x - top) for x in scores]
            total = functools.reduce(jnp.add, [jnp.sum(x, axis=1, keepdims=True) for x in raised])
            spread = 1.0 / total
            probs = [x * spread for x in raised]
            probs_low = [x.astype(jnp.bfloat16) for x in probs]
            attended = functools.reduce(jnp.add, [
                jnp.dot(probs_low[s], values[s], preferred_element_type=jnp.float32) for s in range(slots)
            ])
            grad_probs = [
                lax.dot_general(gm, values[s], contract_last, preferred_element_type=jnp.float32)
                for s in range(slots)
            ]
            delta = functools.reduce(jnp.add, [
                jnp.sum(probs[s] * grad_probs[s], axis=1, keepdims=True) for s in range(slots)
            ])
            grad_scores = [
                (probs[s] * (grad_probs[s] - delta) * scale).astype(jnp.bfloat16)
                for s in range(slots)
            ]
            grad_query = functools.reduce(jnp.add, [
                jnp.dot(grad_scores[s], keys[s], preferred_element_type=jnp.float32)
                for s in range(slots)
            ])
            key_terms = [
                lax.dot_general(grad_scores[s], q2, contract_first,
                                preferred_element_type=jnp.float32)
                for s in range(slots)
            ]
            value_terms = [
                lax.dot_general(probs_low[s], g2, contract_first, preferred_element_type=jnp.float32)
                for s in range(slots)
            ]
            outs.append((attended, grad_query, key_terms, value_terms))
        (att_a, gq_a, kt_a, vt_a), (att_b, gq_b, kt_b, vt_b) = outs
        att_ref[:, cols] = jnp.where(low_lanes, att_a, att_b).astype(att_ref.dtype)
        gq_ref[:, cols] = jnp.where(low_lanes, gq_a, gq_b).astype(gq_ref.dtype)
        for s in range(slots):
            term_refs[s][:, cols] = jnp.where(low_lanes, kt_a[s], kt_b[s]).astype(jnp.bfloat16)
            term_refs[s][:, pl.ds(q_ref.shape[1] + pair * width, width)] = jnp.where(
                low_lanes, vt_a[s], vt_b[s]
            ).astype(jnp.bfloat16)


def block_attention(active, query, grad, joined_slots):
    blocks, rows, columns = query.shape
    slots = len(joined_slots)
    pairs = columns // (2 * HEAD_DIM)
    spec = pl.BlockSpec((None, rows, columns), lambda b, act: (b, 0, 0))
    value_spec = pl.BlockSpec((None, rows, columns), lambda b, act: (b, 0, 1))
    wide_spec = pl.BlockSpec((None, rows, 2 * columns), lambda b, act: (b, 0, 0))
    shape = jax.ShapeDtypeStruct((blocks, rows, columns), jnp.bfloat16)
    wide = jax.ShapeDtypeStruct((blocks, rows, 2 * columns), jnp.bfloat16)
    outs = pl.pallas_call(
        functools.partial(attention_kernel, slots, pairs),
        grid_spec=pltpu.PrefetchScalarGridSpec(
            num_scalar_prefetch=1,
            grid=(blocks,),
            in_specs=[spec] * (2 + slots) + [value_spec] * slots,
            out_specs=[spec] * 2 + [wide_spec] * slots,
        ),
        out_shape=[shape] * 2 + [wide] * slots,
    )(active.reshape(-1), query, grad, *joined_slots, *joined_slots)
    return outs[0], outs[1], outs[2:]


def shards(nodes, gain, w_query, w_key, w_value, w_out, links, cotangent):
    blocks_dev = links.shape[0]
    local_levels = blocks_dev.bit_length() - 1
    graph_levels = lax.axis_size("graph").bit_length() - 1
    node_rows, width = nodes.shape
    block_len = node_rows // blocks_dev
    columns = w_query.shape[1]
    local_heads = columns // HEAD_DIM
    score_scale = HEAD_DIM ** (-0.5)
    contract_rows = (((0,), (0,)), ((), ()))
    wide_nodes = nodes.astype(jnp.float32)
    inverse = lax.rsqrt(jnp.mean(wide_nodes * wide_nodes, axis=1, keepdims=True) + EPS)
    normed = (wide_nodes * inverse * gain).astype(jnp.bfloat16)
    query = jnp.dot(normed, w_query, preferred_element_type=jnp.float32).astype(jnp.bfloat16)
    keys = jnp.dot(normed, w_key, preferred_element_type=jnp.float32).astype(jnp.bfloat16)
    values = jnp.dot(normed, w_value, preferred_element_type=jnp.float32).astype(jnp.bfloat16)
    key_blocks = keys.reshape(blocks_dev, block_len, columns)
    value_blocks = values.reshape(blocks_dev, block_len, columns)
    bit_order = list(range(graph_levels))[::-1]
    joined_blocks = jnp.concatenate([key_blocks, value_blocks], axis=2)
    remote = {}
    for bit in bit_order:
        remote[bit] = from_partner(joined_blocks, "graph", bit)
    joined_slots = (
        [joined_blocks]
        + [flip_blocks(joined_blocks, level) for level in range(local_levels)]
        + [remote[bit] for bit in range(graph_levels)]
    )
    active = jnp.concatenate([jnp.ones((blocks_dev, 1), jnp.int32), links], axis=1)
    grad_attended = jnp.dot(cotangent, w_out.T, preferred_element_type=jnp.float32).astype(
        jnp.bfloat16
    )
    attended, grad_query, term_slots = block_attention(
        active,
        query.reshape(blocks_dev, block_len, columns),
        grad_attended.reshape(blocks_dev, block_len, columns),
        joined_slots,
    )
    attended = attended.reshape(node_rows, columns)
    grad_query = grad_query.reshape(node_rows, columns)
    head_me = lax.axis_index("head")
    mixed_terms = jnp.dot(attended, w_out, preferred_element_type=jnp.float32)
    own_mixed = lax.dynamic_slice_in_dim(mixed_terms, head_me * columns, columns, 1)
    other_mixed = lax.dynamic_slice_in_dim(mixed_terms, (1 - head_me) * columns, columns, 1)
    mixed = (own_mixed + head_swap(other_mixed)).astype(jnp.bfloat16)
    grad_key = term_slots[0][:, :, :columns].astype(jnp.float32)
    grad_value = term_slots[0][:, :, columns:].astype(jnp.float32)
    returned = {}
    for bit in bit_order:
        slot = 1 + local_levels + bit
        got = from_partner(term_slots[slot], "graph", bit)
        returned[bit] = (got[:, :, :columns], got[:, :, columns:])
    for bit in range(graph_levels):
        grad_key = grad_key + returned[bit][0].astype(jnp.float32)
        grad_value = grad_value + returned[bit][1].astype(jnp.float32)
    grad_key = grad_key.astype(jnp.bfloat16).reshape(node_rows, columns)
    grad_value = grad_value.astype(jnp.bfloat16).reshape(node_rows, columns)
    (w_out_rows, w_query_grad), _ = scatter_rows(
        [(cotangent, attended), (normed, grad_query)], "graph", graph_levels
    )
    w_out_grad = w_out_rows.T
    feature_terms = (
        jnp.dot(grad_query, w_query.T, preferred_element_type=jnp.float32)
        + jnp.dot(grad_key, w_key.T, preferred_element_type=jnp.float32)
        + jnp.dot(grad_value, w_value.T, preferred_element_type=jnp.float32)
    )
    low_terms = feature_terms.astype(jnp.bfloat16)
    gain_terms = jnp.sum(low_terms.astype(jnp.float32) * wide_nodes * inverse, axis=0)
    (w_key_grad, w_value_grad), gain_part = scatter_rows(
        [(normed, grad_key), (normed, grad_value)], "graph", graph_levels, gain_terms
    )
    gain_grad = gain_part + head_swap(gain_part)
    grad_normed = low_terms.astype(jnp.float32) + head_swap(low_terms).astype(jnp.float32)
    scaled = grad_normed * gain
    nodes_grad = (
        inverse
        * (
            scaled
            - wide_nodes * inverse * inverse * jnp.mean(scaled * wide_nodes, axis=1, keepdims=True)
        )
    ).astype(jnp.bfloat16)
    return (mixed, nodes_grad, gain_grad, w_query_grad, w_key_grad, w_value_grad, w_out_grad)


def solution(mesh):
    in_specs = (
        P("graph", None),
        P(),
        P(None, "head"),
        P(None, "head"),
        P(None, "head"),
        P("head", None),
        P("graph", None),
        P("graph", None),
    )
    out_specs = (
        P("graph", "head"),
        P("graph", None),
        P(),
        P("graph", "head"),
        P("graph", "head"),
        P("graph", "head"),
        P("head", "graph"),
    )
    return jax.shard_map(shards, mesh=mesh, in_specs=in_specs, out_specs=out_specs, check_vma=False)
```

```python
import jax
import jax.numpy as jnp
from jax import lax
from jax.sharding import PartitionSpec as P
import functools
from jax.experimental import pallas as pl
from jax.experimental.pallas import tpu as pltpu

HEAD_DIM = 64


EPS = 1e-05
NEG = -1e30


def from_partner(value, axis, apart):
    mask = 2**apart
    pairs = [(source, source ^ mask) for source in range(lax.axis_size(axis))]
    return lax.ppermute(value, axis, pairs)


def bit_major_rows(matrix, order):
    rows, width = matrix.shape
    levels = len(order)
    inner = width >> levels
    shaped = matrix.reshape((rows,) + (2,) * levels + (inner,))
    axes = (0,) + tuple(levels - bit for bit in order) + (levels + 1,)
    return shaped.transpose(axes).reshape(rows, width)


def halving_step(partial, axis, bit):
    me = lax.axis_index(axis)
    half = partial.shape[0] // 2
    mine = (me >> bit) & 1
    keep = lax.dynamic_slice_in_dim(partial, mine * half, half, 0)
    send = lax.dynamic_slice_in_dim(partial, (1 - mine) * half, half, 0)
    got = from_partner(send.astype(jnp.bfloat16), axis, bit)
    return keep + got.astype(jnp.float32)


def split_orders(levels):
    first = tuple(range(levels))
    if levels < 3:
        return first, first
    return first, (0, 2, 1) + first[3:]


def scatter_rows(pairs, axis, levels, extra=None):
    contract = (((0,), (0,)), ((), ()))
    orders = split_orders(levels)
    chunks = []
    for index, order in enumerate(orders):
        for left, right in pairs:
            cut = right.shape[1] // 2
            piece = right[:, index * cut : (index + 1) * cut]
            chunks.append(
                lax.dot_general(
                    bit_major_rows(left, order), piece, contract,
                    preferred_element_type=jnp.float32,
                )
            )
    first = sum(right.shape[1] // 2 for left, right in pairs)
    joined = jnp.concatenate(chunks, axis=1)
    parts = None
    for step in range(levels):
        bit_a, bit_b = orders[0][step], orders[1][step]
        if bit_a == bit_b:
            if parts is not None:
                joined = jnp.concatenate(parts, axis=1)
                parts = None
            (joined,), extra = halving_many([joined], [bit_a], axis, extra)
        else:
            if parts is None:
                parts = [joined[:, :first], joined[:, first:]]
            parts, extra = halving_many(parts, [bit_a, bit_b], axis, extra)
    if parts is not None:
        joined = jnp.concatenate(parts, axis=1)
    results = []
    offset = 0
    for left, right in pairs:
        cut = right.shape[1] // 2
        results.append(
            jnp.concatenate(
                [joined[:, offset : offset + cut], joined[:, first + offset : first + offset + cut]],
                axis=1,
            )
        )
        offset += cut
    return results, extra


def halving_many(parts, bits, axis, extra):
    parts = [halving_step(part, axis, bit) for part, bit in zip(parts, bits)]
    if extra is not None:
        extra = extra + from_partner(extra, axis, bits[0])
        parts, extra = lax.optimization_barrier((parts, extra))
    return parts, extra


def doubling_sum(value, axis, levels):
    for bit in range(levels):
        value = value + from_partner(value, axis, bit)
    return value


def head_swap(value):
    return lax.ppermute(value, "head", [(0, 1), (1, 0)])


def flip_blocks(array, level):
    step = 1 << level
    shaped = array.reshape((array.shape[0] // (2 * step), 2, step) + array.shape[1:])
    return jnp.flip(shaped, axis=1).reshape(array.shape)


def attention_kernel(slots, pairs, active_ref, q_ref, g_ref, *refs):
    key_refs = refs[:slots]
    value_refs = refs[slots : 2 * slots]
    att_ref, gq_ref = refs[2 * slots], refs[2 * slots + 1]
    term_refs = refs[2 * slots + 2 : 3 * slots + 2]
    block = pl.program_id(0)
    scale = HEAD_DIM ** (-0.5)
    width = 2 * HEAD_DIM
    lane = lax.broadcasted_iota(jnp.int32, (q_ref.shape[0], width), 1)
    low_lanes = lane < HEAD_DIM
    flags = [active_ref[block * slots + s] > 0 for s in range(slots)]
    contract_last = (((1,), (1,)), ((), ()))
    contract_first = (((0,), (0,)), ((), ()))
    for pair in range(pairs):
        cols = pl.ds(pair * width, width)
        q2 = q_ref[:, cols]
        g2 = g_ref[:, cols]
        keys = [key_refs[s][:, cols] for s in range(slots)]
        values = [value_refs[s][:, cols] for s in range(slots)]
        outs = []
        for half in range(2):
            sel = low_lanes if half == 0 else jnp.logical_not(low_lanes)
            qm = jnp.where(sel, q2, jnp.zeros_like(q2))
            gm = jnp.where(sel, g2, jnp.zeros_like(g2))
            scores = []
            for s in range(slots):
                raw = lax.dot_general(qm, keys[s], contract_last, preferred_element_type=jnp.float32) * scale
                scores.append(jnp.where(flags[s], raw, NEG))
            top = functools.reduce(jnp.maximum, [jnp.max(x, axis=1, keepdims=True) for x in scores])
            raised = [jnp.exp(x - top) for x in scores]
            total = functools.reduce(jnp.add, [jnp.sum(x, axis=1, keepdims=True) for x in raised])
            spread = 1.0 / total
            probs = [x * spread for x in raised]
            probs_low = [x.astype(jnp.bfloat16) for x in probs]
            attended = functools.reduce(jnp.add, [
                jnp.dot(probs_low[s], values[s], preferred_element_type=jnp.float32) for s in range(slots)
            ])
            grad_probs = [
                lax.dot_general(gm, values[s], contract_last, preferred_element_type=jnp.float32)
                for s in range(slots)
            ]
            delta = functools.reduce(jnp.add, [
                jnp.sum(probs[s] * grad_probs[s], axis=1, keepdims=True) for s in range(slots)
            ])
            grad_scores = [
                (probs[s] * (grad_probs[s] - delta) * scale).astype(jnp.bfloat16)
                for s in range(slots)
            ]
            grad_query = functools.reduce(jnp.add, [
                jnp.dot(grad_scores[s], keys[s], preferred_element_type=jnp.float32)
                for s in range(slots)
            ])
            key_terms = [
                lax.dot_general(grad_scores[s], q2, contract_first,
                                preferred_element_type=jnp.float32)
                for s in range(slots)
            ]
            value_terms = [
                lax.dot_general(probs_low[s], g2, contract_first, preferred_element_type=jnp.float32)
                for s in range(slots)
            ]
            outs.append((attended, grad_query, key_terms, value_terms))
        (att_a, gq_a, kt_a, vt_a), (att_b, gq_b, kt_b, vt_b) = outs
        att_ref[:, cols] = jnp.where(low_lanes, att_a, att_b).astype(att_ref.dtype)
        gq_ref[:, cols] = jnp.where(low_lanes, gq_a, gq_b).astype(gq_ref.dtype)
        for s in range(slots):
            term_refs[s][:, cols] = jnp.where(low_lanes, kt_a[s], kt_b[s]).astype(jnp.bfloat16)
            term_refs[s][:, pl.ds(q_ref.shape[1] + pair * width, width)] = jnp.where(
                low_lanes, vt_a[s], vt_b[s]
            ).astype(jnp.bfloat16)


def block_attention(active, query, grad, joined_slots):
    blocks, rows, columns = query.shape
    slots = len(joined_slots)
    pairs = columns // (2 * HEAD_DIM)
    spec = pl.BlockSpec((None, rows, columns), lambda b, act: (b, 0, 0))
    value_spec = pl.BlockSpec((None, rows, columns), lambda b, act: (b, 0, 1))
    wide_spec = pl.BlockSpec((None, rows, 2 * columns), lambda b, act: (b, 0, 0))
    shape = jax.ShapeDtypeStruct((blocks, rows, columns), jnp.bfloat16)
    wide = jax.ShapeDtypeStruct((blocks, rows, 2 * columns), jnp.bfloat16)
    outs = pl.pallas_call(
        functools.partial(attention_kernel, slots, pairs),
        grid_spec=pltpu.PrefetchScalarGridSpec(
            num_scalar_prefetch=1,
            grid=(blocks,),
            in_specs=[spec] * (2 + slots) + [value_spec] * slots,
            out_specs=[spec] * 2 + [wide_spec] * slots,
        ),
        out_shape=[shape] * 2 + [wide] * slots,
    )(active.reshape(-1), query, grad, *joined_slots, *joined_slots)
    return outs[0], outs[1], outs[2:]


def shards(nodes, gain, w_query, w_key, w_value, w_out, links, cotangent):
    blocks_dev = links.shape[0]
    local_levels = blocks_dev.bit_length() - 1
    graph_levels = lax.axis_size("graph").bit_length() - 1
    node_rows, width = nodes.shape
    block_len = node_rows // blocks_dev
    columns = w_query.shape[1]
    local_heads = columns // HEAD_DIM
    score_scale = HEAD_DIM ** (-0.5)
    contract_rows = (((0,), (0,)), ((), ()))
    wide_nodes = nodes.astype(jnp.float32)
    inverse = lax.rsqrt(jnp.mean(wide_nodes * wide_nodes, axis=1, keepdims=True) + EPS)
    normed = (wide_nodes * inverse * gain).astype(jnp.bfloat16)
    query = jnp.dot(normed, w_query, preferred_element_type=jnp.float32).astype(jnp.bfloat16)
    keys = jnp.dot(normed, w_key, preferred_element_type=jnp.float32).astype(jnp.bfloat16)
    values = jnp.dot(normed, w_value, preferred_element_type=jnp.float32).astype(jnp.bfloat16)
    key_blocks = keys.reshape(blocks_dev, block_len, columns)
    value_blocks = values.reshape(blocks_dev, block_len, columns)
    bit_order = list(range(graph_levels))[::-1]
    joined_blocks = jnp.concatenate([key_blocks, value_blocks], axis=2)
    remote = {}
    for bit in bit_order:
        remote[bit] = from_partner(joined_blocks, "graph", bit)
    joined_slots = (
        [joined_blocks]
        + [flip_blocks(joined_blocks, level) for level in range(local_levels)]
        + [remote[bit] for bit in range(graph_levels)]
    )
    active = jnp.concatenate([jnp.ones((blocks_dev, 1), jnp.int32), links], axis=1)
    grad_attended = jnp.dot(cotangent, w_out.T, preferred_element_type=jnp.float32).astype(
        jnp.bfloat16
    )
    attended, grad_query, term_slots = block_attention(
        active,
        query.reshape(blocks_dev, block_len, columns),
        grad_attended.reshape(blocks_dev, block_len, columns),
        joined_slots,
    )
    attended = attended.reshape(node_rows, columns)
    grad_query = grad_query.reshape(node_rows, columns)
    head_me = lax.axis_index("head")
    mixed_terms = jnp.dot(attended, w_out, preferred_element_type=jnp.float32)
    own_mixed = lax.dynamic_slice_in_dim(mixed_terms, head_me * columns, columns, 1)
    other_mixed = lax.dynamic_slice_in_dim(mixed_terms, (1 - head_me) * columns, columns, 1)
    mixed = (own_mixed + head_swap(other_mixed)).astype(jnp.bfloat16)
    grad_key = term_slots[0][:, :, :columns].astype(jnp.float32)
    grad_value = term_slots[0][:, :, columns:].astype(jnp.float32)
    returned = {}
    for bit in bit_order:
        slot = 1 + local_levels + bit
        got = from_partner(term_slots[slot], "graph", bit)
        returned[bit] = (got[:, :, :columns], got[:, :, columns:])
    for bit in range(graph_levels):
        grad_key = grad_key + returned[bit][0].astype(jnp.float32)
        grad_value = grad_value + returned[bit][1].astype(jnp.float32)
    grad_key = grad_key.astype(jnp.bfloat16).reshape(node_rows, columns)
    grad_value = grad_value.astype(jnp.bfloat16).reshape(node_rows, columns)
    (w_out_rows, w_query_grad), _ = scatter_rows(
        [(cotangent, attended), (normed, grad_query)], "graph", graph_levels
    )
    w_out_grad = w_out_rows.T
    feature_terms = (
        jnp.dot(grad_query, w_query.T, preferred_element_type=jnp.float32)
        + jnp.dot(grad_key, w_key.T, preferred_element_type=jnp.float32)
        + jnp.dot(grad_value, w_value.T, preferred_element_type=jnp.float32)
    )
    low_terms = feature_terms.astype(jnp.bfloat16)
    gain_terms = jnp.sum(low_terms.astype(jnp.float32) * wide_nodes * inverse, axis=0)
    (w_key_grad, w_value_grad), gain_part = scatter_rows(
        [(normed, grad_key), (normed, grad_value)], "graph", graph_levels, gain_terms
    )
    gain_grad = gain_part + head_swap(gain_part)
    grad_normed = low_terms.astype(jnp.float32) + head_swap(low_terms).astype(jnp.float32)
    scaled = grad_normed * gain
    nodes_grad = (
        inverse
        * (
            scaled
            - wide_nodes * inverse * inverse * jnp.mean(scaled * wide_nodes, axis=1, keepdims=True)
        )
    ).astype(jnp.bfloat16)
    return (mixed, nodes_grad, gain_grad, w_query_grad, w_key_grad, w_value_grad, w_out_grad)


def solution(mesh):
    in_specs = (
        P("graph", None),
        P(),
        P(None, "head"),
        P(None, "head"),
        P(None, "head"),
        P("head", None),
        P("graph", None),
        P("graph", None),
    )
    out_specs = (
        P("graph", "head"),
        P("graph", None),
        P(),
        P("graph", "head"),
        P("graph", "head"),
        P("graph", "head"),
        P("head", "graph"),
    )
    return jax.shard_map(shards, mesh=mesh, in_specs=in_specs, out_specs=out_specs, check_vma=False)
```

```python
import jax
import jax.numpy as jnp
from jax import lax
from jax.sharding import PartitionSpec as P
import functools
from jax.experimental import pallas as pl
from jax.experimental.pallas import tpu as pltpu

HEAD_DIM = 64


EPS = 1e-05
NEG = -1e30


def from_partner(value, axis, apart):
    mask = 2**apart
    pairs = [(source, source ^ mask) for source in range(lax.axis_size(axis))]
    return lax.ppermute(value, axis, pairs)


def bit_major_rows(matrix, order):
    rows, width = matrix.shape
    levels = len(order)
    inner = width >> levels
    shaped = matrix.reshape((rows,) + (2,) * levels + (inner,))
    axes = (0,) + tuple(levels - bit for bit in order) + (levels + 1,)
    return shaped.transpose(axes).reshape(rows, width)


def halving_step(partial, axis, bit):
    me = lax.axis_index(axis)
    half = partial.shape[0] // 2
    mine = (me >> bit) & 1
    keep = lax.dynamic_slice_in_dim(partial, mine * half, half, 0)
    send = lax.dynamic_slice_in_dim(partial, (1 - mine) * half, half, 0)
    got = from_partner(send.astype(jnp.bfloat16), axis, bit)
    return keep + got.astype(jnp.float32)


def split_orders(levels):
    first = tuple(range(levels))
    if levels < 3:
        return first, first
    return first, (0, 2, 1) + first[3:]


def scatter_rows(pairs, axis, levels, extra=None):
    contract = (((0,), (0,)), ((), ()))
    orders = split_orders(levels)
    chunks = []
    for index, order in enumerate(orders):
        for left, right in pairs:
            cut = right.shape[1] // 2
            piece = right[:, index * cut : (index + 1) * cut]
            chunks.append(
                lax.dot_general(
                    bit_major_rows(left, order), piece, contract,
                    preferred_element_type=jnp.float32,
                )
            )
    first = sum(right.shape[1] // 2 for left, right in pairs)
    joined = jnp.concatenate(chunks, axis=1)
    parts = None
    for step in range(levels):
        bit_a, bit_b = orders[0][step], orders[1][step]
        if bit_a == bit_b:
            if parts is not None:
                joined = jnp.concatenate(parts, axis=1)
                parts = None
            (joined,), extra = halving_many([joined], [bit_a], axis, extra)
        else:
            if parts is None:
                parts = [joined[:, :first], joined[:, first:]]
            parts, extra = halving_many(parts, [bit_a, bit_b], axis, extra)
    if parts is not None:
        joined = jnp.concatenate(parts, axis=1)
    results = []
    offset = 0
    for left, right in pairs:
        cut = right.shape[1] // 2
        results.append(
            jnp.concatenate(
                [joined[:, offset : offset + cut], joined[:, first + offset : first + offset + cut]],
                axis=1,
            )
        )
        offset += cut
    return results, extra


def halving_many(parts, bits, axis, extra):
    parts = [halving_step(part, axis, bit) for part, bit in zip(parts, bits)]
    if extra is not None:
        extra = extra + from_partner(extra, axis, bits[0])
        parts, extra = lax.optimization_barrier((parts, extra))
    return parts, extra


def doubling_sum(value, axis, levels):
    for bit in range(levels):
        value = value + from_partner(value, axis, bit)
    return value


def head_swap(value):
    return lax.ppermute(value, "head", [(0, 1), (1, 0)])


def flip_blocks(array, level):
    step = 1 << level
    shaped = array.reshape((array.shape[0] // (2 * step), 2, step) + array.shape[1:])
    return jnp.flip(shaped, axis=1).reshape(array.shape)


def attention_kernel(slots, pairs, active_ref, q_ref, g_ref, *refs):
    key_refs = refs[:slots]
    value_refs = refs[slots : 2 * slots]
    att_ref, gq_ref = refs[2 * slots], refs[2 * slots + 1]
    term_refs = refs[2 * slots + 2 : 3 * slots + 2]
    block = pl.program_id(0)
    scale = HEAD_DIM ** (-0.5)
    width = 2 * HEAD_DIM
    lane = lax.broadcasted_iota(jnp.int32, (q_ref.shape[0], width), 1)
    low_lanes = lane < HEAD_DIM
    flags = [active_ref[block * slots + s] > 0 for s in range(slots)]
    contract_last = (((1,), (1,)), ((), ()))
    contract_first = (((0,), (0,)), ((), ()))
    for pair in range(pairs):
        cols = pl.ds(pair * width, width)
        q2 = q_ref[:, cols]
        g2 = g_ref[:, cols]
        keys = [key_refs[s][:, cols] for s in range(slots)]
        values = [value_refs[s][:, cols] for s in range(slots)]
        outs = []
        for half in range(2):
            sel = low_lanes if half == 0 else jnp.logical_not(low_lanes)
            qm = jnp.where(sel, q2, jnp.zeros_like(q2))
            gm = jnp.where(sel, g2, jnp.zeros_like(g2))
            scores = []
            for s in range(slots):
                raw = lax.dot_general(qm, keys[s], contract_last, preferred_element_type=jnp.float32) * scale
                scores.append(jnp.where(flags[s], raw, NEG))
            top = functools.reduce(jnp.maximum, [jnp.max(x, axis=1, keepdims=True) for x in scores])
            raised = [jnp.exp(x - top) for x in scores]
            total = functools.reduce(jnp.add, [jnp.sum(x, axis=1, keepdims=True) for x in raised])
            spread = 1.0 / total
            probs = [x * spread for x in raised]
            probs_low = [x.astype(jnp.bfloat16) for x in probs]
            attended = functools.reduce(jnp.add, [
                jnp.dot(probs_low[s], values[s], preferred_element_type=jnp.float32) for s in range(slots)
            ])
            grad_probs = [
                lax.dot_general(gm, values[s], contract_last, preferred_element_type=jnp.float32)
                for s in range(slots)
            ]
            delta = functools.reduce(jnp.add, [
                jnp.sum(probs[s] * grad_probs[s], axis=1, keepdims=True) for s in range(slots)
            ])
            grad_scores = [
                (probs[s] * (grad_probs[s] - delta) * scale).astype(jnp.bfloat16)
                for s in range(slots)
            ]
            grad_query = functools.reduce(jnp.add, [
                jnp.dot(grad_scores[s], keys[s], preferred_element_type=jnp.float32)
                for s in range(slots)
            ])
            key_terms = [
                lax.dot_general(grad_scores[s], q2, contract_first,
                                preferred_element_type=jnp.float32)
                for s in range(slots)
            ]
            value_terms = [
                lax.dot_general(probs_low[s], g2, contract_first, preferred_element_type=jnp.float32)
                for s in range(slots)
            ]
            outs.append((attended, grad_query, key_terms, value_terms))
        (att_a, gq_a, kt_a, vt_a), (att_b, gq_b, kt_b, vt_b) = outs
        att_ref[:, cols] = jnp.where(low_lanes, att_a, att_b).astype(att_ref.dtype)
        gq_ref[:, cols] = jnp.where(low_lanes, gq_a, gq_b).astype(gq_ref.dtype)
        for s in range(slots):
            term_refs[s][:, cols] = jnp.where(low_lanes, kt_a[s], kt_b[s]).astype(jnp.bfloat16)
            term_refs[s][:, pl.ds(q_ref.shape[1] + pair * width, width)] = jnp.where(
                low_lanes, vt_a[s], vt_b[s]
            ).astype(jnp.bfloat16)


def block_attention(active, query, grad, joined_slots):
    blocks, rows, columns = query.shape
    slots = len(joined_slots)
    pairs = columns // (2 * HEAD_DIM)
    spec = pl.BlockSpec((None, rows, columns), lambda b, act: (b, 0, 0))
    value_spec = pl.BlockSpec((None, rows, columns), lambda b, act: (b, 0, 1))
    wide_spec = pl.BlockSpec((None, rows, 2 * columns), lambda b, act: (b, 0, 0))
    shape = jax.ShapeDtypeStruct((blocks, rows, columns), jnp.bfloat16)
    wide = jax.ShapeDtypeStruct((blocks, rows, 2 * columns), jnp.bfloat16)
    outs = pl.pallas_call(
        functools.partial(attention_kernel, slots, pairs),
        grid_spec=pltpu.PrefetchScalarGridSpec(
            num_scalar_prefetch=1,
            grid=(blocks,),
            in_specs=[spec] * (2 + slots) + [value_spec] * slots,
            out_specs=[spec] * 2 + [wide_spec] * slots,
        ),
        out_shape=[shape] * 2 + [wide] * slots,
    )(active.reshape(-1), query, grad, *joined_slots, *joined_slots)
    return outs[0], outs[1], outs[2:]


def shards(nodes, gain, w_query, w_key, w_value, w_out, links, cotangent):
    blocks_dev = links.shape[0]
    local_levels = blocks_dev.bit_length() - 1
    graph_levels = lax.axis_size("graph").bit_length() - 1
    node_rows, width = nodes.shape
    block_len = node_rows // blocks_dev
    columns = w_query.shape[1]
    local_heads = columns // HEAD_DIM
    score_scale = HEAD_DIM ** (-0.5)
    contract_rows = (((0,), (0,)), ((), ()))
    wide_nodes = nodes.astype(jnp.float32)
    inverse = lax.rsqrt(jnp.mean(wide_nodes * wide_nodes, axis=1, keepdims=True) + EPS)
    normed = (wide_nodes * inverse * gain).astype(jnp.bfloat16)
    query = jnp.dot(normed, w_query, preferred_element_type=jnp.float32).astype(jnp.bfloat16)
    keys = jnp.dot(normed, w_key, preferred_element_type=jnp.float32).astype(jnp.bfloat16)
    values = jnp.dot(normed, w_value, preferred_element_type=jnp.float32).astype(jnp.bfloat16)
    key_blocks = keys.reshape(blocks_dev, block_len, columns)
    value_blocks = values.reshape(blocks_dev, block_len, columns)
    bit_order = list(range(graph_levels))[::-1]
    joined_blocks = jnp.concatenate([key_blocks, value_blocks], axis=2)
    remote = {}
    for bit in bit_order:
        remote[bit] = from_partner(joined_blocks, "graph", bit)
    joined_slots = (
        [joined_blocks]
        + [flip_blocks(joined_blocks, level) for level in range(local_levels)]
        + [remote[bit] for bit in range(graph_levels)]
    )
    active = jnp.concatenate([jnp.ones((blocks_dev, 1), jnp.int32), links], axis=1)
    grad_attended = jnp.dot(cotangent, w_out.T, preferred_element_type=jnp.float32).astype(
        jnp.bfloat16
    )
    attended, grad_query, term_slots = block_attention(
        active,
        query.reshape(blocks_dev, block_len, columns),
        grad_attended.reshape(blocks_dev, block_len, columns),
        joined_slots,
    )
    attended = attended.reshape(node_rows, columns)
    grad_query = grad_query.reshape(node_rows, columns)
    head_me = lax.axis_index("head")
    mixed_terms = jnp.dot(attended, w_out, preferred_element_type=jnp.float32)
    own_mixed = lax.dynamic_slice_in_dim(mixed_terms, head_me * columns, columns, 1)
    other_mixed = lax.dynamic_slice_in_dim(mixed_terms, (1 - head_me) * columns, columns, 1)
    mixed = (own_mixed + head_swap(other_mixed)).astype(jnp.bfloat16)
    grad_key = term_slots[0][:, :, :columns].astype(jnp.float32)
    grad_value = term_slots[0][:, :, columns:].astype(jnp.float32)
    returned = {}
    for bit in bit_order:
        slot = 1 + local_levels + bit
        got = from_partner(term_slots[slot], "graph", bit)
        returned[bit] = (got[:, :, :columns], got[:, :, columns:])
    for bit in range(graph_levels):
        grad_key = grad_key + returned[bit][0].astype(jnp.float32)
        grad_value = grad_value + returned[bit][1].astype(jnp.float32)
    grad_key = grad_key.astype(jnp.bfloat16).reshape(node_rows, columns)
    grad_value = grad_value.astype(jnp.bfloat16).reshape(node_rows, columns)
    feature_terms = (
        jnp.dot(grad_query, w_query.T, preferred_element_type=jnp.float32)
        + jnp.dot(grad_key, w_key.T, preferred_element_type=jnp.float32)
        + jnp.dot(grad_value, w_value.T, preferred_element_type=jnp.float32)
    )
    low_terms = feature_terms.astype(jnp.bfloat16)
    gain_terms = jnp.sum(low_terms.astype(jnp.float32) * wide_nodes * inverse, axis=0)
    (w_out_rows, w_query_grad, w_key_grad, w_value_grad), gain_part = scatter_rows(
        [(cotangent, attended), (normed, grad_query), (normed, grad_key), (normed, grad_value)],
        "graph", graph_levels, gain_terms,
    )
    w_out_grad = w_out_rows.T
    gain_grad = gain_part + head_swap(gain_part)
    grad_normed = low_terms.astype(jnp.float32) + head_swap(low_terms).astype(jnp.float32)
    scaled = grad_normed * gain
    nodes_grad = (
        inverse
        * (
            scaled
            - wide_nodes * inverse * inverse * jnp.mean(scaled * wide_nodes, axis=1, keepdims=True)
        )
    ).astype(jnp.bfloat16)
    return (mixed, nodes_grad, gain_grad, w_query_grad, w_key_grad, w_value_grad, w_out_grad)


def solution(mesh):
    in_specs = (
        P("graph", None),
        P(),
        P(None, "head"),
        P(None, "head"),
        P(None, "head"),
        P("head", None),
        P("graph", None),
        P("graph", None),
    )
    out_specs = (
        P("graph", "head"),
        P("graph", None),
        P(),
        P("graph", "head"),
        P("graph", "head"),
        P("graph", "head"),
        P("head", "graph"),
    )
    return jax.shard_map(shards, mesh=mesh, in_specs=in_specs, out_specs=out_specs, check_vma=False)
```

```python
import jax
import jax.numpy as jnp
from jax import lax
from jax.sharding import PartitionSpec as P
import functools
from jax.experimental import pallas as pl
from jax.experimental.pallas import tpu as pltpu

HEAD_DIM = 64


EPS = 1e-05
NEG = -1e30


def from_partner(value, axis, apart):
    mask = 2**apart
    pairs = [(source, source ^ mask) for source in range(lax.axis_size(axis))]
    return lax.ppermute(value, axis, pairs)


def bit_major_rows(matrix, order):
    rows, width = matrix.shape
    levels = len(order)
    inner = width >> levels
    shaped = matrix.reshape((rows,) + (2,) * levels + (inner,))
    axes = (0,) + tuple(levels - bit for bit in order) + (levels + 1,)
    return shaped.transpose(axes).reshape(rows, width)


def halving_step(partial, axis, bit):
    me = lax.axis_index(axis)
    half = partial.shape[0] // 2
    mine = (me >> bit) & 1
    keep = lax.dynamic_slice_in_dim(partial, mine * half, half, 0)
    send = lax.dynamic_slice_in_dim(partial, (1 - mine) * half, half, 0)
    got = from_partner(send.astype(jnp.bfloat16), axis, bit)
    return keep + got.astype(jnp.float32)


def split_orders(levels):
    first = tuple(range(levels))
    if levels < 3:
        return first, first
    return first, (0, 2, 1) + first[3:]


def scatter_rows(pairs, axis, levels, extra=None):
    contract = (((0,), (0,)), ((), ()))
    orders = split_orders(levels)
    chunks = []
    for index, order in enumerate(orders):
        for left, right in pairs:
            cut = right.shape[1] // 2
            piece = right[:, index * cut : (index + 1) * cut]
            chunks.append(
                lax.dot_general(
                    bit_major_rows(left, order), piece, contract,
                    preferred_element_type=jnp.float32,
                )
            )
    first = sum(right.shape[1] // 2 for left, right in pairs)
    joined = jnp.concatenate(chunks, axis=1)
    parts = None
    for step in range(levels):
        bit_a, bit_b = orders[0][step], orders[1][step]
        if bit_a == bit_b:
            if parts is not None:
                joined = jnp.concatenate(parts, axis=1)
                parts = None
            (joined,), extra = halving_many([joined], [bit_a], axis, extra, step + 1 < levels)
        else:
            if parts is None:
                parts = [joined[:, :first], joined[:, first:]]
            parts, extra = halving_many(parts, [bit_a, bit_b], axis, extra, step + 1 < levels)
    if parts is not None:
        joined = jnp.concatenate(parts, axis=1)
    results = []
    offset = 0
    for left, right in pairs:
        cut = right.shape[1] // 2
        results.append(
            jnp.concatenate(
                [joined[:, offset : offset + cut], joined[:, first + offset : first + offset + cut]],
                axis=1,
            )
        )
        offset += cut
    return results, extra


def halving_many(parts, bits, axis, extra, tie):
    parts = [halving_step(part, axis, bit) for part, bit in zip(parts, bits)]
    if extra is not None:
        extra = extra + from_partner(extra, axis, bits[0])
        if tie:
            parts, extra = lax.optimization_barrier((parts, extra))
    return parts, extra


def doubling_sum(value, axis, levels):
    for bit in range(levels):
        value = value + from_partner(value, axis, bit)
    return value


def head_swap(value):
    return lax.ppermute(value, "head", [(0, 1), (1, 0)])


def flip_blocks(array, level):
    step = 1 << level
    shaped = array.reshape((array.shape[0] // (2 * step), 2, step) + array.shape[1:])
    return jnp.flip(shaped, axis=1).reshape(array.shape)


def attention_kernel(slots, pairs, active_ref, q_ref, g_ref, *refs):
    key_refs = refs[:slots]
    value_refs = refs[slots : 2 * slots]
    att_ref, gq_ref = refs[2 * slots], refs[2 * slots + 1]
    term_refs = refs[2 * slots + 2 : 3 * slots + 2]
    block = pl.program_id(0)
    scale = HEAD_DIM ** (-0.5)
    width = 2 * HEAD_DIM
    lane = lax.broadcasted_iota(jnp.int32, (q_ref.shape[0], width), 1)
    low_lanes = lane < HEAD_DIM
    flags = [active_ref[block * slots + s] > 0 for s in range(slots)]
    contract_last = (((1,), (1,)), ((), ()))
    contract_first = (((0,), (0,)), ((), ()))
    for pair in range(pairs):
        cols = pl.ds(pair * width, width)
        q2 = q_ref[:, cols]
        g2 = g_ref[:, cols]
        keys = [key_refs[s][:, cols] for s in range(slots)]
        values = [value_refs[s][:, cols] for s in range(slots)]
        outs = []
        for half in range(2):
            sel = low_lanes if half == 0 else jnp.logical_not(low_lanes)
            qm = jnp.where(sel, q2, jnp.zeros_like(q2))
            gm = jnp.where(sel, g2, jnp.zeros_like(g2))
            scores = []
            for s in range(slots):
                raw = lax.dot_general(qm, keys[s], contract_last, preferred_element_type=jnp.float32) * scale
                scores.append(jnp.where(flags[s], raw, NEG))
            top = functools.reduce(jnp.maximum, [jnp.max(x, axis=1, keepdims=True) for x in scores])
            raised = [jnp.exp(x - top) for x in scores]
            total = functools.reduce(jnp.add, [jnp.sum(x, axis=1, keepdims=True) for x in raised])
            spread = 1.0 / total
            probs = [x * spread for x in raised]
            probs_low = [x.astype(jnp.bfloat16) for x in probs]
            attended = functools.reduce(jnp.add, [
                jnp.dot(probs_low[s], values[s], preferred_element_type=jnp.float32) for s in range(slots)
            ])
            grad_probs = [
                lax.dot_general(gm, values[s], contract_last, preferred_element_type=jnp.float32)
                for s in range(slots)
            ]
            delta = functools.reduce(jnp.add, [
                jnp.sum(probs[s] * grad_probs[s], axis=1, keepdims=True) for s in range(slots)
            ])
            grad_scores = [
                (probs[s] * (grad_probs[s] - delta) * scale).astype(jnp.bfloat16)
                for s in range(slots)
            ]
            grad_query = functools.reduce(jnp.add, [
                jnp.dot(grad_scores[s], keys[s], preferred_element_type=jnp.float32)
                for s in range(slots)
            ])
            key_terms = [
                lax.dot_general(grad_scores[s], q2, contract_first,
                                preferred_element_type=jnp.float32)
                for s in range(slots)
            ]
            value_terms = [
                lax.dot_general(probs_low[s], g2, contract_first, preferred_element_type=jnp.float32)
                for s in range(slots)
            ]
            outs.append((attended, grad_query, key_terms, value_terms))
        (att_a, gq_a, kt_a, vt_a), (att_b, gq_b, kt_b, vt_b) = outs
        att_ref[:, cols] = jnp.where(low_lanes, att_a, att_b).astype(att_ref.dtype)
        gq_ref[:, cols] = jnp.where(low_lanes, gq_a, gq_b).astype(gq_ref.dtype)
        for s in range(slots):
            term_refs[s][:, cols] = jnp.where(low_lanes, kt_a[s], kt_b[s]).astype(jnp.bfloat16)
            term_refs[s][:, pl.ds(q_ref.shape[1] + pair * width, width)] = jnp.where(
                low_lanes, vt_a[s], vt_b[s]
            ).astype(jnp.bfloat16)


def block_attention(active, query, grad, joined_slots):
    blocks, rows, columns = query.shape
    slots = len(joined_slots)
    pairs = columns // (2 * HEAD_DIM)
    spec = pl.BlockSpec((None, rows, columns), lambda b, act: (b, 0, 0))
    value_spec = pl.BlockSpec((None, rows, columns), lambda b, act: (b, 0, 1))
    wide_spec = pl.BlockSpec((None, rows, 2 * columns), lambda b, act: (b, 0, 0))
    shape = jax.ShapeDtypeStruct((blocks, rows, columns), jnp.bfloat16)
    wide = jax.ShapeDtypeStruct((blocks, rows, 2 * columns), jnp.bfloat16)
    outs = pl.pallas_call(
        functools.partial(attention_kernel, slots, pairs),
        grid_spec=pltpu.PrefetchScalarGridSpec(
            num_scalar_prefetch=1,
            grid=(blocks,),
            in_specs=[spec] * (2 + slots) + [value_spec] * slots,
            out_specs=[spec] * 2 + [wide_spec] * slots,
        ),
        out_shape=[shape] * 2 + [wide] * slots,
    )(active.reshape(-1), query, grad, *joined_slots, *joined_slots)
    return outs[0], outs[1], outs[2:]


def shards(nodes, gain, w_query, w_key, w_value, w_out, links, cotangent):
    blocks_dev = links.shape[0]
    local_levels = blocks_dev.bit_length() - 1
    graph_levels = lax.axis_size("graph").bit_length() - 1
    node_rows, width = nodes.shape
    block_len = node_rows // blocks_dev
    columns = w_query.shape[1]
    local_heads = columns // HEAD_DIM
    score_scale = HEAD_DIM ** (-0.5)
    contract_rows = (((0,), (0,)), ((), ()))
    wide_nodes = nodes.astype(jnp.float32)
    inverse = lax.rsqrt(jnp.mean(wide_nodes * wide_nodes, axis=1, keepdims=True) + EPS)
    normed = (wide_nodes * inverse * gain).astype(jnp.bfloat16)
    query = jnp.dot(normed, w_query, preferred_element_type=jnp.float32).astype(jnp.bfloat16)
    keys = jnp.dot(normed, w_key, preferred_element_type=jnp.float32).astype(jnp.bfloat16)
    values = jnp.dot(normed, w_value, preferred_element_type=jnp.float32).astype(jnp.bfloat16)
    key_blocks = keys.reshape(blocks_dev, block_len, columns)
    value_blocks = values.reshape(blocks_dev, block_len, columns)
    bit_order = list(range(graph_levels))[::-1]
    joined_blocks = jnp.concatenate([key_blocks, value_blocks], axis=2)
    remote = {}
    for bit in bit_order:
        remote[bit] = from_partner(joined_blocks, "graph", bit)
    joined_slots = (
        [joined_blocks]
        + [flip_blocks(joined_blocks, level) for level in range(local_levels)]
        + [remote[bit] for bit in range(graph_levels)]
    )
    active = jnp.concatenate([jnp.ones((blocks_dev, 1), jnp.int32), links], axis=1)
    grad_attended = jnp.dot(cotangent, w_out.T, preferred_element_type=jnp.float32).astype(
        jnp.bfloat16
    )
    attended, grad_query, term_slots = block_attention(
        active,
        query.reshape(blocks_dev, block_len, columns),
        grad_attended.reshape(blocks_dev, block_len, columns),
        joined_slots,
    )
    attended = attended.reshape(node_rows, columns)
    grad_query = grad_query.reshape(node_rows, columns)
    head_me = lax.axis_index("head")
    mixed_terms = jnp.dot(attended, w_out, preferred_element_type=jnp.float32)
    own_mixed = lax.dynamic_slice_in_dim(mixed_terms, head_me * columns, columns, 1)
    other_mixed = lax.dynamic_slice_in_dim(mixed_terms, (1 - head_me) * columns, columns, 1)
    mixed = (own_mixed + head_swap(other_mixed)).astype(jnp.bfloat16)
    grad_key = term_slots[0][:, :, :columns].astype(jnp.float32)
    grad_value = term_slots[0][:, :, columns:].astype(jnp.float32)
    returned = {}
    for bit in bit_order:
        slot = 1 + local_levels + bit
        got = from_partner(term_slots[slot], "graph", bit)
        returned[bit] = (got[:, :, :columns], got[:, :, columns:])
    for bit in range(graph_levels):
        grad_key = grad_key + returned[bit][0].astype(jnp.float32)
        grad_value = grad_value + returned[bit][1].astype(jnp.float32)
    grad_key = grad_key.astype(jnp.bfloat16).reshape(node_rows, columns)
    grad_value = grad_value.astype(jnp.bfloat16).reshape(node_rows, columns)
    (w_out_rows, w_query_grad), _ = scatter_rows(
        [(cotangent, attended), (normed, grad_query)], "graph", graph_levels
    )
    w_out_grad = w_out_rows.T
    feature_terms = (
        jnp.dot(grad_query, w_query.T, preferred_element_type=jnp.float32)
        + jnp.dot(grad_key, w_key.T, preferred_element_type=jnp.float32)
        + jnp.dot(grad_value, w_value.T, preferred_element_type=jnp.float32)
    )
    low_terms = feature_terms.astype(jnp.bfloat16)
    grad_normed = low_terms.astype(jnp.float32) + head_swap(low_terms).astype(jnp.float32)
    gain_terms = jnp.sum(grad_normed * wide_nodes * inverse, axis=0)
    (w_key_grad, w_value_grad), gain_part = scatter_rows(
        [(normed, grad_key), (normed, grad_value)], "graph", graph_levels, gain_terms
    )
    gain_grad = gain_part
    scaled = grad_normed * gain
    nodes_grad = (
        inverse
        * (
            scaled
            - wide_nodes * inverse * inverse * jnp.mean(scaled * wide_nodes, axis=1, keepdims=True)
        )
    ).astype(jnp.bfloat16)
    return (mixed, nodes_grad, gain_grad, w_query_grad, w_key_grad, w_value_grad, w_out_grad)


def solution(mesh):
    in_specs = (
        P("graph", None),
        P(),
        P(None, "head"),
        P(None, "head"),
        P(None, "head"),
        P("head", None),
        P("graph", None),
        P("graph", None),
    )
    out_specs = (
        P("graph", "head"),
        P("graph", None),
        P(),
        P("graph", "head"),
        P("graph", "head"),
        P("graph", "head"),
        P("head", "graph"),
    )
    return jax.shard_map(shards, mesh=mesh, in_specs=in_specs, out_specs=out_specs, check_vma=False)
```

```python
import jax
import jax.numpy as jnp
from jax import lax
from jax.sharding import PartitionSpec as P
import functools
from jax.experimental import pallas as pl
from jax.experimental.pallas import tpu as pltpu

HEAD_DIM = 64


EPS = 1e-05
NEG = -1e30


def from_partner(value, axis, apart):
    mask = 2**apart
    pairs = [(source, source ^ mask) for source in range(lax.axis_size(axis))]
    return lax.ppermute(value, axis, pairs)


def bit_major_rows(matrix, order):
    rows, width = matrix.shape
    levels = len(order)
    inner = width >> levels
    shaped = matrix.reshape((rows,) + (2,) * levels + (inner,))
    axes = (0,) + tuple(levels - bit for bit in order) + (levels + 1,)
    return shaped.transpose(axes).reshape(rows, width)


def halving_step(partial, axis, bit):
    me = lax.axis_index(axis)
    half = partial.shape[0] // 2
    mine = (me >> bit) & 1
    keep = lax.dynamic_slice_in_dim(partial, mine * half, half, 0)
    send = lax.dynamic_slice_in_dim(partial, (1 - mine) * half, half, 0)
    got = from_partner(send.astype(jnp.bfloat16), axis, bit)
    return keep + got.astype(jnp.float32)


def split_orders(levels):
    first = tuple(range(levels))
    if levels < 3:
        return first, first
    return first, (0, 2, 1) + first[3:]


def scatter_rows(pairs, axis, levels, extra=None):
    contract = (((0,), (0,)), ((), ()))
    orders = split_orders(levels)
    chunks = []
    for index, order in enumerate(orders):
        for left, right in pairs:
            cut = right.shape[1] // 2
            piece = right[:, index * cut : (index + 1) * cut]
            chunks.append(
                lax.dot_general(
                    bit_major_rows(left, order), piece, contract,
                    preferred_element_type=jnp.float32,
                )
            )
    first = sum(right.shape[1] // 2 for left, right in pairs)
    joined = jnp.concatenate(chunks, axis=1)
    parts = None
    for step in range(levels):
        bit_a, bit_b = orders[0][step], orders[1][step]
        if bit_a == bit_b:
            if parts is not None:
                joined = jnp.concatenate(parts, axis=1)
                parts = None
            (joined,), extra = halving_many([joined], [bit_a], axis, extra, step + 1 < levels)
        else:
            if parts is None:
                parts = [joined[:, :first], joined[:, first:]]
            parts, extra = halving_many(parts, [bit_a, bit_b], axis, extra, step + 1 < levels)
    if parts is not None:
        joined = jnp.concatenate(parts, axis=1)
    results = []
    offset = 0
    for left, right in pairs:
        cut = right.shape[1] // 2
        results.append(
            jnp.concatenate(
                [joined[:, offset : offset + cut], joined[:, first + offset : first + offset + cut]],
                axis=1,
            )
        )
        offset += cut
    return results, extra


def halving_many(parts, bits, axis, extra, tie):
    parts = [halving_step(part, axis, bit) for part, bit in zip(parts, bits)]
    if extra is not None:
        extra = extra + from_partner(extra, axis, bits[0])
        if tie:
            parts, extra = lax.optimization_barrier((parts, extra))
    return parts, extra


def doubling_sum(value, axis, levels):
    for bit in range(levels):
        value = value + from_partner(value, axis, bit)
    return value


def head_swap(value):
    return lax.ppermute(value, "head", [(0, 1), (1, 0)])


def flip_blocks(array, level):
    step = 1 << level
    shaped = array.reshape((array.shape[0] // (2 * step), 2, step) + array.shape[1:])
    return jnp.flip(shaped, axis=1).reshape(array.shape)


def attention_kernel(slots, pairs, active_ref, q_ref, g_ref, *refs):
    key_refs = refs[:slots]
    value_refs = refs[slots : 2 * slots]
    att_ref, gq_ref = refs[2 * slots], refs[2 * slots + 1]
    term_refs = refs[2 * slots + 2 : 3 * slots + 2]
    block = pl.program_id(0)
    scale = HEAD_DIM ** (-0.5)
    width = 2 * HEAD_DIM
    lane = lax.broadcasted_iota(jnp.int32, (q_ref.shape[0], width), 1)
    low_lanes = lane < HEAD_DIM
    flags = [active_ref[block * slots + s] > 0 for s in range(slots)]
    contract_last = (((1,), (1,)), ((), ()))
    contract_first = (((0,), (0,)), ((), ()))
    for pair in range(pairs):
        cols = pl.ds(pair * width, width)
        q2 = q_ref[:, cols]
        g2 = g_ref[:, cols]
        keys = [key_refs[s][:, cols] for s in range(slots)]
        values = [value_refs[s][:, cols] for s in range(slots)]
        outs = []
        for half in range(2):
            sel = low_lanes if half == 0 else jnp.logical_not(low_lanes)
            qm = jnp.where(sel, q2, jnp.zeros_like(q2))
            gm = jnp.where(sel, g2, jnp.zeros_like(g2))
            scores = []
            for s in range(slots):
                raw = lax.dot_general(qm, keys[s], contract_last, preferred_element_type=jnp.float32) * scale
                scores.append(jnp.where(flags[s], raw, NEG))
            top = functools.reduce(jnp.maximum, [jnp.max(x, axis=1, keepdims=True) for x in scores])
            raised = [jnp.exp(x - top) for x in scores]
            total = functools.reduce(jnp.add, [jnp.sum(x, axis=1, keepdims=True) for x in raised])
            spread = 1.0 / total
            probs = [x * spread for x in raised]
            probs_low = [x.astype(jnp.bfloat16) for x in probs]
            attended = functools.reduce(jnp.add, [
                jnp.dot(probs_low[s], values[s], preferred_element_type=jnp.float32) for s in range(slots)
            ])
            grad_probs = [
                lax.dot_general(gm, values[s], contract_last, preferred_element_type=jnp.float32)
                for s in range(slots)
            ]
            delta = functools.reduce(jnp.add, [
                jnp.sum(probs[s] * grad_probs[s], axis=1, keepdims=True) for s in range(slots)
            ])
            grad_scores = [
                (probs[s] * (grad_probs[s] - delta) * scale).astype(jnp.bfloat16)
                for s in range(slots)
            ]
            grad_query = functools.reduce(jnp.add, [
                jnp.dot(grad_scores[s], keys[s], preferred_element_type=jnp.float32)
                for s in range(slots)
            ])
            key_terms = [
                lax.dot_general(grad_scores[s], q2, contract_first,
                                preferred_element_type=jnp.float32)
                for s in range(slots)
            ]
            value_terms = [
                lax.dot_general(probs_low[s], g2, contract_first, preferred_element_type=jnp.float32)
                for s in range(slots)
            ]
            outs.append((attended, grad_query, key_terms, value_terms))
        (att_a, gq_a, kt_a, vt_a), (att_b, gq_b, kt_b, vt_b) = outs
        att_ref[:, cols] = jnp.where(low_lanes, att_a, att_b).astype(att_ref.dtype)
        gq_ref[:, cols] = jnp.where(low_lanes, gq_a, gq_b).astype(gq_ref.dtype)
        for s in range(slots):
            term_refs[s][:, cols] = jnp.where(low_lanes, kt_a[s], kt_b[s]).astype(jnp.bfloat16)
            term_refs[s][:, pl.ds(q_ref.shape[1] + pair * width, width)] = jnp.where(
                low_lanes, vt_a[s], vt_b[s]
            ).astype(jnp.bfloat16)


def block_attention(active, query, grad, joined_slots):
    blocks, rows, columns = query.shape
    slots = len(joined_slots)
    pairs = columns // (2 * HEAD_DIM)
    spec = pl.BlockSpec((None, rows, columns), lambda b, act: (b, 0, 0))
    value_spec = pl.BlockSpec((None, rows, columns), lambda b, act: (b, 0, 1))
    wide_spec = pl.BlockSpec((None, rows, 2 * columns), lambda b, act: (b, 0, 0))
    shape = jax.ShapeDtypeStruct((blocks, rows, columns), jnp.bfloat16)
    wide = jax.ShapeDtypeStruct((blocks, rows, 2 * columns), jnp.bfloat16)
    outs = pl.pallas_call(
        functools.partial(attention_kernel, slots, pairs),
        grid_spec=pltpu.PrefetchScalarGridSpec(
            num_scalar_prefetch=1,
            grid=(blocks,),
            in_specs=[spec] * (2 + slots) + [value_spec] * slots,
            out_specs=[spec] * 2 + [wide_spec] * slots,
        ),
        out_shape=[shape] * 2 + [wide] * slots,
    )(active.reshape(-1), query, grad, *joined_slots, *joined_slots)
    return outs[0], outs[1], outs[2:]


def shards(nodes, gain, w_query, w_key, w_value, w_out, links, cotangent):
    blocks_dev = links.shape[0]
    local_levels = blocks_dev.bit_length() - 1
    graph_levels = lax.axis_size("graph").bit_length() - 1
    node_rows, width = nodes.shape
    block_len = node_rows // blocks_dev
    columns = w_query.shape[1]
    local_heads = columns // HEAD_DIM
    score_scale = HEAD_DIM ** (-0.5)
    contract_rows = (((0,), (0,)), ((), ()))
    wide_nodes = nodes.astype(jnp.float32)
    inverse = lax.rsqrt(jnp.mean(wide_nodes * wide_nodes, axis=1, keepdims=True) + EPS)
    normed = (wide_nodes * inverse * gain).astype(jnp.bfloat16)
    query = jnp.dot(normed, w_query, preferred_element_type=jnp.float32).astype(jnp.bfloat16)
    keys = jnp.dot(normed, w_key, preferred_element_type=jnp.float32).astype(jnp.bfloat16)
    values = jnp.dot(normed, w_value, preferred_element_type=jnp.float32).astype(jnp.bfloat16)
    key_blocks = keys.reshape(blocks_dev, block_len, columns)
    value_blocks = values.reshape(blocks_dev, block_len, columns)
    bit_order = list(range(graph_levels))[::-1]
    joined_blocks = jnp.concatenate([key_blocks, value_blocks], axis=2)
    remote = {}
    for bit in bit_order:
        remote[bit] = from_partner(joined_blocks, "graph", bit)
    joined_slots = (
        [joined_blocks]
        + [flip_blocks(joined_blocks, level) for level in range(local_levels)]
        + [remote[bit] for bit in range(graph_levels)]
    )
    active = jnp.concatenate([jnp.ones((blocks_dev, 1), jnp.int32), links], axis=1)
    grad_attended = jnp.dot(cotangent, w_out.T, preferred_element_type=jnp.float32).astype(
        jnp.bfloat16
    )
    attended, grad_query, term_slots = block_attention(
        active,
        query.reshape(blocks_dev, block_len, columns),
        grad_attended.reshape(blocks_dev, block_len, columns),
        joined_slots,
    )
    attended = attended.reshape(node_rows, columns)
    grad_query = grad_query.reshape(node_rows, columns)
    head_me = lax.axis_index("head")
    mixed_terms = jnp.dot(attended, w_out, preferred_element_type=jnp.float32)
    own_mixed = lax.dynamic_slice_in_dim(mixed_terms, head_me * columns, columns, 1)
    other_mixed = lax.dynamic_slice_in_dim(mixed_terms, (1 - head_me) * columns, columns, 1)
    grad_key = term_slots[0][:, :, :columns].astype(jnp.float32)
    grad_value = term_slots[0][:, :, columns:].astype(jnp.float32)
    returned = {}
    for bit in bit_order:
        slot = 1 + local_levels + bit
        got = from_partner(term_slots[slot], "graph", bit)
        returned[bit] = (got[:, :, :columns], got[:, :, columns:])
    for bit in range(graph_levels):
        grad_key = grad_key + returned[bit][0].astype(jnp.float32)
        grad_value = grad_value + returned[bit][1].astype(jnp.float32)
    grad_key = grad_key.astype(jnp.bfloat16).reshape(node_rows, columns)
    grad_value = grad_value.astype(jnp.bfloat16).reshape(node_rows, columns)
    (w_out_rows, w_query_grad), _ = scatter_rows(
        [(cotangent, attended), (normed, grad_query)], "graph", graph_levels
    )
    w_out_grad = w_out_rows.T
    feature_terms = (
        jnp.dot(grad_query, w_query.T, preferred_element_type=jnp.float32)
        + jnp.dot(grad_key, w_key.T, preferred_element_type=jnp.float32)
        + jnp.dot(grad_value, w_value.T, preferred_element_type=jnp.float32)
    )
    low_terms = feature_terms.astype(jnp.bfloat16)
    swapped = head_swap(jnp.concatenate([low_terms, other_mixed.astype(jnp.bfloat16)], axis=1))
    mixed = (own_mixed + swapped[:, width:].astype(jnp.float32)).astype(jnp.bfloat16)
    grad_normed = low_terms.astype(jnp.float32) + swapped[:, :width].astype(jnp.float32)
    gain_terms = jnp.sum(grad_normed * wide_nodes * inverse, axis=0)
    (w_key_grad, w_value_grad), gain_part = scatter_rows(
        [(normed, grad_key), (normed, grad_value)], "graph", graph_levels, gain_terms
    )
    gain_grad = gain_part
    scaled = grad_normed * gain
    nodes_grad = (
        inverse
        * (
            scaled
            - wide_nodes * inverse * inverse * jnp.mean(scaled * wide_nodes, axis=1, keepdims=True)
        )
    ).astype(jnp.bfloat16)
    return (mixed, nodes_grad, gain_grad, w_query_grad, w_key_grad, w_value_grad, w_out_grad)


def solution(mesh):
    in_specs = (
        P("graph", None),
        P(),
        P(None, "head"),
        P(None, "head"),
        P(None, "head"),
        P("head", None),
        P("graph", None),
        P("graph", None),
    )
    out_specs = (
        P("graph", "head"),
        P("graph", None),
        P(),
        P("graph", "head"),
        P("graph", "head"),
        P("graph", "head"),
        P("head", "graph"),
    )
    return jax.shard_map(shards, mesh=mesh, in_specs=in_specs, out_specs=out_specs, check_vma=False)
```

```python
import jax
import jax.numpy as jnp
from jax import lax
from jax.sharding import PartitionSpec as P
import functools
from jax.experimental import pallas as pl
from jax.experimental.pallas import tpu as pltpu

HEAD_DIM = 64


EPS = 1e-05
NEG = -1e30


def from_partner(value, axis, apart):
    mask = 2**apart
    pairs = [(source, source ^ mask) for source in range(lax.axis_size(axis))]
    return lax.ppermute(value, axis, pairs)


def bit_major_rows(matrix, order):
    rows, width = matrix.shape
    levels = len(order)
    inner = width >> levels
    shaped = matrix.reshape((rows,) + (2,) * levels + (inner,))
    axes = (0,) + tuple(levels - bit for bit in order) + (levels + 1,)
    return shaped.transpose(axes).reshape(rows, width)


def halving_step(partial, axis, bit, code=None):
    me = lax.axis_index(axis)
    half = partial.shape[0] // 2
    mine = (me >> bit) & 1
    keep = lax.dynamic_slice_in_dim(partial, mine * half, half, 0)
    send = lax.dynamic_slice_in_dim(partial, (1 - mine) * half, half, 0).astype(jnp.bfloat16)
    if code is not None:
        send = jnp.concatenate([send, code], axis=0)
    got = from_partner(send, axis, bit)
    return keep + got[:half].astype(jnp.float32), got[half:]


def as_pairs(vector):
    high = vector.astype(jnp.bfloat16)
    low = (vector - high.astype(jnp.float32)).astype(jnp.bfloat16)
    return jnp.concatenate([high, low])


def from_pairs(pairs):
    high, low = pairs.reshape(2, -1)
    return high.astype(jnp.float32) + low.astype(jnp.float32)


def split_orders(levels):
    first = tuple(range(levels))
    if levels < 3:
        return first, first
    return first, (0, 2, 1) + first[3:]


def scatter_rows(pairs, axis, levels, extra=None):
    contract = (((0,), (0,)), ((), ()))
    orders = split_orders(levels)
    chunks = []
    for index, order in enumerate(orders):
        for left, right in pairs:
            cut = right.shape[1] // 2
            piece = right[:, index * cut : (index + 1) * cut]
            chunks.append(
                lax.dot_general(
                    bit_major_rows(left, order), piece, contract,
                    preferred_element_type=jnp.float32,
                )
            )
    first = sum(right.shape[1] // 2 for left, right in pairs)
    joined = jnp.concatenate(chunks, axis=1)
    parts = None
    for step in range(levels):
        bit_a, bit_b = orders[0][step], orders[1][step]
        if bit_a == bit_b:
            if parts is not None:
                joined = jnp.concatenate(parts, axis=1)
                parts = None
            (joined,), extra = halving_many([joined], [bit_a], axis, extra, step + 1 < levels)
        else:
            if parts is None:
                parts = [joined[:, :first], joined[:, first:]]
            parts, extra = halving_many(parts, [bit_a, bit_b], axis, extra, step + 1 < levels)
    if parts is not None:
        joined = jnp.concatenate(parts, axis=1)
    results = []
    offset = 0
    for left, right in pairs:
        cut = right.shape[1] // 2
        results.append(
            jnp.concatenate(
                [joined[:, offset : offset + cut], joined[:, first + offset : first + offset + cut]],
                axis=1,
            )
        )
        offset += cut
    return results, extra


def halving_many(parts, bits, axis, extra, tie):
    if extra is None:
        return [halving_step(part, axis, bit)[0] for part, bit in zip(parts, bits)], None
    pairs = as_pairs(extra)
    first, got = halving_step(parts[0], axis, bits[0], pairs.reshape(-1, parts[0].shape[1]))
    extra = from_pairs(pairs) + from_pairs(got.reshape(-1))
    parts = [first] + [halving_step(part, axis, bit)[0] for part, bit in zip(parts[1:], bits[1:])]
    return parts, extra


def doubling_sum(value, axis, levels):
    for bit in range(levels):
        value = value + from_partner(value, axis, bit)
    return value


def head_swap(value):
    return lax.ppermute(value, "head", [(0, 1), (1, 0)])


def flip_blocks(array, level):
    step = 1 << level
    shaped = array.reshape((array.shape[0] // (2 * step), 2, step) + array.shape[1:])
    return jnp.flip(shaped, axis=1).reshape(array.shape)


def attention_kernel(slots, pairs, active_ref, q_ref, g_ref, *refs):
    key_refs = refs[:slots]
    value_refs = refs[slots : 2 * slots]
    att_ref, gq_ref = refs[2 * slots], refs[2 * slots + 1]
    term_refs = refs[2 * slots + 2 : 3 * slots + 2]
    block = pl.program_id(0)
    scale = HEAD_DIM ** (-0.5)
    width = 2 * HEAD_DIM
    lane = lax.broadcasted_iota(jnp.int32, (q_ref.shape[0], width), 1)
    low_lanes = lane < HEAD_DIM
    flags = [active_ref[block * slots + s] > 0 for s in range(slots)]
    contract_last = (((1,), (1,)), ((), ()))
    contract_first = (((0,), (0,)), ((), ()))
    for pair in range(pairs):
        cols = pl.ds(pair * width, width)
        q2 = q_ref[:, cols]
        g2 = g_ref[:, cols]
        keys = [key_refs[s][:, cols] for s in range(slots)]
        values = [value_refs[s][:, cols] for s in range(slots)]
        outs = []
        for half in range(2):
            sel = low_lanes if half == 0 else jnp.logical_not(low_lanes)
            qm = jnp.where(sel, q2, jnp.zeros_like(q2))
            gm = jnp.where(sel, g2, jnp.zeros_like(g2))
            scores = []
            for s in range(slots):
                raw = lax.dot_general(qm, keys[s], contract_last, preferred_element_type=jnp.float32) * scale
                scores.append(jnp.where(flags[s], raw, NEG))
            top = functools.reduce(jnp.maximum, [jnp.max(x, axis=1, keepdims=True) for x in scores])
            raised = [jnp.exp(x - top) for x in scores]
            total = functools.reduce(jnp.add, [jnp.sum(x, axis=1, keepdims=True) for x in raised])
            spread = 1.0 / total
            probs = [x * spread for x in raised]
            probs_low = [x.astype(jnp.bfloat16) for x in probs]
            attended = functools.reduce(jnp.add, [
                jnp.dot(probs_low[s], values[s], preferred_element_type=jnp.float32) for s in range(slots)
            ])
            grad_probs = [
                lax.dot_general(gm, values[s], contract_last, preferred_element_type=jnp.float32)
                for s in range(slots)
            ]
            delta = functools.reduce(jnp.add, [
                jnp.sum(probs[s] * grad_probs[s], axis=1, keepdims=True) for s in range(slots)
            ])
            grad_scores = [
                (probs[s] * (grad_probs[s] - delta) * scale).astype(jnp.bfloat16)
                for s in range(slots)
            ]
            grad_query = functools.reduce(jnp.add, [
                jnp.dot(grad_scores[s], keys[s], preferred_element_type=jnp.float32)
                for s in range(slots)
            ])
            key_terms = [
                lax.dot_general(grad_scores[s], q2, contract_first,
                                preferred_element_type=jnp.float32)
                for s in range(slots)
            ]
            value_terms = [
                lax.dot_general(probs_low[s], g2, contract_first, preferred_element_type=jnp.float32)
                for s in range(slots)
            ]
            outs.append((attended, grad_query, key_terms, value_terms))
        (att_a, gq_a, kt_a, vt_a), (att_b, gq_b, kt_b, vt_b) = outs
        att_ref[:, cols] = jnp.where(low_lanes, att_a, att_b).astype(att_ref.dtype)
        gq_ref[:, cols] = jnp.where(low_lanes, gq_a, gq_b).astype(gq_ref.dtype)
        for s in range(slots):
            term_refs[s][:, cols] = jnp.where(low_lanes, kt_a[s], kt_b[s]).astype(jnp.bfloat16)
            term_refs[s][:, pl.ds(q_ref.shape[1] + pair * width, width)] = jnp.where(
                low_lanes, vt_a[s], vt_b[s]
            ).astype(jnp.bfloat16)


def block_attention(active, query, grad, joined_slots):
    blocks, rows, columns = query.shape
    slots = len(joined_slots)
    pairs = columns // (2 * HEAD_DIM)
    spec = pl.BlockSpec((None, rows, columns), lambda b, act: (b, 0, 0))
    value_spec = pl.BlockSpec((None, rows, columns), lambda b, act: (b, 0, 1))
    wide_spec = pl.BlockSpec((None, rows, 2 * columns), lambda b, act: (b, 0, 0))
    shape = jax.ShapeDtypeStruct((blocks, rows, columns), jnp.bfloat16)
    wide = jax.ShapeDtypeStruct((blocks, rows, 2 * columns), jnp.bfloat16)
    outs = pl.pallas_call(
        functools.partial(attention_kernel, slots, pairs),
        grid_spec=pltpu.PrefetchScalarGridSpec(
            num_scalar_prefetch=1,
            grid=(blocks,),
            in_specs=[spec] * (2 + slots) + [value_spec] * slots,
            out_specs=[spec] * 2 + [wide_spec] * slots,
        ),
        out_shape=[shape] * 2 + [wide] * slots,
    )(active.reshape(-1), query, grad, *joined_slots, *joined_slots)
    return outs[0], outs[1], outs[2:]


def shards(nodes, gain, w_query, w_key, w_value, w_out, links, cotangent):
    blocks_dev = links.shape[0]
    local_levels = blocks_dev.bit_length() - 1
    graph_levels = lax.axis_size("graph").bit_length() - 1
    node_rows, width = nodes.shape
    block_len = node_rows // blocks_dev
    columns = w_query.shape[1]
    local_heads = columns // HEAD_DIM
    score_scale = HEAD_DIM ** (-0.5)
    contract_rows = (((0,), (0,)), ((), ()))
    wide_nodes = nodes.astype(jnp.float32)
    inverse = lax.rsqrt(jnp.mean(wide_nodes * wide_nodes, axis=1, keepdims=True) + EPS)
    normed = (wide_nodes * inverse * gain).astype(jnp.bfloat16)
    query = jnp.dot(normed, w_query, preferred_element_type=jnp.float32).astype(jnp.bfloat16)
    keys = jnp.dot(normed, w_key, preferred_element_type=jnp.float32).astype(jnp.bfloat16)
    values = jnp.dot(normed, w_value, preferred_element_type=jnp.float32).astype(jnp.bfloat16)
    key_blocks = keys.reshape(blocks_dev, block_len, columns)
    value_blocks = values.reshape(blocks_dev, block_len, columns)
    bit_order = list(range(graph_levels))[::-1]
    joined_blocks = jnp.concatenate([key_blocks, value_blocks], axis=2)
    remote = {}
    for bit in bit_order:
        remote[bit] = from_partner(joined_blocks, "graph", bit)
    joined_slots = (
        [joined_blocks]
        + [flip_blocks(joined_blocks, level) for level in range(local_levels)]
        + [remote[bit] for bit in range(graph_levels)]
    )
    active = jnp.concatenate([jnp.ones((blocks_dev, 1), jnp.int32), links], axis=1)
    grad_attended = jnp.dot(cotangent, w_out.T, preferred_element_type=jnp.float32).astype(
        jnp.bfloat16
    )
    attended, grad_query, term_slots = block_attention(
        active,
        query.reshape(blocks_dev, block_len, columns),
        grad_attended.reshape(blocks_dev, block_len, columns),
        joined_slots,
    )
    attended = attended.reshape(node_rows, columns)
    grad_query = grad_query.reshape(node_rows, columns)
    head_me = lax.axis_index("head")
    mixed_terms = jnp.dot(attended, w_out, preferred_element_type=jnp.float32)
    own_mixed = lax.dynamic_slice_in_dim(mixed_terms, head_me * columns, columns, 1)
    other_mixed = lax.dynamic_slice_in_dim(mixed_terms, (1 - head_me) * columns, columns, 1)
    grad_key = term_slots[0][:, :, :columns].astype(jnp.float32)
    grad_value = term_slots[0][:, :, columns:].astype(jnp.float32)
    returned = {}
    for bit in bit_order:
        slot = 1 + local_levels + bit
        got = from_partner(term_slots[slot], "graph", bit)
        returned[bit] = (got[:, :, :columns], got[:, :, columns:])
    for bit in range(graph_levels):
        grad_key = grad_key + returned[bit][0].astype(jnp.float32)
        grad_value = grad_value + returned[bit][1].astype(jnp.float32)
    grad_key = grad_key.astype(jnp.bfloat16).reshape(node_rows, columns)
    grad_value = grad_value.astype(jnp.bfloat16).reshape(node_rows, columns)
    (w_out_rows, w_query_grad), _ = scatter_rows(
        [(cotangent, attended), (normed, grad_query)], "graph", graph_levels
    )
    w_out_grad = w_out_rows.T
    feature_terms = (
        jnp.dot(grad_query, w_query.T, preferred_element_type=jnp.float32)
        + jnp.dot(grad_key, w_key.T, preferred_element_type=jnp.float32)
        + jnp.dot(grad_value, w_value.T, preferred_element_type=jnp.float32)
    )
    low_terms = feature_terms.astype(jnp.bfloat16)
    swapped = head_swap(jnp.concatenate([low_terms, other_mixed.astype(jnp.bfloat16)], axis=1))
    mixed = (own_mixed + swapped[:, width:].astype(jnp.float32)).astype(jnp.bfloat16)
    grad_normed = low_terms.astype(jnp.float32) + swapped[:, :width].astype(jnp.float32)
    gain_terms = jnp.sum(grad_normed * wide_nodes * inverse, axis=0)
    (w_key_grad, w_value_grad), gain_part = scatter_rows(
        [(normed, grad_key), (normed, grad_value)], "graph", graph_levels, gain_terms
    )
    gain_grad = gain_part
    scaled = grad_normed * gain
    nodes_grad = (
        inverse
        * (
            scaled
            - wide_nodes * inverse * inverse * jnp.mean(scaled * wide_nodes, axis=1, keepdims=True)
        )
    ).astype(jnp.bfloat16)
    return (mixed, nodes_grad, gain_grad, w_query_grad, w_key_grad, w_value_grad, w_out_grad)


def solution(mesh):
    in_specs = (
        P("graph", None),
        P(),
        P(None, "head"),
        P(None, "head"),
        P(None, "head"),
        P("head", None),
        P("graph", None),
        P("graph", None),
    )
    out_specs = (
        P("graph", "head"),
        P("graph", None),
        P(),
        P("graph", "head"),
        P("graph", "head"),
        P("graph", "head"),
        P("head", "graph"),
    )
    return jax.shard_map(shards, mesh=mesh, in_specs=in_specs, out_specs=out_specs, check_vma=False)
```

```python
import jax
import jax.numpy as jnp
from jax import lax
from jax.sharding import PartitionSpec as P
from jax.experimental.layout import Layout, with_layout_constraint
import functools
from jax.experimental import pallas as pl
from jax.experimental.pallas import tpu as pltpu

HEAD_DIM = 64


EPS = 1e-05
NEG = -1e30


def from_partner(value, axis, apart):
    mask = 2**apart
    pairs = [(source, source ^ mask) for source in range(lax.axis_size(axis))]
    return lax.ppermute(value, axis, pairs)


def bit_major_rows(matrix, order):
    rows, width = matrix.shape
    levels = len(order)
    inner = width >> levels
    shaped = matrix.reshape((rows,) + (2,) * levels + (inner,))
    axes = (0,) + tuple(levels - bit for bit in order) + (levels + 1,)
    return shaped.transpose(axes).reshape(rows, width)


def halving_step(partial, axis, bit):
    me = lax.axis_index(axis)
    half = partial.shape[0] // 2
    mine = (me >> bit) & 1
    keep = lax.dynamic_slice_in_dim(partial, mine * half, half, 0)
    send = lax.dynamic_slice_in_dim(partial, (1 - mine) * half, half, 0)
    got = from_partner(send.astype(jnp.bfloat16), axis, bit)
    return keep + got.astype(jnp.float32)


def split_orders(levels):
    first = tuple(range(levels))
    if levels < 3:
        return first, first
    return first, (0, 2, 1) + first[3:]


def scatter_rows(pairs, axis, levels, extra=None):
    contract = (((0,), (0,)), ((), ()))
    orders = split_orders(levels)
    chunks = []
    for index, order in enumerate(orders):
        for left, right in pairs:
            cut = right.shape[1] // 2
            piece = right[:, index * cut : (index + 1) * cut]
            chunks.append(
                lax.dot_general(
                    bit_major_rows(left, order), piece, contract,
                    preferred_element_type=jnp.float32,
                )
            )
    first = sum(right.shape[1] // 2 for left, right in pairs)
    joined = with_layout_constraint(jnp.concatenate(chunks, axis=1), Layout((0, 1)))
    parts = None
    for step in range(levels):
        bit_a, bit_b = orders[0][step], orders[1][step]
        if bit_a == bit_b:
            if parts is not None:
                joined = jnp.concatenate(parts, axis=1)
                parts = None
            (joined,), extra = halving_many([joined], [bit_a], axis, extra, step + 1 < levels)
        else:
            if parts is None:
                parts = [joined[:, :first], joined[:, first:]]
            parts, extra = halving_many(parts, [bit_a, bit_b], axis, extra, step + 1 < levels)
    if parts is not None:
        joined = jnp.concatenate(parts, axis=1)
    results = []
    offset = 0
    for left, right in pairs:
        cut = right.shape[1] // 2
        results.append(
            jnp.concatenate(
                [joined[:, offset : offset + cut], joined[:, first + offset : first + offset + cut]],
                axis=1,
            )
        )
        offset += cut
    return results, extra


def halving_many(parts, bits, axis, extra, tie):
    parts = [halving_step(part, axis, bit) for part, bit in zip(parts, bits)]
    if extra is not None:
        extra = extra + from_partner(extra, axis, bits[0])
        if tie:
            parts, extra = lax.optimization_barrier((parts, extra))
    return parts, extra


def doubling_sum(value, axis, levels):
    for bit in range(levels):
        value = value + from_partner(value, axis, bit)
    return value


def head_swap(value):
    return lax.ppermute(value, "head", [(0, 1), (1, 0)])


def flip_blocks(array, level):
    step = 1 << level
    shaped = array.reshape((array.shape[0] // (2 * step), 2, step) + array.shape[1:])
    return jnp.flip(shaped, axis=1).reshape(array.shape)


def attention_kernel(slots, pairs, active_ref, q_ref, g_ref, *refs):
    key_refs = refs[:slots]
    value_refs = refs[slots : 2 * slots]
    att_ref, gq_ref = refs[2 * slots], refs[2 * slots + 1]
    term_refs = refs[2 * slots + 2 : 3 * slots + 2]
    block = pl.program_id(0)
    scale = HEAD_DIM ** (-0.5)
    width = 2 * HEAD_DIM
    lane = lax.broadcasted_iota(jnp.int32, (q_ref.shape[0], width), 1)
    low_lanes = lane < HEAD_DIM
    flags = [active_ref[block * slots + s] > 0 for s in range(slots)]
    contract_last = (((1,), (1,)), ((), ()))
    contract_first = (((0,), (0,)), ((), ()))
    for pair in range(pairs):
        cols = pl.ds(pair * width, width)
        q2 = q_ref[:, cols]
        g2 = g_ref[:, cols]
        keys = [key_refs[s][:, cols] for s in range(slots)]
        values = [value_refs[s][:, cols] for s in range(slots)]
        outs = []
        for half in range(2):
            sel = low_lanes if half == 0 else jnp.logical_not(low_lanes)
            qm = jnp.where(sel, q2, jnp.zeros_like(q2))
            gm = jnp.where(sel, g2, jnp.zeros_like(g2))
            scores = []
            for s in range(slots):
                raw = lax.dot_general(qm, keys[s], contract_last, preferred_element_type=jnp.float32) * scale
                scores.append(jnp.where(flags[s], raw, NEG))
            top = functools.reduce(jnp.maximum, [jnp.max(x, axis=1, keepdims=True) for x in scores])
            raised = [jnp.exp(x - top) for x in scores]
            total = functools.reduce(jnp.add, [jnp.sum(x, axis=1, keepdims=True) for x in raised])
            spread = 1.0 / total
            probs = [x * spread for x in raised]
            probs_low = [x.astype(jnp.bfloat16) for x in probs]
            attended = functools.reduce(jnp.add, [
                jnp.dot(probs_low[s], values[s], preferred_element_type=jnp.float32) for s in range(slots)
            ])
            grad_probs = [
                lax.dot_general(gm, values[s], contract_last, preferred_element_type=jnp.float32)
                for s in range(slots)
            ]
            delta = functools.reduce(jnp.add, [
                jnp.sum(probs[s] * grad_probs[s], axis=1, keepdims=True) for s in range(slots)
            ])
            grad_scores = [
                (probs[s] * (grad_probs[s] - delta) * scale).astype(jnp.bfloat16)
                for s in range(slots)
            ]
            grad_query = functools.reduce(jnp.add, [
                jnp.dot(grad_scores[s], keys[s], preferred_element_type=jnp.float32)
                for s in range(slots)
            ])
            key_terms = [
                lax.dot_general(grad_scores[s], q2, contract_first,
                                preferred_element_type=jnp.float32)
                for s in range(slots)
            ]
            value_terms = [
                lax.dot_general(probs_low[s], g2, contract_first, preferred_element_type=jnp.float32)
                for s in range(slots)
            ]
            outs.append((attended, grad_query, key_terms, value_terms))
        (att_a, gq_a, kt_a, vt_a), (att_b, gq_b, kt_b, vt_b) = outs
        att_ref[:, cols] = jnp.where(low_lanes, att_a, att_b).astype(att_ref.dtype)
        gq_ref[:, cols] = jnp.where(low_lanes, gq_a, gq_b).astype(gq_ref.dtype)
        for s in range(slots):
            term_refs[s][:, cols] = jnp.where(low_lanes, kt_a[s], kt_b[s]).astype(jnp.bfloat16)
            term_refs[s][:, pl.ds(q_ref.shape[1] + pair * width, width)] = jnp.where(
                low_lanes, vt_a[s], vt_b[s]
            ).astype(jnp.bfloat16)


def block_attention(active, query, grad, joined_slots):
    blocks, rows, columns = query.shape
    slots = len(joined_slots)
    pairs = columns // (2 * HEAD_DIM)
    spec = pl.BlockSpec((None, rows, columns), lambda b, act: (b, 0, 0))
    value_spec = pl.BlockSpec((None, rows, columns), lambda b, act: (b, 0, 1))
    wide_spec = pl.BlockSpec((None, rows, 2 * columns), lambda b, act: (b, 0, 0))
    shape = jax.ShapeDtypeStruct((blocks, rows, columns), jnp.bfloat16)
    wide = jax.ShapeDtypeStruct((blocks, rows, 2 * columns), jnp.bfloat16)
    outs = pl.pallas_call(
        functools.partial(attention_kernel, slots, pairs),
        grid_spec=pltpu.PrefetchScalarGridSpec(
            num_scalar_prefetch=1,
            grid=(blocks,),
            in_specs=[spec] * (2 + slots) + [value_spec] * slots,
            out_specs=[spec] * 2 + [wide_spec] * slots,
        ),
        out_shape=[shape] * 2 + [wide] * slots,
    )(active.reshape(-1), query, grad, *joined_slots, *joined_slots)
    return outs[0], outs[1], outs[2:]


def shards(nodes, gain, w_query, w_key, w_value, w_out, links, cotangent):
    blocks_dev = links.shape[0]
    local_levels = blocks_dev.bit_length() - 1
    graph_levels = lax.axis_size("graph").bit_length() - 1
    node_rows, width = nodes.shape
    block_len = node_rows // blocks_dev
    columns = w_query.shape[1]
    local_heads = columns // HEAD_DIM
    score_scale = HEAD_DIM ** (-0.5)
    contract_rows = (((0,), (0,)), ((), ()))
    wide_nodes = nodes.astype(jnp.float32)
    inverse = lax.rsqrt(jnp.mean(wide_nodes * wide_nodes, axis=1, keepdims=True) + EPS)
    normed = (wide_nodes * inverse * gain).astype(jnp.bfloat16)
    query = jnp.dot(normed, w_query, preferred_element_type=jnp.float32).astype(jnp.bfloat16)
    keys = jnp.dot(normed, w_key, preferred_element_type=jnp.float32).astype(jnp.bfloat16)
    values = jnp.dot(normed, w_value, preferred_element_type=jnp.float32).astype(jnp.bfloat16)
    key_blocks = keys.reshape(blocks_dev, block_len, columns)
    value_blocks = values.reshape(blocks_dev, block_len, columns)
    bit_order = list(range(graph_levels))[::-1]
    joined_blocks = jnp.concatenate([key_blocks, value_blocks], axis=2)
    remote = {}
    for bit in bit_order:
        remote[bit] = from_partner(joined_blocks, "graph", bit)
    joined_slots = (
        [joined_blocks]
        + [flip_blocks(joined_blocks, level) for level in range(local_levels)]
        + [remote[bit] for bit in range(graph_levels)]
    )
    active = jnp.concatenate([jnp.ones((blocks_dev, 1), jnp.int32), links], axis=1)
    grad_attended = jnp.dot(cotangent, w_out.T, preferred_element_type=jnp.float32).astype(
        jnp.bfloat16
    )
    attended, grad_query, term_slots = block_attention(
        active,
        query.reshape(blocks_dev, block_len, columns),
        grad_attended.reshape(blocks_dev, block_len, columns),
        joined_slots,
    )
    attended = attended.reshape(node_rows, columns)
    grad_query = grad_query.reshape(node_rows, columns)
    head_me = lax.axis_index("head")
    mixed_terms = jnp.dot(attended, w_out, preferred_element_type=jnp.float32)
    own_mixed = lax.dynamic_slice_in_dim(mixed_terms, head_me * columns, columns, 1)
    other_mixed = lax.dynamic_slice_in_dim(mixed_terms, (1 - head_me) * columns, columns, 1)
    grad_key = term_slots[0][:, :, :columns].astype(jnp.float32)
    grad_value = term_slots[0][:, :, columns:].astype(jnp.float32)
    returned = {}
    for bit in bit_order:
        slot = 1 + local_levels + bit
        got = from_partner(term_slots[slot], "graph", bit)
        returned[bit] = (got[:, :, :columns], got[:, :, columns:])
    for bit in range(graph_levels):
        grad_key = grad_key + returned[bit][0].astype(jnp.float32)
        grad_value = grad_value + returned[bit][1].astype(jnp.float32)
    grad_key = grad_key.astype(jnp.bfloat16).reshape(node_rows, columns)
    grad_value = grad_value.astype(jnp.bfloat16).reshape(node_rows, columns)
    (w_out_rows, w_query_grad), _ = scatter_rows(
        [(cotangent, attended), (normed, grad_query)], "graph", graph_levels
    )
    w_out_grad = w_out_rows.T
    feature_terms = (
        jnp.dot(grad_query, w_query.T, preferred_element_type=jnp.float32)
        + jnp.dot(grad_key, w_key.T, preferred_element_type=jnp.float32)
        + jnp.dot(grad_value, w_value.T, preferred_element_type=jnp.float32)
    )
    low_terms = feature_terms.astype(jnp.bfloat16)
    swapped = head_swap(jnp.concatenate([low_terms, other_mixed.astype(jnp.bfloat16)], axis=1))
    mixed = (own_mixed + swapped[:, width:].astype(jnp.float32)).astype(jnp.bfloat16)
    grad_normed = low_terms.astype(jnp.float32) + swapped[:, :width].astype(jnp.float32)
    gain_terms = jnp.sum(grad_normed * wide_nodes * inverse, axis=0)
    (w_key_grad, w_value_grad), gain_part = scatter_rows(
        [(normed, grad_key), (normed, grad_value)], "graph", graph_levels, gain_terms
    )
    gain_grad = gain_part
    scaled = grad_normed * gain
    nodes_grad = (
        inverse
        * (
            scaled
            - wide_nodes * inverse * inverse * jnp.mean(scaled * wide_nodes, axis=1, keepdims=True)
        )
    ).astype(jnp.bfloat16)
    return (mixed, nodes_grad, gain_grad, w_query_grad, w_key_grad, w_value_grad, w_out_grad)


def solution(mesh):
    in_specs = (
        P("graph", None),
        P(),
        P(None, "head"),
        P(None, "head"),
        P(None, "head"),
        P("head", None),
        P("graph", None),
        P("graph", None),
    )
    out_specs = (
        P("graph", "head"),
        P("graph", None),
        P(),
        P("graph", "head"),
        P("graph", "head"),
        P("graph", "head"),
        P("head", "graph"),
    )
    return jax.shard_map(shards, mesh=mesh, in_specs=in_specs, out_specs=out_specs, check_vma=False)
```

```python
import jax
import jax.numpy as jnp
from jax import lax
from jax.sharding import PartitionSpec as P
from jax.experimental.layout import Layout, with_layout_constraint
import functools
from jax.experimental import pallas as pl
from jax.experimental.pallas import tpu as pltpu

HEAD_DIM = 64


EPS = 1e-05
NEG = -1e30


def from_partner(value, axis, apart):
    mask = 2**apart
    pairs = [(source, source ^ mask) for source in range(lax.axis_size(axis))]
    return lax.ppermute(value, axis, pairs)


def bit_major_rows(matrix, order):
    rows, width = matrix.shape
    levels = len(order)
    inner = width >> levels
    shaped = matrix.reshape((rows,) + (2,) * levels + (inner,))
    axes = (0,) + tuple(levels - bit for bit in order) + (levels + 1,)
    return shaped.transpose(axes).reshape(rows, width)


def halving_step(partial, axis, bit):
    me = lax.axis_index(axis)
    half = partial.shape[0] // 2
    mine = (me >> bit) & 1
    keep = lax.dynamic_slice_in_dim(partial, mine * half, half, 0)
    send = lax.dynamic_slice_in_dim(partial, (1 - mine) * half, half, 0)
    got = from_partner(send.astype(jnp.bfloat16), axis, bit)
    return keep + got.astype(jnp.float32)


def split_orders(levels):
    first = tuple(range(levels))
    if levels < 3:
        return first, first
    return first, (0, 2, 1) + first[3:]


def scatter_rows(pairs, axis, levels, extra=None):
    contract = (((0,), (0,)), ((), ()))
    orders = split_orders(levels)
    chunks = []
    for index, order in enumerate(orders):
        for left, right in pairs:
            cut = right.shape[1] // 2
            piece = right[:, index * cut : (index + 1) * cut]
            chunks.append(
                lax.dot_general(
                    bit_major_rows(left, order), piece, contract,
                    preferred_element_type=jnp.float32,
                )
            )
    first = sum(right.shape[1] // 2 for left, right in pairs)
    joined = with_layout_constraint(jnp.concatenate(chunks, axis=1), Layout((0, 1)))
    parts = None
    for step in range(levels):
        bit_a, bit_b = orders[0][step], orders[1][step]
        if bit_a == bit_b:
            if parts is not None:
                joined = jnp.concatenate(parts, axis=1)
                parts = None
            (joined,), extra = halving_many([joined], [bit_a], axis, extra, step + 1 < levels)
        else:
            if parts is None:
                parts = [joined[:, :first], joined[:, first:]]
            parts, extra = halving_many(parts, [bit_a, bit_b], axis, extra, step + 1 < levels)
    if parts is not None:
        joined = jnp.concatenate(parts, axis=1)
    results = []
    offset = 0
    for left, right in pairs:
        cut = right.shape[1] // 2
        results.append(
            jnp.concatenate(
                [joined[:, offset : offset + cut], joined[:, first + offset : first + offset + cut]],
                axis=1,
            )
        )
        offset += cut
    return results, extra


def halving_many(parts, bits, axis, extra, tie):
    parts = [halving_step(part, axis, bit) for part, bit in zip(parts, bits)]
    if extra is not None:
        extra = extra + from_partner(extra, axis, bits[0])
        if tie:
            parts, extra = lax.optimization_barrier((parts, extra))
    return parts, extra


def doubling_sum(value, axis, levels):
    for bit in range(levels):
        value = value + from_partner(value, axis, bit)
    return value


def head_swap(value):
    return lax.ppermute(value, "head", [(0, 1), (1, 0)])


def flip_blocks(array, level):
    step = 1 << level
    shaped = array.reshape((array.shape[0] // (2 * step), 2, step) + array.shape[1:])
    return jnp.flip(shaped, axis=1).reshape(array.shape)


def attention_kernel(slots, pairs, active_ref, q_ref, g_ref, *refs):
    key_refs = refs[:slots]
    value_refs = refs[slots : 2 * slots]
    att_ref, gq_ref = refs[2 * slots], refs[2 * slots + 1]
    term_refs = refs[2 * slots + 2 : 3 * slots + 2]
    block = pl.program_id(0)
    scale = HEAD_DIM ** (-0.5)
    width = 2 * HEAD_DIM
    lane = lax.broadcasted_iota(jnp.int32, (q_ref.shape[0], width), 1)
    low_lanes = lane < HEAD_DIM
    flags = [active_ref[block * slots + s] > 0 for s in range(slots)]
    contract_last = (((1,), (1,)), ((), ()))
    contract_first = (((0,), (0,)), ((), ()))
    for pair in range(pairs):
        cols = pl.ds(pair * width, width)
        q2 = q_ref[:, cols]
        g2 = g_ref[:, cols]
        keys = [key_refs[s][:, cols] for s in range(slots)]
        values = [value_refs[s][:, cols] for s in range(slots)]
        outs = []
        for half in range(2):
            sel = low_lanes if half == 0 else jnp.logical_not(low_lanes)
            qm = jnp.where(sel, q2, jnp.zeros_like(q2))
            gm = jnp.where(sel, g2, jnp.zeros_like(g2))
            scores = []
            for s in range(slots):
                raw = lax.dot_general(qm, keys[s], contract_last, preferred_element_type=jnp.float32) * scale
                scores.append(jnp.where(flags[s], raw, NEG))
            top = functools.reduce(jnp.maximum, [jnp.max(x, axis=1, keepdims=True) for x in scores])
            raised = [jnp.exp(x - top) for x in scores]
            total = functools.reduce(jnp.add, [jnp.sum(x, axis=1, keepdims=True) for x in raised])
            spread = 1.0 / total
            probs = [x * spread for x in raised]
            probs_low = [x.astype(jnp.bfloat16) for x in probs]
            attended = functools.reduce(jnp.add, [
                jnp.dot(probs_low[s], values[s], preferred_element_type=jnp.float32) for s in range(slots)
            ])
            grad_probs = [
                lax.dot_general(gm, values[s], contract_last, preferred_element_type=jnp.float32)
                for s in range(slots)
            ]
            delta = functools.reduce(jnp.add, [
                jnp.sum(probs[s] * grad_probs[s], axis=1, keepdims=True) for s in range(slots)
            ])
            grad_scores = [
                (probs[s] * (grad_probs[s] - delta) * scale).astype(jnp.bfloat16)
                for s in range(slots)
            ]
            grad_query = functools.reduce(jnp.add, [
                jnp.dot(grad_scores[s], keys[s], preferred_element_type=jnp.float32)
                for s in range(slots)
            ])
            key_terms = [
                lax.dot_general(grad_scores[s], q2, contract_first,
                                preferred_element_type=jnp.float32)
                for s in range(slots)
            ]
            value_terms = [
                lax.dot_general(probs_low[s], g2, contract_first, preferred_element_type=jnp.float32)
                for s in range(slots)
            ]
            outs.append((attended, grad_query, key_terms, value_terms))
        (att_a, gq_a, kt_a, vt_a), (att_b, gq_b, kt_b, vt_b) = outs
        att_ref[:, cols] = jnp.where(low_lanes, att_a, att_b).astype(att_ref.dtype)
        gq_ref[:, cols] = jnp.where(low_lanes, gq_a, gq_b).astype(gq_ref.dtype)
        for s in range(slots):
            term_refs[s][:, cols] = jnp.where(low_lanes, kt_a[s], kt_b[s]).astype(jnp.bfloat16)
            term_refs[s][:, pl.ds(q_ref.shape[1] + pair * width, width)] = jnp.where(
                low_lanes, vt_a[s], vt_b[s]
            ).astype(jnp.bfloat16)


def block_attention(active, query, grad, joined_slots):
    blocks, rows, columns = query.shape
    slots = len(joined_slots)
    pairs = columns // (2 * HEAD_DIM)
    spec = pl.BlockSpec((None, rows, columns), lambda b, act: (b, 0, 0))
    value_spec = pl.BlockSpec((None, rows, columns), lambda b, act: (b, 0, 1))
    wide_spec = pl.BlockSpec((None, rows, 2 * columns), lambda b, act: (b, 0, 0))
    shape = jax.ShapeDtypeStruct((blocks, rows, columns), jnp.bfloat16)
    wide = jax.ShapeDtypeStruct((blocks, rows, 2 * columns), jnp.bfloat16)
    outs = pl.pallas_call(
        functools.partial(attention_kernel, slots, pairs),
        grid_spec=pltpu.PrefetchScalarGridSpec(
            num_scalar_prefetch=1,
            grid=(blocks,),
            in_specs=[spec] * (2 + slots) + [value_spec] * slots,
            out_specs=[spec] * 2 + [wide_spec] * slots,
        ),
        out_shape=[shape] * 2 + [wide] * slots,
    )(active.reshape(-1), query, grad, *joined_slots, *joined_slots)
    return outs[0], outs[1], outs[2:]


def shards(nodes, gain, w_query, w_key, w_value, w_out, links, cotangent):
    blocks_dev = links.shape[0]
    local_levels = blocks_dev.bit_length() - 1
    graph_levels = lax.axis_size("graph").bit_length() - 1
    node_rows, width = nodes.shape
    block_len = node_rows // blocks_dev
    columns = w_query.shape[1]
    local_heads = columns // HEAD_DIM
    score_scale = HEAD_DIM ** (-0.5)
    contract_rows = (((0,), (0,)), ((), ()))
    wide_nodes = nodes.astype(jnp.float32)
    inverse = lax.rsqrt(jnp.mean(wide_nodes * wide_nodes, axis=1, keepdims=True) + EPS)
    normed = (wide_nodes * inverse * gain).astype(jnp.bfloat16)
    query = jnp.dot(normed, w_query, preferred_element_type=jnp.float32).astype(jnp.bfloat16)
    keys = jnp.dot(normed, w_key, preferred_element_type=jnp.float32).astype(jnp.bfloat16)
    values = jnp.dot(normed, w_value, preferred_element_type=jnp.float32).astype(jnp.bfloat16)
    key_blocks = keys.reshape(blocks_dev, block_len, columns)
    value_blocks = values.reshape(blocks_dev, block_len, columns)
    bit_order = list(range(graph_levels))[::-1]
    joined_blocks = jnp.concatenate([key_blocks, value_blocks], axis=2)
    remote = {}
    for bit in bit_order:
        remote[bit] = from_partner(joined_blocks, "graph", bit)
    joined_slots = (
        [joined_blocks]
        + [flip_blocks(joined_blocks, level) for level in range(local_levels)]
        + [remote[bit] for bit in range(graph_levels)]
    )
    active = jnp.concatenate([jnp.ones((blocks_dev, 1), jnp.int32), links], axis=1)
    grad_attended = jnp.dot(cotangent, w_out.T, preferred_element_type=jnp.float32).astype(
        jnp.bfloat16
    )
    attended, grad_query, term_slots = block_attention(
        active,
        query.reshape(blocks_dev, block_len, columns),
        grad_attended.reshape(blocks_dev, block_len, columns),
        joined_slots,
    )
    attended = attended.reshape(node_rows, columns)
    grad_query = grad_query.reshape(node_rows, columns)
    head_me = lax.axis_index("head")
    mixed_terms = jnp.dot(attended, w_out, preferred_element_type=jnp.float32)
    own_mixed = lax.dynamic_slice_in_dim(mixed_terms, head_me * columns, columns, 1)
    other_mixed = lax.dynamic_slice_in_dim(mixed_terms, (1 - head_me) * columns, columns, 1)
    grad_key = term_slots[0][:, :, :columns].astype(jnp.float32)
    grad_value = term_slots[0][:, :, columns:].astype(jnp.float32)
    returned = {}
    for bit in bit_order:
        slot = 1 + local_levels + bit
        got = from_partner(term_slots[slot], "graph", bit)
        returned[bit] = (got[:, :, :columns], got[:, :, columns:])
    for bit in range(graph_levels):
        grad_key = grad_key + returned[bit][0].astype(jnp.float32)
        grad_value = grad_value + returned[bit][1].astype(jnp.float32)
    grad_key = grad_key.astype(jnp.bfloat16).reshape(node_rows, columns)
    grad_value = grad_value.astype(jnp.bfloat16).reshape(node_rows, columns)
    (w_out_rows, w_query_grad), _ = scatter_rows(
        [(cotangent, attended), (normed, grad_query)], "graph", graph_levels
    )
    w_out_grad = w_out_rows.T
    feature_terms = (
        jnp.dot(grad_query, w_query.T, preferred_element_type=jnp.float32)
        + jnp.dot(grad_key, w_key.T, preferred_element_type=jnp.float32)
        + jnp.dot(grad_value, w_value.T, preferred_element_type=jnp.float32)
    )
    low_terms = feature_terms.astype(jnp.bfloat16)
    swapped = head_swap(jnp.concatenate([low_terms, other_mixed.astype(jnp.bfloat16)], axis=1))
    mixed = (own_mixed + swapped[:, width:].astype(jnp.float32)).astype(jnp.bfloat16)
    grad_normed = low_terms.astype(jnp.float32) + swapped[:, :width].astype(jnp.float32)
    head_gain = jnp.sum(low_terms.astype(jnp.float32) * wide_nodes * inverse, axis=0)
    gain_terms = head_gain + head_swap(head_gain)
    (w_key_grad, w_value_grad), gain_part = scatter_rows(
        [(normed, grad_key), (normed, grad_value)], "graph", graph_levels, gain_terms
    )
    gain_grad = gain_part
    scaled = grad_normed * gain
    nodes_grad = (
        inverse
        * (
            scaled
            - wide_nodes * inverse * inverse * jnp.mean(scaled * wide_nodes, axis=1, keepdims=True)
        )
    ).astype(jnp.bfloat16)
    return (mixed, nodes_grad, gain_grad, w_query_grad, w_key_grad, w_value_grad, w_out_grad)


def solution(mesh):
    in_specs = (
        P("graph", None),
        P(),
        P(None, "head"),
        P(None, "head"),
        P(None, "head"),
        P("head", None),
        P("graph", None),
        P("graph", None),
    )
    out_specs = (
        P("graph", "head"),
        P("graph", None),
        P(),
        P("graph", "head"),
        P("graph", "head"),
        P("graph", "head"),
        P("head", "graph"),
    )
    return jax.shard_map(shards, mesh=mesh, in_specs=in_specs, out_specs=out_specs, check_vma=False)
```

```python
import jax
import jax.numpy as jnp
from jax import lax
from jax.sharding import PartitionSpec as P
from jax.experimental.layout import Layout, with_layout_constraint
import functools
from jax.experimental import pallas as pl
from jax.experimental.pallas import tpu as pltpu

HEAD_DIM = 64


EPS = 1e-05
NEG = -1e30


def from_partner(value, axis, apart):
    mask = 2**apart
    pairs = [(source, source ^ mask) for source in range(lax.axis_size(axis))]
    return lax.ppermute(value, axis, pairs)


def bit_major_rows(matrix, order):
    rows, width = matrix.shape
    levels = len(order)
    inner = width >> levels
    shaped = matrix.reshape((rows,) + (2,) * levels + (inner,))
    axes = (0,) + tuple(levels - bit for bit in order) + (levels + 1,)
    return shaped.transpose(axes).reshape(rows, width)


def halving_step(partial, axis, bit):
    me = lax.axis_index(axis)
    half = partial.shape[0] // 2
    mine = (me >> bit) & 1
    keep = lax.dynamic_slice_in_dim(partial, mine * half, half, 0)
    send = lax.dynamic_slice_in_dim(partial, (1 - mine) * half, half, 0)
    got = from_partner(send.astype(jnp.bfloat16), axis, bit)
    return keep + got.astype(jnp.float32)


def split_orders(levels):
    first = tuple(range(levels))
    if levels < 3:
        return first, first
    return first, (0, 2, 1) + first[3:]


def scatter_rows(pairs, axis, levels, extra=None):
    contract = (((0,), (0,)), ((), ()))
    orders = split_orders(levels)
    chunks = []
    for index, order in enumerate(orders):
        for left, right in pairs:
            cut = right.shape[1] // 2
            piece = right[:, index * cut : (index + 1) * cut]
            chunks.append(
                lax.dot_general(
                    bit_major_rows(left, order), piece, contract,
                    preferred_element_type=jnp.float32,
                )
            )
    first = sum(right.shape[1] // 2 for left, right in pairs)
    joined = with_layout_constraint(jnp.concatenate(chunks, axis=1), Layout((0, 1)))
    parts = None
    for step in range(levels):
        bit_a, bit_b = orders[0][step], orders[1][step]
        if bit_a == bit_b:
            if parts is not None:
                joined = jnp.concatenate(parts, axis=1)
                parts = None
            (joined,), extra = halving_many([joined], [bit_a], axis, extra, step + 1 < levels)
        else:
            if parts is None:
                parts = [joined[:, :first], joined[:, first:]]
            parts, extra = halving_many(parts, [bit_a, bit_b], axis, extra, step + 1 < levels)
    if parts is not None:
        joined = jnp.concatenate(parts, axis=1)
    results = []
    offset = 0
    for left, right in pairs:
        cut = right.shape[1] // 2
        results.append(
            jnp.concatenate(
                [joined[:, offset : offset + cut], joined[:, first + offset : first + offset + cut]],
                axis=1,
            )
        )
        offset += cut
    return results, extra


def halving_many(parts, bits, axis, extra, tie):
    parts = [halving_step(part, axis, bit) for part, bit in zip(parts, bits)]
    if extra is not None:
        extra = extra + from_partner(extra, axis, bits[0])
        if tie:
            parts, extra = lax.optimization_barrier((parts, extra))
    return parts, extra


def doubling_sum(value, axis, levels):
    for bit in range(levels):
        value = value + from_partner(value, axis, bit)
    return value


def head_swap(value):
    return lax.ppermute(value, "head", [(0, 1), (1, 0)])


def flip_blocks(array, level):
    step = 1 << level
    shaped = array.reshape((array.shape[0] // (2 * step), 2, step) + array.shape[1:])
    return jnp.flip(shaped, axis=1).reshape(array.shape)


def attention_kernel(slots, pairs, active_ref, q_ref, g_ref, *refs):
    key_refs = refs[:slots]
    value_refs = refs[slots : 2 * slots]
    att_ref, gq_ref = refs[2 * slots], refs[2 * slots + 1]
    term_refs = refs[2 * slots + 2 : 3 * slots + 2]
    block = pl.program_id(0)
    scale = HEAD_DIM ** (-0.5)
    width = 2 * HEAD_DIM
    lane = lax.broadcasted_iota(jnp.int32, (q_ref.shape[0], width), 1)
    low_lanes = lane < HEAD_DIM
    flags = [active_ref[block * slots + s] > 0 for s in range(slots)]
    contract_last = (((1,), (1,)), ((), ()))
    contract_first = (((0,), (0,)), ((), ()))
    for pair in range(pairs):
        cols = pl.ds(pair * width, width)
        q2 = q_ref[:, cols]
        g2 = g_ref[:, cols]
        keys = [key_refs[s][:, cols] for s in range(slots)]
        values = [value_refs[s][:, cols] for s in range(slots)]
        outs = []
        for half in range(2):
            sel = low_lanes if half == 0 else jnp.logical_not(low_lanes)
            qm = jnp.where(sel, q2, jnp.zeros_like(q2))
            gm = jnp.where(sel, g2, jnp.zeros_like(g2))
            scores = []
            for s in range(slots):
                raw = lax.dot_general(qm, keys[s], contract_last, preferred_element_type=jnp.float32) * scale
                scores.append(jnp.where(flags[s], raw, NEG))
            top = functools.reduce(jnp.maximum, [jnp.max(x, axis=1, keepdims=True) for x in scores])
            raised = [jnp.exp(x - top) for x in scores]
            total = functools.reduce(jnp.add, [jnp.sum(x, axis=1, keepdims=True) for x in raised])
            spread = 1.0 / total
            probs = [x * spread for x in raised]
            probs_low = [x.astype(jnp.bfloat16) for x in probs]
            attended = functools.reduce(jnp.add, [
                jnp.dot(probs_low[s], values[s], preferred_element_type=jnp.float32) for s in range(slots)
            ])
            grad_probs = [
                lax.dot_general(gm, values[s], contract_last, preferred_element_type=jnp.float32)
                for s in range(slots)
            ]
            delta = functools.reduce(jnp.add, [
                jnp.sum(probs[s] * grad_probs[s], axis=1, keepdims=True) for s in range(slots)
            ])
            grad_scores = [
                (probs[s] * (grad_probs[s] - delta) * scale).astype(jnp.bfloat16)
                for s in range(slots)
            ]
            grad_query = functools.reduce(jnp.add, [
                jnp.dot(grad_scores[s], keys[s], preferred_element_type=jnp.float32)
                for s in range(slots)
            ])
            key_terms = [
                lax.dot_general(grad_scores[s], q2, contract_first,
                                preferred_element_type=jnp.float32)
                for s in range(slots)
            ]
            value_terms = [
                lax.dot_general(probs_low[s], g2, contract_first, preferred_element_type=jnp.float32)
                for s in range(slots)
            ]
            outs.append((attended, grad_query, key_terms, value_terms))
        (att_a, gq_a, kt_a, vt_a), (att_b, gq_b, kt_b, vt_b) = outs
        att_ref[:, cols] = jnp.where(low_lanes, att_a, att_b).astype(att_ref.dtype)
        gq_ref[:, cols] = jnp.where(low_lanes, gq_a, gq_b).astype(gq_ref.dtype)
        for s in range(slots):
            term_refs[s][:, cols] = jnp.where(low_lanes, kt_a[s], kt_b[s]).astype(jnp.bfloat16)
            term_refs[s][:, pl.ds(q_ref.shape[1] + pair * width, width)] = jnp.where(
                low_lanes, vt_a[s], vt_b[s]
            ).astype(jnp.bfloat16)


def block_attention(active, query, grad, joined_slots):
    blocks, rows, columns = query.shape
    slots = len(joined_slots)
    pairs = columns // (2 * HEAD_DIM)
    spec = pl.BlockSpec((None, rows, columns), lambda b, act: (b, 0, 0))
    value_spec = pl.BlockSpec((None, rows, columns), lambda b, act: (b, 0, 1))
    wide_spec = pl.BlockSpec((None, rows, 2 * columns), lambda b, act: (b, 0, 0))
    shape = jax.ShapeDtypeStruct((blocks, rows, columns), jnp.bfloat16)
    wide = jax.ShapeDtypeStruct((blocks, rows, 2 * columns), jnp.bfloat16)
    outs = pl.pallas_call(
        functools.partial(attention_kernel, slots, pairs),
        grid_spec=pltpu.PrefetchScalarGridSpec(
            num_scalar_prefetch=1,
            grid=(blocks,),
            in_specs=[spec] * (2 + slots) + [value_spec] * slots,
            out_specs=[spec] * 2 + [wide_spec] * slots,
        ),
        out_shape=[shape] * 2 + [wide] * slots,
    )(active.reshape(-1), query, grad, *joined_slots, *joined_slots)
    return outs[0], outs[1], outs[2:]


def shards(nodes, gain, w_query, w_key, w_value, w_out, links, cotangent):
    blocks_dev = links.shape[0]
    local_levels = blocks_dev.bit_length() - 1
    graph_levels = lax.axis_size("graph").bit_length() - 1
    node_rows, width = nodes.shape
    block_len = node_rows // blocks_dev
    columns = w_query.shape[1]
    local_heads = columns // HEAD_DIM
    score_scale = HEAD_DIM ** (-0.5)
    contract_rows = (((0,), (0,)), ((), ()))
    wide_nodes = nodes.astype(jnp.float32)
    inverse = lax.rsqrt(jnp.mean(wide_nodes * wide_nodes, axis=1, keepdims=True) + EPS)
    normed = (wide_nodes * inverse * gain).astype(jnp.bfloat16)
    query = jnp.dot(normed, w_query, preferred_element_type=jnp.float32).astype(jnp.bfloat16)
    keys = jnp.dot(normed, w_key, preferred_element_type=jnp.float32).astype(jnp.bfloat16)
    values = jnp.dot(normed, w_value, preferred_element_type=jnp.float32).astype(jnp.bfloat16)
    key_blocks = keys.reshape(blocks_dev, block_len, columns)
    value_blocks = values.reshape(blocks_dev, block_len, columns)
    bit_order = list(range(graph_levels))[::-1]
    joined_blocks = jnp.concatenate([key_blocks, value_blocks], axis=2)
    remote = {}
    for bit in bit_order:
        remote[bit] = from_partner(joined_blocks, "graph", bit)
    joined_slots = (
        [joined_blocks]
        + [flip_blocks(joined_blocks, level) for level in range(local_levels)]
        + [remote[bit] for bit in range(graph_levels)]
    )
    active = jnp.concatenate([jnp.ones((blocks_dev, 1), jnp.int32), links], axis=1)
    grad_attended = jnp.dot(cotangent, w_out.T, preferred_element_type=jnp.float32).astype(
        jnp.bfloat16
    )
    attended, grad_query, term_slots = block_attention(
        active,
        query.reshape(blocks_dev, block_len, columns),
        grad_attended.reshape(blocks_dev, block_len, columns),
        joined_slots,
    )
    attended = attended.reshape(node_rows, columns)
    grad_query = grad_query.reshape(node_rows, columns)
    head_me = lax.axis_index("head")
    mixed_terms = jnp.dot(attended, w_out, preferred_element_type=jnp.float32)
    own_mixed = lax.dynamic_slice_in_dim(mixed_terms, head_me * columns, columns, 1)
    other_mixed = lax.dynamic_slice_in_dim(mixed_terms, (1 - head_me) * columns, columns, 1)
    mixed = (own_mixed + head_swap(other_mixed)).astype(jnp.bfloat16)
    grad_key = term_slots[0][:, :, :columns].astype(jnp.float32)
    grad_value = term_slots[0][:, :, columns:].astype(jnp.float32)
    returned = {}
    for bit in bit_order:
        slot = 1 + local_levels + bit
        got = from_partner(term_slots[slot], "graph", bit)
        returned[bit] = (got[:, :, :columns], got[:, :, columns:])
    for bit in range(graph_levels):
        grad_key = grad_key + returned[bit][0].astype(jnp.float32)
        grad_value = grad_value + returned[bit][1].astype(jnp.float32)
    grad_key = grad_key.astype(jnp.bfloat16).reshape(node_rows, columns)
    grad_value = grad_value.astype(jnp.bfloat16).reshape(node_rows, columns)
    (w_out_rows, w_query_grad), _ = scatter_rows(
        [(cotangent, attended), (normed, grad_query)], "graph", graph_levels
    )
    w_out_grad = w_out_rows.T
    feature_terms = (
        jnp.dot(grad_query, w_query.T, preferred_element_type=jnp.float32)
        + jnp.dot(grad_key, w_key.T, preferred_element_type=jnp.float32)
        + jnp.dot(grad_value, w_value.T, preferred_element_type=jnp.float32)
    )
    low_terms = feature_terms.astype(jnp.bfloat16)
    grad_normed = low_terms.astype(jnp.float32) + head_swap(low_terms).astype(jnp.float32)
    gain_terms = jnp.sum(grad_normed * wide_nodes * inverse, axis=0)
    (w_key_grad, w_value_grad), gain_part = scatter_rows(
        [(normed, grad_key), (normed, grad_value)], "graph", graph_levels, gain_terms
    )
    gain_grad = gain_part
    scaled = grad_normed * gain
    nodes_grad = (
        inverse
        * (
            scaled
            - wide_nodes * inverse * inverse * jnp.mean(scaled * wide_nodes, axis=1, keepdims=True)
        )
    ).astype(jnp.bfloat16)
    return (mixed, nodes_grad, gain_grad, w_query_grad, w_key_grad, w_value_grad, w_out_grad)


def solution(mesh):
    in_specs = (
        P("graph", None),
        P(),
        P(None, "head"),
        P(None, "head"),
        P(None, "head"),
        P("head", None),
        P("graph", None),
        P("graph", None),
    )
    out_specs = (
        P("graph", "head"),
        P("graph", None),
        P(),
        P("graph", "head"),
        P("graph", "head"),
        P("graph", "head"),
        P("head", "graph"),
    )
    return jax.shard_map(shards, mesh=mesh, in_specs=in_specs, out_specs=out_specs, check_vma=False)
```
